32 devices in a mesh: groups: 2 (over y), expert: 4 (over x, core), head: 4 (over z).
Axes of the slice: x: 2, y: 2, z: 4, core: 2. Of those that a mesh axis runs over, the one named last changes fastest.
Arguments:
- hidden_in: bfloat16 [512, 2048], P(('groups', 'expert', 'head')), parts along dimension 0, may hold values from -6 to 6
- out_grad: bfloat16 [512, 2048], P(('groups', 'expert', 'head')), parts along dimension 0, may hold values from -6 to 6
- loss_mask: int32 [512], P(('groups', 'expert', 'head')), parts along dimension 0, may hold values 0 or 1
- expert_ids: int32 [512, 8], P(('groups', 'expert', 'head')), parts along dimension 0, may hold values from 0 to 15, all different within a row; in each aligned block of 16 rows (0 to 15, 16 to 31, ...) at most 11 rows name the same one
- gate_weights: float32 [512, 8], P(('groups', 'expert', 'head')), parts along dimension 0, may hold values from 0.02 to 0.3
- cache_lengths: int32 [32], P(('groups', 'expert')), parts along dimension 0, may hold values from 1 to 32, as said below
- key_cache: bfloat16 [32, 32, 256], P(('groups', 'expert')), parts along dimension 0, may hold values from -94 to 94
- prefix_value_cache: bfloat16 [32, 32, 256], P(('groups', 'expert')), parts along dimension 0, may hold values from -6 to 6
- attn_gain: float32 [2048], replicated, may hold values from 0.1 to 1.9
- moe_gain: float32 [2048], replicated, may hold values from 0.1 to 1.9
- w_query: bfloat16 [2048, 2048], P(None, 'head'), may hold values from -0.125 to 0.125
- key_value_weight: bfloat16 [2048, 512], P(None, 'head'), may hold values from -0.125 to 0.125
- w_output: bfloat16 [2048, 2048], P('head'), may hold values from -0.125 to 0.125
- w_gate: bfloat16 [16, 2048, 768], P(('expert', 'head')), may hold values from -0.125 to 0.125
- w_up: bfloat16 [16, 2048, 768], P(('expert', 'head')), may hold values from -0.125 to 0.125
- w_down: bfloat16 [16, 768, 2048], P(('expert', 'head')), may hold values from -0.21875 to 0.21875
Outputs:
- layer_out: bfloat16 [512, 2048], P(('groups', 'expert', 'head')), parts along dimension 0
- input_grad: bfloat16 [512, 2048], P(('groups', 'expert', 'head')), parts along dimension 0
The draws below stay inside these ranges and needn't reach their ends.
There are 2 independent parts, one for each index of `groups`. The reference program is written for one: setup_inputs(seed, part) draws one part's arguments, and reference() takes and returns one part's arrays. A program takes and returns all parts, laid end to end along the dimension named above; an argument that names none is the same for every part. Nothing has to cross between parts.
Inputs may be any that keep to these rules, and one draw needn't show every extreme that they name: `expert_ids`: each row names 8 different experts. Among the rows of one device no expert is named more than 11 times, and in every draw some expert is named exactly 11 times by the rows of some device. `cache_lengths`: some sequence uses all 32 positions.
All inputs are finite; a program needn't handle non-finite values. No bound on the sum of `loss_mask` on one device may be relied on, other than what follows from the above.
Results may differ from the reference program's by a relative error of at most 0.03.
Values may be sent and summed in bfloat16 or wider, within the bound.
No kernel may reach another device: no remote copies, remote signals or barrier semaphores. Data moves between devices by JAX's collectives and lax.ppermute only.
A program may use at most 64 MiB of HBM per device.

```python
import math
import jax
import jax.numpy as jnp
import numpy as np
from jax import lax

MODEL_WIDTH = 2048
QUERY_HEADS = 16
KEY_VALUE_HEADS = 2
HEAD_SIZE = 128
FF = 768
TOP = 8
BLOCK = 16
PREFIX_SLOTS = 32
TOK_DEV = 16
EXPERTS = 16
TOKENS = 256
PART_SEQUENCES = 16
CAP = 11


def draw_cache_lengths(key, part):
    drawn = jax.random.randint(key, (PART_SEQUENCES,), 1, PREFIX_SLOTS + 1)
    spot = jax.random.randint(jax.random.fold_in(key, 7), (), 0, PART_SEQUENCES)
    return jnp.where(jnp.arange(PART_SEQUENCES) == spot, PREFIX_SLOTS, drawn).astype(jnp.int32)


def draw_key_cache(key, part):
    first_key = jax.random.fold_in(key, 0)
    array_shape = (PART_SEQUENCES, PREFIX_SLOTS, KEY_VALUE_HEADS * HEAD_SIZE)
    return jax.random.normal(first_key, array_shape, jnp.float32).astype(jnp.bfloat16)


def touch_ends(values, key, low, top_value):
    index_at = [jax.random.randint(jax.random.fold_in(key, axis), (), 0, length) for axis, length in enumerate(values.shape)]
    main_axis = values.shape.index(max(values.shape))
    next_to = index_at[:main_axis] + [(index_at[main_axis] + 1) % values.shape[main_axis]] + index_at[main_axis + 1:]
    return values.at[tuple(index_at)].set(low).at[tuple(next_to)].set(top_value)


def steps_of(key, dims, shards, low, high):
    loudness, own = 1.0, jax.random.fold_in(key, 6)
    for dim, shards_of in shards:
        steps = jnp.exp(jax.random.uniform(jax.random.fold_in(own, dim), (shards_of,), jnp.float32, low / len(shards), high / len(shards)))
        loudness = loudness * jnp.repeat(steps, dims[dim] // shards_of).reshape([-1 if axis == dim else 1 for axis in range(len(dims))])
    return loudness


def shared_out(rng, own, number, rows, count, top, bound, lean):
    ranking = jax.random.permutation(rng, count)
    packed, ordinary = portions_of(count, rows * top, bound, lean, True), portions_of(count, rows * top, bound, lean, False)
    places = jnp.arange(count)

    def named(sizes, rotation):
        used = int((sizes > 0).sum())
        fixed = max(1, used // 4)
        shifted = fixed + (places - fixed + rotation * (used - fixed)) % max(1, count - fixed)
        return jnp.zeros((count,), jnp.int32).at[ranking[jnp.where(places < fixed, places, shifted)]].set(jnp.asarray(sizes, jnp.int32))

    sizes = jnp.where(number % 4 == 0, named(packed, number // 4), named(ordinary, number - number // 4 - 1))
    mixed = jax.random.permutation(jax.random.fold_in(own, 3), count)
    giver, sink = mixed[0:count // 2 * 2:2], mixed[1:count // 2 * 2:2]
    slack = jnp.minimum(sizes[giver] - 1, bound - sizes[sink]) // 2
    slack = jnp.where((giver == ranking[0]) | (sink == ranking[0]) | (sizes[sink] == 0), 0, jnp.maximum(slack, 0))
    shifted = jax.random.randint(jax.random.fold_in(own, 4), (count // 2,), 0, 1 << 20) % (slack + 1)
    sizes = sizes.at[giver].add(-shifted).at[sink].add(shifted)
    labels = jnp.searchsorted(jnp.cumsum(sizes), jnp.arange(rows * top), side="right").astype(jnp.int32)
    listing = labels.reshape(top, rows).T
    listing = listing[jax.random.permutation(jax.random.fold_in(own, 1), rows)]
    rotation = jax.random.randint(jax.random.fold_in(own, 2), (rows, 1), 0, top)
    return jnp.take_along_axis(listing, (jnp.arange(top)[None, :] + rotation) % top, axis=1)


def portions_of(amount, total, most, lean, full):
    loads = [(1 << 20) // math.isqrt(rank ** lean) + 1 for rank in range(1, amount + 1)]
    largest = most if full else min(most, max(-(-total // amount), total * loads[0] // sum(loads)))
    least = 1 if total - largest >= amount - 1 else 0
    given, surplus = [largest] + [least] * (amount - 1), total - largest - least * (amount - 1)
    while surplus > 0:
        free = [i for i in range(1, amount) if given[i] < largest] or [i for i in range(1, amount) if given[i] < most]
        whole, left = sum([loads[i] for i in free]), surplus
        for i in free:
            more = min(most - given[i], max(1, left * loads[i] // whole), surplus)
            given[i] = given[i] + more
            surplus = surplus - more
    return np.array(given)


def scatter_about(own_key, dims, spread, reach, pieces=(), held_as=jnp.bfloat16):
    array = jax.random.normal(own_key, dims, jnp.float32) * spread
    if len(pieces) > 0:
        array = steps_of(own_key, dims, pieces, -0.22, 0.18) * array
    return jnp.clip(array, min=-reach, max=reach).astype(held_as)


def setup_inputs(seed: int = 0, part: int = 0) -> dict:
    splits = jax.random.split(jax.random.key(seed), 17)
    own_keys = jax.random.split(jax.random.fold_in(splits[16], part), 17)
    hidden_in = scatter_about(own_keys[0], (TOKENS, MODEL_WIDTH), 1.0, 6.0, ((0, 16),))
    out_grad = scatter_about(own_keys[1], (TOKENS, MODEL_WIDTH), 1.0, 6.0, ((0, 16),))
    loss_mask = touch_ends((jax.random.randint(own_keys[2], (TOKENS,), 0, 2) < 1).astype(jnp.int32), jax.random.fold_in(own_keys[2], 1), 0, 1)
    expert_ids_keys = jax.random.split(jax.random.fold_in(own_keys[3], 1), TOKENS // TOK_DEV)
    expert_ids_turns = jax.random.permutation(jax.random.fold_in(own_keys[3], 3), TOKENS // TOK_DEV)
    expert_ids = jax.vmap(lambda own, number: shared_out(jax.random.fold_in(own_keys[3], 2), own, number, TOK_DEV, EXPERTS, TOP, CAP, 2))(expert_ids_keys, expert_ids_turns).reshape((TOKENS, TOP))
    gate_weights = jnp.clip(jnp.exp(math.log(0.3) - 2.7080503 * jax.random.uniform(own_keys[4], (TOKENS, TOP), jnp.float32) ** steps_of(own_keys[4], (TOKENS, TOP), ((0, 16),), -0.2, 0.2)), 0.02, 0.3)
    cache_lengths = draw_cache_lengths(jax.random.fold_in(jax.random.fold_in(splits[16], part), 71), part)
    key_cache = draw_key_cache(jax.random.fold_in(jax.random.fold_in(splits[16], part), 71), part)
    prefix_value_cache = scatter_about(own_keys[7], (PART_SEQUENCES, PREFIX_SLOTS, KEY_VALUE_HEADS * HEAD_SIZE), 1.0, 6.0, ((0, 4),))
    attn_gain = jnp.clip(1.0 + 0.18 * jax.random.normal(splits[8], (MODEL_WIDTH,), jnp.float32), 0.1, 1.9)
    moe_gain = jnp.clip(1.0 + 0.18 * jax.random.normal(splits[9], (MODEL_WIDTH,), jnp.float32), 0.1, 1.9)
    w_query = scatter_about(splits[10], (MODEL_WIDTH, QUERY_HEADS * HEAD_SIZE), MODEL_WIDTH ** -0.5, 0.125, ((1, 4),))
    key_value_weight = scatter_about(splits[11], (MODEL_WIDTH, 2 * KEY_VALUE_HEADS * HEAD_SIZE), MODEL_WIDTH ** -0.5, 0.125, ((1, 4),))
    w_output = scatter_about(splits[12], (QUERY_HEADS * HEAD_SIZE, MODEL_WIDTH), (QUERY_HEADS * HEAD_SIZE) ** -0.5, 0.125, ((0, 4),))
    w_gate = scatter_about(splits[13], (EXPERTS, MODEL_WIDTH, FF), MODEL_WIDTH ** -0.5, 0.125, ((0, 16),))
    w_up = scatter_about(splits[14], (EXPERTS, MODEL_WIDTH, FF), MODEL_WIDTH ** -0.5, 0.125, ((0, 16),))
    w_down = scatter_about(splits[15], (EXPERTS, FF, MODEL_WIDTH), FF ** -0.5, 0.21875, ((0, 16),))
    return {"hidden_in": hidden_in, "out_grad": out_grad, "loss_mask": loss_mask, "expert_ids": expert_ids, "gate_weights": gate_weights, "cache_lengths": cache_lengths, "key_cache": key_cache, "prefix_value_cache": prefix_value_cache, "attn_gain": attn_gain, "moe_gain": moe_gain, "w_query": w_query, "key_value_weight": key_value_weight, "w_output": w_output, "w_gate": w_gate, "w_up": w_up, "w_down": w_down}


EPS = 1e-06
NEG_FILL = -1e+30

def rms_forward(row_block, gain_vec):
    values = row_block.astype(jnp.float32)
    inverse = lax.rsqrt(lax.optimization_barrier(jnp.mean(values * values, axis=-1, keepdims=True)) + EPS)
    return (values * inverse * gain_vec, inverse)

def rms_backward(row_block, gain_vec, inverse, upstream):
    scaled_rows = row_block.astype(jnp.float32) * inverse
    weighted = upstream * gain_vec
    inner_mean = lax.optimization_barrier(jnp.mean(weighted * scaled_rows, axis=-1, keepdims=True))
    return inverse * (weighted - scaled_rows * inner_mean)

def attend_forward(queries, key_rows, value_rows, usable):
    factor = queries.shape[-1] ** (-0.5)
    scores = jnp.einsum('sbhd,skd->shbk', queries.astype(jnp.float32), key_rows.astype(jnp.float32)) * factor
    scores = jnp.where(usable[:, None, None, :], scores, NEG_FILL)
    highest = lax.optimization_barrier(jnp.max(scores, axis=-1, keepdims=True))
    exponent_terms = jnp.exp(scores - highest)
    probabilities = exponent_terms / lax.optimization_barrier(jnp.sum(exponent_terms, axis=-1, keepdims=True))
    probs_low = probabilities.astype(jnp.bfloat16)
    attended = jnp.einsum('shbk,skd->sbhd', probs_low.astype(jnp.float32), value_rows.astype(jnp.float32))
    return (probabilities, probs_low, attended.astype(jnp.bfloat16))

def attend_backward(queries, key_rows, value_rows, probabilities, probs_low, grad_attended):
    factor = queries.shape[-1] ** (-0.5)
    grad_probs = jnp.einsum('sbhd,skd->shbk', grad_attended.astype(jnp.float32), value_rows.astype(jnp.float32))
    inner_sum = lax.optimization_barrier(jnp.sum(probabilities * grad_probs, axis=-1, keepdims=True))
    grad_scores = (probabilities * (grad_probs - inner_sum) * factor).astype(jnp.bfloat16)
    grad_queries = jnp.einsum('shbk,skd->sbhd', grad_scores.astype(jnp.float32), key_rows.astype(jnp.float32))
    grad_keys = jnp.einsum('shbk,sbhd->skd', grad_scores.astype(jnp.float32), queries.astype(jnp.float32))
    grad_values = jnp.einsum('shbk,sbhd->skd', probs_low.astype(jnp.float32), grad_attended.astype(jnp.float32))
    return (grad_queries.astype(jnp.bfloat16), grad_keys, grad_values)

def attention_forward(row_block, query_weights, kv_weights, key_cache, prefix_value_cache, lengths, first_head):
    heads_here = query_weights.shape[1] // HEAD_SIZE
    query_group_count = QUERY_HEADS // KEY_VALUE_HEADS
    kv_here = max(1, heads_here // query_group_count)
    per_kv = heads_here // kv_here
    row_count = row_block.shape[0]
    seq_count = row_count // BLOCK
    key_value_width = KEY_VALUE_HEADS * HEAD_SIZE
    kv_first = first_head // query_group_count
    queries = jnp.dot(row_block, query_weights, preferred_element_type=jnp.float32).astype(jnp.bfloat16)
    queries = queries.reshape(seq_count, BLOCK, heads_here, HEAD_SIZE)
    usable = jnp.concatenate([jnp.arange(PREFIX_SLOTS)[None, :] < lengths[:, None], jnp.ones((seq_count, BLOCK), dtype=jnp.bool_)], axis=1)
    outputs = []
    saved = []
    for member in range(kv_here):
        kv_now = kv_first + member
        pair_weights = jnp.concatenate([lax.dynamic_slice_in_dim(kv_weights, kv_now * HEAD_SIZE, HEAD_SIZE, 1), lax.dynamic_slice_in_dim(kv_weights, key_value_width + kv_now * HEAD_SIZE, HEAD_SIZE, 1)], axis=1)
        pair_rows = jnp.dot(row_block, pair_weights, preferred_element_type=jnp.float32).astype(jnp.bfloat16)
        key_rows = jnp.concatenate([lax.dynamic_slice_in_dim(key_cache, kv_now * HEAD_SIZE, HEAD_SIZE, 2), pair_rows[:, :HEAD_SIZE].reshape(seq_count, BLOCK, HEAD_SIZE)], axis=1)
        value_rows = jnp.concatenate([lax.dynamic_slice_in_dim(prefix_value_cache, kv_now * HEAD_SIZE, HEAD_SIZE, 2), pair_rows[:, HEAD_SIZE:].reshape(seq_count, BLOCK, HEAD_SIZE)], axis=1)
        query_part = queries[:, :, member * per_kv:(member + 1) * per_kv]
        probabilities, probs_low, attended = attend_forward(query_part, key_rows, value_rows, usable)
        outputs.append(attended)
        saved.append((query_part, key_rows, value_rows, probabilities, probs_low, pair_weights))
    joined = jnp.concatenate(outputs, axis=2).reshape(row_count, heads_here * HEAD_SIZE)
    return (joined, saved)

def attention_backward(grad_rows, query_weights, output_weights, saved):
    heads_here = query_weights.shape[1] // HEAD_SIZE
    per_kv = heads_here // len(saved)
    row_count = grad_rows.shape[0]
    seq_count = row_count // BLOCK
    grad_attn = jnp.einsum('td,fd->tf', grad_rows, output_weights, preferred_element_type=jnp.float32).astype(jnp.bfloat16)
    grad_attn = grad_attn.reshape(seq_count, BLOCK, heads_here, HEAD_SIZE)
    running = jnp.zeros((row_count, query_weights.shape[0]), jnp.float32)
    query_grads = []
    for member in range(len(saved)):
        query_part, key_rows, value_rows, probabilities, probs_low, pair_weights = saved[member]
        grad_part = grad_attn[:, :, member * per_kv:(member + 1) * per_kv]
        grad_queries, grad_keys, grad_values = attend_backward(query_part, key_rows, value_rows, probabilities, probs_low, grad_part)
        query_grads.append(grad_queries)
        block_grads = jnp.concatenate([grad_keys[:, PREFIX_SLOTS:].reshape(row_count, HEAD_SIZE), grad_values[:, PREFIX_SLOTS:].reshape(row_count, HEAD_SIZE)], axis=1)
        running = running + jnp.einsum('tc,dc->td', block_grads, pair_weights.astype(jnp.float32), precision=lax.Precision.HIGHEST)
    query_flat = jnp.concatenate(query_grads, axis=2).reshape(row_count, heads_here * HEAD_SIZE)
    return running + jnp.einsum('tf,df->td', query_flat, query_weights, preferred_element_type=jnp.float32)

def reference(hidden_in, out_grad, loss_mask, expert_ids, gate_weights, cache_lengths, key_cache, prefix_value_cache, attn_gain, moe_gain, w_query, key_value_weight, w_output, w_gate, w_up, w_down):
    highest_prec = lax.Precision.HIGHEST
    normed_one, inverse_one = rms_forward(hidden_in, attn_gain)
    attn_rows = normed_one.astype(jnp.bfloat16)
    attended, saved = attention_forward(attn_rows, w_query, key_value_weight, key_cache, prefix_value_cache, cache_lengths, 0)
    mixed = jnp.dot(attended, w_output, preferred_element_type=jnp.float32)
    hidden = (hidden_in.astype(jnp.float32) + mixed).astype(jnp.bfloat16)
    normed_two, inverse_two = rms_forward(hidden, moe_gain)
    moe_rows = normed_two.astype(jnp.bfloat16)
    cotangent = out_grad.astype(jnp.float32) * loss_mask.astype(jnp.float32)[:, None]
    flat_ids = expert_ids.reshape(-1)
    flat_gates = gate_weights.reshape(-1)
    limit = EXPERTS * CAP

    def visit(carry, inputs):
        forward_sum, backward_sum = carry
        expert, gate_matrix, up_matrix, down_matrix = inputs
        chosen = flat_ids == expert
        index = jnp.nonzero(chosen, size=limit, fill_value=0)[0].astype(jnp.int32)
        live = (jnp.arange(limit) < jnp.sum(chosen)).astype(jnp.float32)[:, None]
        owner = index // TOP
        picked = moe_rows[owner].astype(jnp.float32)
        gate_f = gate_matrix.astype(jnp.float32)
        up_f = up_matrix.astype(jnp.float32)
        down_f = down_matrix.astype(jnp.float32)
        gate_pre = jnp.dot(picked, gate_f, precision=highest_prec)
        up_pre = jnp.dot(picked, up_f, precision=highest_prec)
        sigma = jax.nn.sigmoid(gate_pre)
        activated = (gate_pre * sigma * up_pre).astype(jnp.bfloat16)
        result = jnp.dot(activated.astype(jnp.float32), down_f, precision=highest_prec).astype(jnp.bfloat16)
        weighting = flat_gates[index][:, None] * live
        forward_sum = forward_sum.at[owner].add(weighting * result.astype(jnp.float32))
        grad_in = (weighting * cotangent[owner]).astype(jnp.bfloat16)
        grad_act = jnp.dot(grad_in.astype(jnp.float32), down_f.T, precision=highest_prec)
        grad_gate = (grad_act * up_pre * sigma * (1.0 + gate_pre * (1.0 - sigma))).astype(jnp.bfloat16)
        grad_up = (grad_act * gate_pre * sigma).astype(jnp.bfloat16)
        grad_back = jnp.dot(grad_gate.astype(jnp.float32), gate_f.T, precision=highest_prec) + jnp.dot(grad_up.astype(jnp.float32), up_f.T, precision=highest_prec)
        backward_sum = backward_sum.at[owner].add(grad_back.astype(jnp.bfloat16).astype(jnp.float32) * live)
        return ((forward_sum, backward_sum), None)
    empty = jnp.zeros(hidden_in.shape, jnp.float32)
    (moe_sum, grad_moe), _ = lax.scan(visit, (empty, empty), (jnp.arange(EXPERTS, dtype=jnp.int32), w_gate, w_up, w_down))
    layer_out = (hidden.astype(jnp.float32) + moe_sum).astype(jnp.bfloat16)
    grad_hidden = cotangent + rms_backward(hidden, moe_gain, inverse_two, grad_moe)
    grad_attn_rows = attention_backward(grad_hidden.astype(jnp.bfloat16), w_query, w_output, saved)
    input_grad = (grad_hidden + rms_backward(hidden_in, attn_gain, inverse_one, grad_attn_rows)).astype(jnp.bfloat16)
    return (layer_out, input_grad)
```

```python
import jax
import jax.numpy as jnp
from jax import lax
from jax.sharding import PartitionSpec as P

QUERY_HEADS = 16
KEY_VALUE_HEADS = 2
HEAD_SIZE = 128
TOP = 8
BLOCK = 16
PREFIX_SLOTS = 32


EPS = 1e-06
NEG_FILL = -1e30


def rms_forward(row_block, gain_vec):
    values = row_block.astype(jnp.float32)
    inverse = lax.rsqrt(jnp.mean(values * values, axis=-1, keepdims=True) + EPS)
    return (values * inverse * gain_vec, inverse)


def rms_backward(row_block, gain_vec, inverse, upstream):
    scaled_rows = row_block.astype(jnp.float32) * inverse
    weighted = upstream * gain_vec
    inner_mean = jnp.mean(weighted * scaled_rows, axis=-1, keepdims=True)
    return inverse * (weighted - scaled_rows * inner_mean)


def attend_forward(queries, key_rows, value_rows, usable):
    factor = queries.shape[-1] ** (-0.5)
    scores = (
        jnp.einsum("sbhd,skd->shbk", queries.astype(jnp.float32), key_rows.astype(jnp.float32))
        * factor
    )
    scores = jnp.where(usable[:, None, None, :], scores, NEG_FILL)
    highest = jnp.max(scores, axis=-1, keepdims=True)
    exponent_terms = jnp.exp(scores - highest)
    probabilities = exponent_terms / jnp.sum(exponent_terms, axis=-1, keepdims=True)
    probs_low = probabilities.astype(jnp.bfloat16)
    attended = jnp.einsum(
        "shbk,skd->sbhd", probs_low.astype(jnp.float32), value_rows.astype(jnp.float32)
    )
    return (probabilities, probs_low, attended.astype(jnp.bfloat16))


def attend_backward(queries, key_rows, value_rows, probabilities, probs_low, grad_attended):
    factor = queries.shape[-1] ** (-0.5)
    grad_probs = jnp.einsum(
        "sbhd,skd->shbk", grad_attended.astype(jnp.float32), value_rows.astype(jnp.float32)
    )
    inner_sum = jnp.sum(probabilities * grad_probs, axis=-1, keepdims=True)
    grad_scores = (probabilities * (grad_probs - inner_sum) * factor).astype(jnp.bfloat16)
    grad_queries = jnp.einsum(
        "shbk,skd->sbhd", grad_scores.astype(jnp.float32), key_rows.astype(jnp.float32)
    )
    grad_keys = jnp.einsum(
        "shbk,sbhd->skd", grad_scores.astype(jnp.float32), queries.astype(jnp.float32)
    )
    grad_values = jnp.einsum(
        "shbk,sbhd->skd", probs_low.astype(jnp.float32), grad_attended.astype(jnp.float32)
    )
    return (grad_queries.astype(jnp.bfloat16), grad_keys, grad_values)


def attention_forward(
    row_block, query_weights, kv_weights, key_cache, prefix_value_cache, lengths, first_head
):
    heads_here = query_weights.shape[1] // HEAD_SIZE
    query_group_count = QUERY_HEADS // KEY_VALUE_HEADS
    row_count = row_block.shape[0]
    seq_count = row_count // BLOCK
    key_value_width = KEY_VALUE_HEADS * HEAD_SIZE
    kv_first = first_head // query_group_count
    queries = jnp.dot(row_block, query_weights, preferred_element_type=jnp.float32).astype(
        jnp.bfloat16
    )
    queries = queries.reshape(seq_count, BLOCK, heads_here, HEAD_SIZE)
    usable = jnp.concatenate(
        [
            jnp.arange(PREFIX_SLOTS)[None, :] < lengths[:, None],
            jnp.ones((seq_count, BLOCK), dtype=jnp.bool_),
        ],
        axis=1,
    )
    kv_now = kv_first + 0
    pair_weights = jnp.concatenate(
        [
            lax.dynamic_slice_in_dim(kv_weights, kv_now * HEAD_SIZE, HEAD_SIZE, 1),
            lax.dynamic_slice_in_dim(
                kv_weights, key_value_width + kv_now * HEAD_SIZE, HEAD_SIZE, 1
            ),
        ],
        axis=1,
    )
    pair_rows = jnp.dot(row_block, pair_weights, preferred_element_type=jnp.float32).astype(
        jnp.bfloat16
    )
    key_rows = jnp.concatenate(
        [
            lax.dynamic_slice_in_dim(key_cache, kv_now * HEAD_SIZE, HEAD_SIZE, 2),
            pair_rows[:, :HEAD_SIZE].reshape(seq_count, BLOCK, HEAD_SIZE),
        ],
        axis=1,
    )
    value_rows = jnp.concatenate(
        [
            lax.dynamic_slice_in_dim(prefix_value_cache, kv_now * HEAD_SIZE, HEAD_SIZE, 2),
            pair_rows[:, HEAD_SIZE:].reshape(seq_count, BLOCK, HEAD_SIZE),
        ],
        axis=1,
    )
    probabilities, probs_low, attended = attend_forward(queries, key_rows, value_rows, usable)
    saved = [(queries, key_rows, value_rows, probabilities, probs_low, pair_weights)]
    joined = attended.reshape(row_count, heads_here * HEAD_SIZE)
    return (joined, saved)


def attention_backward(grad_rows, query_weights, output_weights, saved):
    heads_here = query_weights.shape[1] // HEAD_SIZE
    row_count = grad_rows.shape[0]
    seq_count = row_count // BLOCK
    grad_attn = jnp.einsum(
        "td,fd->tf", grad_rows, output_weights, preferred_element_type=jnp.float32
    ).astype(jnp.bfloat16)
    grad_attn = grad_attn.reshape(seq_count, BLOCK, heads_here, HEAD_SIZE)
    query_part, key_rows, value_rows, probabilities, probs_low, pair_weights = saved[0]
    grad_queries, grad_keys, grad_values = attend_backward(
        query_part, key_rows, value_rows, probabilities, probs_low, grad_attn
    )
    block_grads = jnp.concatenate(
        [
            grad_keys[:, PREFIX_SLOTS:].reshape(row_count, HEAD_SIZE),
            grad_values[:, PREFIX_SLOTS:].reshape(row_count, HEAD_SIZE),
        ],
        axis=1,
    )
    running = jnp.einsum(
        "tc,dc->td", block_grads, pair_weights.astype(jnp.float32), precision=lax.Precision.HIGHEST
    )
    query_flat = grad_queries.reshape(row_count, heads_here * HEAD_SIZE)
    return running + jnp.einsum(
        "tf,df->td", query_flat, query_weights, preferred_element_type=jnp.float32
    )


def head_rows(row_block):
    return lax.all_gather(row_block, "head", axis=0, tiled=True)


def head_sums(partial_rows):
    return lax.psum_scatter(partial_rows, "head", scatter_dimension=0, tiled=True)


def to_experts(outgoing):
    return lax.all_to_all(outgoing, ("expert", "head"), split_axis=0, concat_axis=0, tiled=True)


def from_experts(results):
    return lax.all_to_all(results, ("expert", "head"), split_axis=0, concat_axis=0, tiled=True)


def body(
    hidden_in,
    out_grad,
    loss_mask,
    expert_ids,
    gate_weights,
    cache_lengths,
    key_cache,
    prefix_value_cache,
    attn_gain,
    moe_gain,
    w_query,
    key_value_weight,
    w_output,
    w_gate,
    w_up,
    w_down,
):
    highest_prec = lax.Precision.HIGHEST
    owned = hidden_in.shape[0]
    width = hidden_in.shape[1]
    normed_one, inverse_one = rms_forward(hidden_in, attn_gain)
    attn_rows = normed_one.astype(jnp.bfloat16)
    kv_full = lax.all_gather(key_value_weight, "head", axis=1, tiled=True)
    heads_here = w_query.shape[1] // HEAD_SIZE
    first_head = lax.axis_index("head") * heads_here
    gathered_rows = head_rows(attn_rows)
    attended, saved = attention_forward(
        gathered_rows, w_query, kv_full, key_cache, prefix_value_cache, cache_lengths, first_head
    )
    mixed = head_sums(jnp.dot(attended, w_output, preferred_element_type=jnp.float32))
    hidden = (hidden_in.astype(jnp.float32) + mixed).astype(jnp.bfloat16)
    normed_two, inverse_two = rms_forward(hidden, moe_gain)
    moe_rows = normed_two.astype(jnp.bfloat16)
    device_count = lax.axis_size("expert") * lax.axis_size("head")
    capacity = (owned * TOP * 4 + 3 * device_count - 1) // (3 * device_count)
    slot_total = device_count * capacity
    flat_ids = expert_ids.reshape(-1)
    one_hot = (flat_ids[:, None] == jnp.arange(device_count, dtype=jnp.int32)[None, :]).astype(
        jnp.int32
    )
    earlier = jnp.cumsum(one_hot, axis=0) - one_hot
    position = jnp.sum(earlier * one_hot, axis=1)
    target = flat_ids * capacity + position
    matched = (jnp.arange(slot_total, dtype=jnp.int32)[:, None] == target[None, :]).reshape(
        device_count, capacity, owned, TOP
    )
    placement = jnp.any(matched, axis=3).astype(jnp.bfloat16)
    weighting = jnp.sum(jnp.where(matched, gate_weights[None, None, :, :], 0.0), axis=3)
    cotangent = out_grad.astype(jnp.float32) * loss_mask.astype(jnp.float32)[:, None]
    outgoing = jnp.einsum(
        "dct,tw->dcw", placement, moe_rows, preferred_element_type=jnp.float32
    ).astype(jnp.bfloat16)
    grad_out = jnp.einsum(
        "dct,tw->dcw", weighting, cotangent, precision=highest_prec
    ).astype(jnp.bfloat16)
    arrived = to_experts(jnp.concatenate([outgoing, grad_out], axis=2))
    rows_in = arrived[:, :, :width]
    grads_in = arrived[:, :, width:]
    gate_matrix = w_gate[0]
    up_matrix = w_up[0]
    down_matrix = w_down[0]
    gate_pre = jnp.einsum("scw,wf->scf", rows_in, gate_matrix, preferred_element_type=jnp.float32)
    up_pre = jnp.einsum("scw,wf->scf", rows_in, up_matrix, preferred_element_type=jnp.float32)
    sigma = jax.nn.sigmoid(gate_pre)
    activated = (gate_pre * sigma * up_pre).astype(jnp.bfloat16)
    result = jnp.einsum(
        "scf,fw->scw", activated, down_matrix, preferred_element_type=jnp.float32
    ).astype(jnp.bfloat16)
    grad_act = jnp.einsum(
        "scw,fw->scf", grads_in, down_matrix, preferred_element_type=jnp.float32
    )
    grad_gate = (grad_act * up_pre * sigma * (1.0 + gate_pre * (1.0 - sigma))).astype(jnp.bfloat16)
    grad_up = (grad_act * gate_pre * sigma).astype(jnp.bfloat16)
    grad_back = jnp.einsum(
        "scf,wf->scw", grad_gate, gate_matrix, preferred_element_type=jnp.float32
    )
    grad_back = grad_back + jnp.einsum(
        "scf,wf->scw", grad_up, up_matrix, preferred_element_type=jnp.float32
    )
    grad_back = grad_back.astype(jnp.bfloat16)
    returned = from_experts(jnp.concatenate([result, grad_back], axis=2))
    moe_sum = jnp.einsum(
        "dct,dcw->tw",
        weighting,
        returned[:, :, :width].astype(jnp.float32),
        precision=highest_prec,
    )
    layer_out = (hidden.astype(jnp.float32) + moe_sum).astype(jnp.bfloat16)
    grad_moe = jnp.einsum(
        "dct,dcw->tw", placement, returned[:, :, width:], preferred_element_type=jnp.float32
    )
    grad_hidden = cotangent + rms_backward(hidden, moe_gain, inverse_two, grad_moe)
    grad_low = grad_hidden.astype(jnp.bfloat16)
    grad_gathered = head_rows(grad_low)
    grad_attn_rows = head_sums(attention_backward(grad_gathered, w_query, w_output, saved))
    input_grad = (
        grad_hidden + rms_backward(hidden_in, attn_gain, inverse_one, grad_attn_rows)
    ).astype(jnp.bfloat16)
    return (layer_out, input_grad)


def solution(mesh):
    in_specs = (
        P(("groups", "expert", "head"), None),
        P(("groups", "expert", "head"), None),
        P(("groups", "expert", "head")),
        P(("groups", "expert", "head"), None),
        P(("groups", "expert", "head"), None),
        P(("groups", "expert")),
        P(("groups", "expert"), None, None),
        P(("groups", "expert"), None, None),
        P(),
        P(),
        P(None, "head"),
        P(None, "head"),
        P("head", None),
        P(("expert", "head"), None, None),
        P(("expert", "head"), None, None),
        P(("expert", "head"), None, None),
    )
    out_specs = (P(("groups", "expert", "head"), None), P(("groups", "expert", "head"), None))
    return jax.shard_map(body, mesh=mesh, in_specs=in_specs, out_specs=out_specs, check_vma=False)
```

```python
import jax
import jax.numpy as jnp
from jax import lax
from jax.sharding import PartitionSpec as P

QUERY_HEADS = 16
KEY_VALUE_HEADS = 2
HEAD_SIZE = 128
TOP = 8
BLOCK = 16
PREFIX_SLOTS = 32


EPS = 1e-06
NEG_FILL = -1e30


def rms_forward(row_block, gain_vec):
    values = row_block.astype(jnp.float32)
    inverse = lax.rsqrt(jnp.mean(values * values, axis=-1, keepdims=True) + EPS)
    return (values * inverse * gain_vec, inverse)


def rms_backward(row_block, gain_vec, inverse, upstream):
    scaled_rows = row_block.astype(jnp.float32) * inverse
    weighted = upstream * gain_vec
    inner_mean = jnp.mean(weighted * scaled_rows, axis=-1, keepdims=True)
    return inverse * (weighted - scaled_rows * inner_mean)


def attend_forward(queries, key_rows, value_rows, usable):
    factor = queries.shape[-1] ** (-0.5)
    scores = (
        jnp.einsum("sbhd,skd->shbk", queries.astype(jnp.float32), key_rows.astype(jnp.float32))
        * factor
    )
    scores = jnp.where(usable[:, None, None, :], scores, NEG_FILL)
    highest = jnp.max(scores, axis=-1, keepdims=True)
    exponent_terms = jnp.exp(scores - highest)
    probabilities = exponent_terms / jnp.sum(exponent_terms, axis=-1, keepdims=True)
    probs_low = probabilities.astype(jnp.bfloat16)
    attended = jnp.einsum(
        "shbk,skd->sbhd", probs_low.astype(jnp.float32), value_rows.astype(jnp.float32)
    )
    return (probabilities, probs_low, attended.astype(jnp.bfloat16))


def attend_backward(queries, key_rows, value_rows, probabilities, probs_low, grad_attended):
    factor = queries.shape[-1] ** (-0.5)
    grad_probs = jnp.einsum(
        "sbhd,skd->shbk", grad_attended.astype(jnp.float32), value_rows.astype(jnp.float32)
    )
    inner_sum = jnp.sum(probabilities * grad_probs, axis=-1, keepdims=True)
    grad_scores = (probabilities * (grad_probs - inner_sum) * factor).astype(jnp.bfloat16)
    grad_queries = jnp.einsum(
        "shbk,skd->sbhd", grad_scores.astype(jnp.float32), key_rows.astype(jnp.float32)
    )
    grad_keys = jnp.einsum(
        "shbk,sbhd->skd", grad_scores.astype(jnp.float32), queries.astype(jnp.float32)
    )
    grad_values = jnp.einsum(
        "shbk,sbhd->skd", probs_low.astype(jnp.float32), grad_attended.astype(jnp.float32)
    )
    return (grad_queries.astype(jnp.bfloat16), grad_keys, grad_values)


def attention_forward(
    row_block, query_weights, kv_weights, key_cache, prefix_value_cache, lengths, first_head
):
    heads_here = query_weights.shape[1] // HEAD_SIZE
    query_group_count = QUERY_HEADS // KEY_VALUE_HEADS
    row_count = row_block.shape[0]
    seq_count = row_count // BLOCK
    key_value_width = KEY_VALUE_HEADS * HEAD_SIZE
    kv_first = first_head // query_group_count
    queries = jnp.dot(row_block, query_weights, preferred_element_type=jnp.float32).astype(
        jnp.bfloat16
    )
    queries = queries.reshape(seq_count, BLOCK, heads_here, HEAD_SIZE)
    usable = jnp.concatenate(
        [
            jnp.arange(PREFIX_SLOTS)[None, :] < lengths[:, None],
            jnp.ones((seq_count, BLOCK), dtype=jnp.bool_),
        ],
        axis=1,
    )
    kv_now = kv_first + 0
    pair_weights = jnp.concatenate(
        [
            lax.dynamic_slice_in_dim(kv_weights, kv_now * HEAD_SIZE, HEAD_SIZE, 1),
            lax.dynamic_slice_in_dim(
                kv_weights, key_value_width + kv_now * HEAD_SIZE, HEAD_SIZE, 1
            ),
        ],
        axis=1,
    )
    pair_rows = jnp.dot(row_block, pair_weights, preferred_element_type=jnp.float32).astype(
        jnp.bfloat16
    )
    key_rows = jnp.concatenate(
        [
            lax.dynamic_slice_in_dim(key_cache, kv_now * HEAD_SIZE, HEAD_SIZE, 2),
            pair_rows[:, :HEAD_SIZE].reshape(seq_count, BLOCK, HEAD_SIZE),
        ],
        axis=1,
    )
    value_rows = jnp.concatenate(
        [
            lax.dynamic_slice_in_dim(prefix_value_cache, kv_now * HEAD_SIZE, HEAD_SIZE, 2),
            pair_rows[:, HEAD_SIZE:].reshape(seq_count, BLOCK, HEAD_SIZE),
        ],
        axis=1,
    )
    probabilities, probs_low, attended = attend_forward(queries, key_rows, value_rows, usable)
    saved = [(queries, key_rows, value_rows, probabilities, probs_low, pair_weights)]
    joined = attended.reshape(row_count, heads_here * HEAD_SIZE)
    return (joined, saved)


def attention_backward(grad_rows, query_weights, output_weights, saved):
    heads_here = query_weights.shape[1] // HEAD_SIZE
    row_count = grad_rows.shape[0]
    seq_count = row_count // BLOCK
    grad_attn = jnp.einsum(
        "td,fd->tf", grad_rows, output_weights, preferred_element_type=jnp.float32
    ).astype(jnp.bfloat16)
    grad_attn = grad_attn.reshape(seq_count, BLOCK, heads_here, HEAD_SIZE)
    query_part, key_rows, value_rows, probabilities, probs_low, pair_weights = saved[0]
    grad_queries, grad_keys, grad_values = attend_backward(
        query_part, key_rows, value_rows, probabilities, probs_low, grad_attn
    )
    block_grads = jnp.concatenate(
        [
            grad_keys[:, PREFIX_SLOTS:].reshape(row_count, HEAD_SIZE),
            grad_values[:, PREFIX_SLOTS:].reshape(row_count, HEAD_SIZE),
        ],
        axis=1,
    )
    running = jnp.einsum(
        "tc,dc->td", block_grads, pair_weights.astype(jnp.float32), precision=lax.Precision.HIGHEST
    )
    query_flat = grad_queries.reshape(row_count, heads_here * HEAD_SIZE)
    return running + jnp.einsum(
        "tf,df->td", query_flat, query_weights, preferred_element_type=jnp.float32
    )


def head_rows(row_block):
    return lax.all_gather(row_block, "head", axis=0, tiled=True)


def head_sums(partial_rows):
    return lax.psum_scatter(partial_rows, "head", scatter_dimension=0, tiled=True)


EXPERT_AXES = ("expert", "head")


def shift_send(block, axes, count, shift):
    return lax.ppermute(block, axes, perm=[(j, (j + shift) % count) for j in range(count)])


def exchange(slots, axes, count, sign):
    moved = [slots[0]]
    for shift in range(1, count):
        moved.append(shift_send(slots[shift], axes, count, (sign * shift) % count))
    return jnp.stack(moved)


def body(
    hidden_in,
    out_grad,
    loss_mask,
    expert_ids,
    gate_weights,
    cache_lengths,
    key_cache,
    prefix_value_cache,
    attn_gain,
    moe_gain,
    w_query,
    key_value_weight,
    w_output,
    w_gate,
    w_up,
    w_down,
):
    highest_prec = lax.Precision.HIGHEST
    owned = hidden_in.shape[0]
    width = hidden_in.shape[1]
    normed_one, inverse_one = rms_forward(hidden_in, attn_gain)
    attn_rows = normed_one.astype(jnp.bfloat16)
    kv_full = lax.all_gather(key_value_weight, "head", axis=1, tiled=True)
    heads_here = w_query.shape[1] // HEAD_SIZE
    first_head = lax.axis_index("head") * heads_here
    gathered_rows = head_rows(attn_rows)
    attended, saved = attention_forward(
        gathered_rows, w_query, kv_full, key_cache, prefix_value_cache, cache_lengths, first_head
    )
    mixed = head_sums(jnp.dot(attended, w_output, preferred_element_type=jnp.float32))
    hidden = (hidden_in.astype(jnp.float32) + mixed).astype(jnp.bfloat16)
    normed_two, inverse_two = rms_forward(hidden, moe_gain)
    moe_rows = normed_two.astype(jnp.bfloat16)
    device_count = lax.axis_size("expert") * lax.axis_size("head")
    capacity = (owned * TOP * 4 + 3 * device_count - 1) // (3 * device_count)
    slot_total = device_count * capacity
    flat_ids = expert_ids.reshape(-1)
    one_hot = (flat_ids[:, None] == jnp.arange(device_count, dtype=jnp.int32)[None, :]).astype(
        jnp.int32
    )
    earlier = jnp.cumsum(one_hot, axis=0) - one_hot
    position = jnp.sum(earlier * one_hot, axis=1)
    me = lax.axis_index(EXPERT_AXES)
    target = ((flat_ids - me) % device_count) * capacity + position
    matched = (jnp.arange(slot_total, dtype=jnp.int32)[:, None] == target[None, :]).reshape(
        device_count, capacity, owned, TOP
    )
    placement = jnp.any(matched, axis=3).astype(jnp.bfloat16)
    weighting = jnp.sum(jnp.where(matched, gate_weights[None, None, :, :], 0.0), axis=3)
    cotangent = out_grad.astype(jnp.float32) * loss_mask.astype(jnp.float32)[:, None]
    outgoing = jnp.einsum(
        "dct,tw->dcw", placement, moe_rows, preferred_element_type=jnp.float32
    ).astype(jnp.bfloat16)
    grad_out = jnp.einsum(
        "dct,tw->dcw", weighting, cotangent, precision=highest_prec
    ).astype(jnp.bfloat16)
    arrived = exchange(jnp.concatenate([outgoing, grad_out], axis=2), EXPERT_AXES, device_count, 1)
    rows_in = arrived[:, :, :width]
    grads_in = arrived[:, :, width:]
    gate_matrix = w_gate[0]
    up_matrix = w_up[0]
    down_matrix = w_down[0]
    gate_pre = jnp.einsum("scw,wf->scf", rows_in, gate_matrix, preferred_element_type=jnp.float32)
    up_pre = jnp.einsum("scw,wf->scf", rows_in, up_matrix, preferred_element_type=jnp.float32)
    sigma = jax.nn.sigmoid(gate_pre)
    activated = (gate_pre * sigma * up_pre).astype(jnp.bfloat16)
    result = jnp.einsum(
        "scf,fw->scw", activated, down_matrix, preferred_element_type=jnp.float32
    ).astype(jnp.bfloat16)
    grad_act = jnp.einsum(
        "scw,fw->scf", grads_in, down_matrix, preferred_element_type=jnp.float32
    )
    grad_gate = (grad_act * up_pre * sigma * (1.0 + gate_pre * (1.0 - sigma))).astype(jnp.bfloat16)
    grad_up = (grad_act * gate_pre * sigma).astype(jnp.bfloat16)
    grad_back = jnp.einsum(
        "scf,wf->scw", grad_gate, gate_matrix, preferred_element_type=jnp.float32
    )
    grad_back = grad_back + jnp.einsum(
        "scf,wf->scw", grad_up, up_matrix, preferred_element_type=jnp.float32
    )
    grad_back = grad_back.astype(jnp.bfloat16)
    returned = exchange(jnp.concatenate([result, grad_back], axis=2), EXPERT_AXES, device_count, -1)
    moe_sum = jnp.einsum(
        "dct,dcw->tw",
        weighting,
        returned[:, :, :width].astype(jnp.float32),
        precision=highest_prec,
    )
    layer_out = (hidden.astype(jnp.float32) + moe_sum).astype(jnp.bfloat16)
    grad_moe = jnp.einsum(
        "dct,dcw->tw", placement, returned[:, :, width:], preferred_element_type=jnp.float32
    )
    grad_hidden = cotangent + rms_backward(hidden, moe_gain, inverse_two, grad_moe)
    grad_low = grad_hidden.astype(jnp.bfloat16)
    grad_gathered = head_rows(grad_low)
    grad_attn_rows = head_sums(attention_backward(grad_gathered, w_query, w_output, saved))
    input_grad = (
        grad_hidden + rms_backward(hidden_in, attn_gain, inverse_one, grad_attn_rows)
    ).astype(jnp.bfloat16)
    return (layer_out, input_grad)


def solution(mesh):
    in_specs = (
        P(("groups", "expert", "head"), None),
        P(("groups", "expert", "head"), None),
        P(("groups", "expert", "head")),
        P(("groups", "expert", "head"), None),
        P(("groups", "expert", "head"), None),
        P(("groups", "expert")),
        P(("groups", "expert"), None, None),
        P(("groups", "expert"), None, None),
        P(),
        P(),
        P(None, "head"),
        P(None, "head"),
        P("head", None),
        P(("expert", "head"), None, None),
        P(("expert", "head"), None, None),
        P(("expert", "head"), None, None),
    )
    out_specs = (P(("groups", "expert", "head"), None), P(("groups", "expert", "head"), None))
    return jax.shard_map(body, mesh=mesh, in_specs=in_specs, out_specs=out_specs, check_vma=False)
```

```python
import jax
import jax.numpy as jnp
from jax import lax
from jax.sharding import PartitionSpec as P

QUERY_HEADS = 16
KEY_VALUE_HEADS = 2
HEAD_SIZE = 128
TOP = 8
BLOCK = 16
PREFIX_SLOTS = 32


EPS = 1e-06
NEG_FILL = -1e30


def rms_forward(row_block, gain_vec):
    values = row_block.astype(jnp.float32)
    inverse = lax.rsqrt(jnp.mean(values * values, axis=-1, keepdims=True) + EPS)
    return (values * inverse * gain_vec, inverse)


def rms_backward(row_block, gain_vec, inverse, upstream):
    scaled_rows = row_block.astype(jnp.float32) * inverse
    weighted = upstream * gain_vec
    inner_mean = jnp.mean(weighted * scaled_rows, axis=-1, keepdims=True)
    return inverse * (weighted - scaled_rows * inner_mean)


def attend_forward(queries, key_rows, value_rows, usable):
    factor = queries.shape[-1] ** (-0.5)
    scores = (
        jnp.einsum("sbhd,skd->shbk", queries.astype(jnp.float32), key_rows.astype(jnp.float32))
        * factor
    )
    scores = jnp.where(usable[:, None, None, :], scores, NEG_FILL)
    highest = jnp.max(scores, axis=-1, keepdims=True)
    exponent_terms = jnp.exp(scores - highest)
    probabilities = exponent_terms / jnp.sum(exponent_terms, axis=-1, keepdims=True)
    probs_low = probabilities.astype(jnp.bfloat16)
    attended = jnp.einsum(
        "shbk,skd->sbhd", probs_low.astype(jnp.float32), value_rows.astype(jnp.float32)
    )
    return (probabilities, probs_low, attended.astype(jnp.bfloat16))


def attend_backward(queries, key_rows, value_rows, probabilities, probs_low, grad_attended):
    factor = queries.shape[-1] ** (-0.5)
    grad_probs = jnp.einsum(
        "sbhd,skd->shbk", grad_attended.astype(jnp.float32), value_rows.astype(jnp.float32)
    )
    inner_sum = jnp.sum(probabilities * grad_probs, axis=-1, keepdims=True)
    grad_scores = (probabilities * (grad_probs - inner_sum) * factor).astype(jnp.bfloat16)
    grad_queries = jnp.einsum(
        "shbk,skd->sbhd", grad_scores.astype(jnp.float32), key_rows.astype(jnp.float32)
    )
    grad_keys = jnp.einsum(
        "shbk,sbhd->skd", grad_scores.astype(jnp.float32), queries.astype(jnp.float32)
    )
    grad_values = jnp.einsum(
        "shbk,sbhd->skd", probs_low.astype(jnp.float32), grad_attended.astype(jnp.float32)
    )
    return (grad_queries.astype(jnp.bfloat16), grad_keys, grad_values)


def attention_forward(
    row_block, query_weights, kv_weights, key_cache, prefix_value_cache, lengths, first_head
):
    heads_here = query_weights.shape[1] // HEAD_SIZE
    query_group_count = QUERY_HEADS // KEY_VALUE_HEADS
    row_count = row_block.shape[0]
    seq_count = row_count // BLOCK
    key_value_width = KEY_VALUE_HEADS * HEAD_SIZE
    kv_first = first_head // query_group_count
    queries = jnp.dot(row_block, query_weights, preferred_element_type=jnp.float32).astype(
        jnp.bfloat16
    )
    queries = queries.reshape(seq_count, BLOCK, heads_here, HEAD_SIZE)
    usable = jnp.concatenate(
        [
            jnp.arange(PREFIX_SLOTS)[None, :] < lengths[:, None],
            jnp.ones((seq_count, BLOCK), dtype=jnp.bool_),
        ],
        axis=1,
    )
    kv_now = kv_first + 0
    pair_weights = jnp.concatenate(
        [
            lax.dynamic_slice_in_dim(kv_weights, kv_now * HEAD_SIZE, HEAD_SIZE, 1),
            lax.dynamic_slice_in_dim(
                kv_weights, key_value_width + kv_now * HEAD_SIZE, HEAD_SIZE, 1
            ),
        ],
        axis=1,
    )
    pair_rows = jnp.dot(row_block, pair_weights, preferred_element_type=jnp.float32).astype(
        jnp.bfloat16
    )
    key_rows = jnp.concatenate(
        [
            lax.dynamic_slice_in_dim(key_cache, kv_now * HEAD_SIZE, HEAD_SIZE, 2),
            pair_rows[:, :HEAD_SIZE].reshape(seq_count, BLOCK, HEAD_SIZE),
        ],
        axis=1,
    )
    value_rows = jnp.concatenate(
        [
            lax.dynamic_slice_in_dim(prefix_value_cache, kv_now * HEAD_SIZE, HEAD_SIZE, 2),
            pair_rows[:, HEAD_SIZE:].reshape(seq_count, BLOCK, HEAD_SIZE),
        ],
        axis=1,
    )
    probabilities, probs_low, attended = attend_forward(queries, key_rows, value_rows, usable)
    saved = [(queries, key_rows, value_rows, probabilities, probs_low, pair_weights)]
    joined = attended.reshape(row_count, heads_here * HEAD_SIZE)
    return (joined, saved)


def attention_backward(grad_rows, query_weights, output_weights, saved):
    heads_here = query_weights.shape[1] // HEAD_SIZE
    row_count = grad_rows.shape[0]
    seq_count = row_count // BLOCK
    grad_attn = jnp.einsum(
        "td,fd->tf", grad_rows, output_weights, preferred_element_type=jnp.float32
    ).astype(jnp.bfloat16)
    grad_attn = grad_attn.reshape(seq_count, BLOCK, heads_here, HEAD_SIZE)
    query_part, key_rows, value_rows, probabilities, probs_low, pair_weights = saved[0]
    grad_queries, grad_keys, grad_values = attend_backward(
        query_part, key_rows, value_rows, probabilities, probs_low, grad_attn
    )
    block_grads = jnp.concatenate(
        [
            grad_keys[:, PREFIX_SLOTS:].reshape(row_count, HEAD_SIZE),
            grad_values[:, PREFIX_SLOTS:].reshape(row_count, HEAD_SIZE),
        ],
        axis=1,
    )
    running = jnp.einsum(
        "tc,dc->td", block_grads, pair_weights.astype(jnp.float32), precision=lax.Precision.HIGHEST
    )
    query_flat = grad_queries.reshape(row_count, heads_here * HEAD_SIZE)
    return running + jnp.einsum(
        "tf,df->td", query_flat, query_weights, preferred_element_type=jnp.float32
    )


def head_rows(row_block):
    return lax.all_gather(row_block, "head", axis=0, tiled=True)


def head_sums(partial_rows):
    return lax.psum_scatter(partial_rows, "head", scatter_dimension=0, tiled=True)


def to_experts(outgoing):
    return lax.all_to_all(outgoing, ("expert", "head"), split_axis=0, concat_axis=0, tiled=True)


def from_experts(results):
    return lax.all_to_all(results, ("expert", "head"), split_axis=0, concat_axis=0, tiled=True)


def body(
    hidden_in,
    out_grad,
    loss_mask,
    expert_ids,
    gate_weights,
    cache_lengths,
    key_cache,
    prefix_value_cache,
    attn_gain,
    moe_gain,
    w_query,
    key_value_weight,
    w_output,
    w_gate,
    w_up,
    w_down,
):
    highest_prec = lax.Precision.HIGHEST
    owned = hidden_in.shape[0]
    width = hidden_in.shape[1]
    normed_one, inverse_one = rms_forward(hidden_in, attn_gain)
    attn_rows = normed_one.astype(jnp.bfloat16)
    kv_full = lax.all_gather(key_value_weight, "head", axis=1, tiled=True)
    heads_here = w_query.shape[1] // HEAD_SIZE
    first_head = lax.axis_index("head") * heads_here
    gathered_rows = head_rows(attn_rows)
    attended, saved = attention_forward(
        gathered_rows, w_query, kv_full, key_cache, prefix_value_cache, cache_lengths, first_head
    )
    mixed = head_sums(jnp.dot(attended, w_output, preferred_element_type=jnp.float32))
    hidden = (hidden_in.astype(jnp.float32) + mixed).astype(jnp.bfloat16)
    normed_two, inverse_two = rms_forward(hidden, moe_gain)
    moe_rows = normed_two.astype(jnp.bfloat16)
    device_count = lax.axis_size("expert") * lax.axis_size("head")
    capacity = (owned * TOP * 4 + 3 * device_count - 1) // (3 * device_count)
    slot_total = device_count * capacity
    flat_ids = expert_ids.reshape(-1)
    one_hot = (flat_ids[:, None] == jnp.arange(device_count, dtype=jnp.int32)[None, :]).astype(
        jnp.int32
    )
    earlier = jnp.cumsum(one_hot, axis=0) - one_hot
    position = jnp.sum(earlier * one_hot, axis=1)
    target = flat_ids * capacity + position
    matched = (jnp.arange(slot_total, dtype=jnp.int32)[:, None] == target[None, :]).reshape(
        device_count, capacity, owned, TOP
    )
    placement = jnp.any(matched, axis=3).astype(jnp.bfloat16)
    weighting = jnp.sum(jnp.where(matched, gate_weights[None, None, :, :], 0.0), axis=3)
    cotangent = out_grad.astype(jnp.float32) * loss_mask.astype(jnp.float32)[:, None]
    outgoing = jnp.einsum(
        "dct,tw->dcw", placement, moe_rows, preferred_element_type=jnp.float32
    ).astype(jnp.bfloat16)
    grad_out = jnp.einsum(
        "dct,tw->dcw", weighting, cotangent, precision=highest_prec
    ).astype(jnp.bfloat16)
    rows_in = to_experts(outgoing)
    grads_in = to_experts(grad_out)
    gate_matrix = w_gate[0]
    up_matrix = w_up[0]
    down_matrix = w_down[0]
    gate_pre = jnp.einsum("scw,wf->scf", rows_in, gate_matrix, preferred_element_type=jnp.float32)
    up_pre = jnp.einsum("scw,wf->scf", rows_in, up_matrix, preferred_element_type=jnp.float32)
    sigma = jax.nn.sigmoid(gate_pre)
    activated = (gate_pre * sigma * up_pre).astype(jnp.bfloat16)
    result = jnp.einsum(
        "scf,fw->scw", activated, down_matrix, preferred_element_type=jnp.float32
    ).astype(jnp.bfloat16)
    grad_act = jnp.einsum(
        "scw,fw->scf", grads_in, down_matrix, preferred_element_type=jnp.float32
    )
    grad_gate = (grad_act * up_pre * sigma * (1.0 + gate_pre * (1.0 - sigma))).astype(jnp.bfloat16)
    grad_up = (grad_act * gate_pre * sigma).astype(jnp.bfloat16)
    grad_back = jnp.einsum(
        "scf,wf->scw", grad_gate, gate_matrix, preferred_element_type=jnp.float32
    )
    grad_back = grad_back + jnp.einsum(
        "scf,wf->scw", grad_up, up_matrix, preferred_element_type=jnp.float32
    )
    grad_back = grad_back.astype(jnp.bfloat16)
    result_home = from_experts(result)
    grad_home = from_experts(grad_back)
    moe_sum = jnp.einsum(
        "dct,dcw->tw",
        weighting,
        result_home.astype(jnp.float32),
        precision=highest_prec,
    )
    layer_out = (hidden.astype(jnp.float32) + moe_sum).astype(jnp.bfloat16)
    grad_moe = jnp.einsum(
        "dct,dcw->tw", placement, grad_home, preferred_element_type=jnp.float32
    )
    grad_hidden = cotangent + rms_backward(hidden, moe_gain, inverse_two, grad_moe)
    grad_low = grad_hidden.astype(jnp.bfloat16)
    grad_gathered = head_rows(grad_low)
    grad_attn_rows = head_sums(attention_backward(grad_gathered, w_query, w_output, saved))
    input_grad = (
        grad_hidden + rms_backward(hidden_in, attn_gain, inverse_one, grad_attn_rows)
    ).astype(jnp.bfloat16)
    return (layer_out, input_grad)


def solution(mesh):
    in_specs = (
        P(("groups", "expert", "head"), None),
        P(("groups", "expert", "head"), None),
        P(("groups", "expert", "head")),
        P(("groups", "expert", "head"), None),
        P(("groups", "expert", "head"), None),
        P(("groups", "expert")),
        P(("groups", "expert"), None, None),
        P(("groups", "expert"), None, None),
        P(),
        P(),
        P(None, "head"),
        P(None, "head"),
        P("head", None),
        P(("expert", "head"), None, None),
        P(("expert", "head"), None, None),
        P(("expert", "head"), None, None),
    )
    out_specs = (P(("groups", "expert", "head"), None), P(("groups", "expert", "head"), None))
    return jax.shard_map(body, mesh=mesh, in_specs=in_specs, out_specs=out_specs, check_vma=False)
```

```python
import jax
import jax.numpy as jnp
from jax import lax
from jax.sharding import PartitionSpec as P

QUERY_HEADS = 16
KEY_VALUE_HEADS = 2
HEAD_SIZE = 128
TOP = 8
BLOCK = 16
PREFIX_SLOTS = 32


EPS = 1e-06
NEG_FILL = -1e30


def rms_forward(row_block, gain_vec):
    values = row_block.astype(jnp.float32)
    inverse = lax.rsqrt(jnp.mean(values * values, axis=-1, keepdims=True) + EPS)
    return (values * inverse * gain_vec, inverse)


def rms_backward(row_block, gain_vec, inverse, upstream):
    scaled_rows = row_block.astype(jnp.float32) * inverse
    weighted = upstream * gain_vec
    inner_mean = jnp.mean(weighted * scaled_rows, axis=-1, keepdims=True)
    return inverse * (weighted - scaled_rows * inner_mean)


def attend_forward(queries, key_rows, value_rows, usable):
    factor = queries.shape[-1] ** (-0.5)
    scores = (
        jnp.einsum("sbhd,skd->shbk", queries.astype(jnp.float32), key_rows.astype(jnp.float32))
        * factor
    )
    scores = jnp.where(usable[:, None, None, :], scores, NEG_FILL)
    highest = jnp.max(scores, axis=-1, keepdims=True)
    exponent_terms = jnp.exp(scores - highest)
    probabilities = exponent_terms / jnp.sum(exponent_terms, axis=-1, keepdims=True)
    probs_low = probabilities.astype(jnp.bfloat16)
    attended = jnp.einsum(
        "shbk,skd->sbhd", probs_low.astype(jnp.float32), value_rows.astype(jnp.float32)
    )
    return (probabilities, probs_low, attended.astype(jnp.bfloat16))


def attend_backward(queries, key_rows, value_rows, probabilities, probs_low, grad_attended):
    factor = queries.shape[-1] ** (-0.5)
    grad_probs = jnp.einsum(
        "sbhd,skd->shbk", grad_attended.astype(jnp.float32), value_rows.astype(jnp.float32)
    )
    inner_sum = jnp.sum(probabilities * grad_probs, axis=-1, keepdims=True)
    grad_scores = (probabilities * (grad_probs - inner_sum) * factor).astype(jnp.bfloat16)
    grad_queries = jnp.einsum(
        "shbk,skd->sbhd", grad_scores.astype(jnp.float32), key_rows.astype(jnp.float32)
    )
    grad_keys = jnp.einsum(
        "shbk,sbhd->skd", grad_scores.astype(jnp.float32), queries.astype(jnp.float32)
    )
    grad_values = jnp.einsum(
        "shbk,sbhd->skd", probs_low.astype(jnp.float32), grad_attended.astype(jnp.float32)
    )
    return (grad_queries.astype(jnp.bfloat16), grad_keys, grad_values)


def attention_forward(
    row_block,
    query_weights,
    kv_weights,
    own_kv_weights,
    key_cache,
    prefix_value_cache,
    lengths,
    first_head,
):
    heads_here = query_weights.shape[1] // HEAD_SIZE
    query_group_count = QUERY_HEADS // KEY_VALUE_HEADS
    row_count = row_block.shape[0]
    seq_count = row_count // BLOCK
    key_value_width = KEY_VALUE_HEADS * HEAD_SIZE
    kv_first = first_head // query_group_count
    queries = jnp.dot(row_block, query_weights, preferred_element_type=jnp.float32).astype(
        jnp.bfloat16
    )
    queries = queries.reshape(seq_count, BLOCK, heads_here, HEAD_SIZE)
    usable = jnp.concatenate(
        [
            jnp.arange(PREFIX_SLOTS)[None, :] < lengths[:, None],
            jnp.ones((seq_count, BLOCK), dtype=jnp.bool_),
        ],
        axis=1,
    )
    kv_now = kv_first + 0
    pair_weights = jnp.concatenate(
        [
            lax.dynamic_slice_in_dim(kv_weights, kv_now * HEAD_SIZE, HEAD_SIZE, 1),
            lax.dynamic_slice_in_dim(
                kv_weights, key_value_width + kv_now * HEAD_SIZE, HEAD_SIZE, 1
            ),
        ],
        axis=1,
    )
    own_rows = jnp.dot(row_block, own_kv_weights, preferred_element_type=jnp.float32).astype(
        jnp.bfloat16
    )
    kv_rows = lax.all_gather(own_rows, "head", axis=1, tiled=True)
    pair_rows = jnp.concatenate(
        [
            lax.dynamic_slice_in_dim(kv_rows, kv_now * HEAD_SIZE, HEAD_SIZE, 1),
            lax.dynamic_slice_in_dim(kv_rows, key_value_width + kv_now * HEAD_SIZE, HEAD_SIZE, 1),
        ],
        axis=1,
    )
    key_rows = jnp.concatenate(
        [
            lax.dynamic_slice_in_dim(key_cache, kv_now * HEAD_SIZE, HEAD_SIZE, 2),
            pair_rows[:, :HEAD_SIZE].reshape(seq_count, BLOCK, HEAD_SIZE),
        ],
        axis=1,
    )
    value_rows = jnp.concatenate(
        [
            lax.dynamic_slice_in_dim(prefix_value_cache, kv_now * HEAD_SIZE, HEAD_SIZE, 2),
            pair_rows[:, HEAD_SIZE:].reshape(seq_count, BLOCK, HEAD_SIZE),
        ],
        axis=1,
    )
    probabilities, probs_low, attended = attend_forward(queries, key_rows, value_rows, usable)
    saved = [(queries, key_rows, value_rows, probabilities, probs_low, pair_weights)]
    joined = attended.reshape(row_count, heads_here * HEAD_SIZE)
    return (joined, saved)


def attention_backward(grad_rows, query_weights, output_weights, saved):
    heads_here = query_weights.shape[1] // HEAD_SIZE
    row_count = grad_rows.shape[0]
    seq_count = row_count // BLOCK
    grad_attn = jnp.einsum(
        "td,fd->tf", grad_rows, output_weights, preferred_element_type=jnp.float32
    ).astype(jnp.bfloat16)
    grad_attn = grad_attn.reshape(seq_count, BLOCK, heads_here, HEAD_SIZE)
    query_part, key_rows, value_rows, probabilities, probs_low, pair_weights = saved[0]
    grad_queries, grad_keys, grad_values = attend_backward(
        query_part, key_rows, value_rows, probabilities, probs_low, grad_attn
    )
    block_grads = jnp.concatenate(
        [
            grad_keys[:, PREFIX_SLOTS:].reshape(row_count, HEAD_SIZE),
            grad_values[:, PREFIX_SLOTS:].reshape(row_count, HEAD_SIZE),
        ],
        axis=1,
    )
    running = jnp.einsum(
        "tc,dc->td", block_grads, pair_weights.astype(jnp.float32), precision=lax.Precision.HIGHEST
    )
    query_flat = grad_queries.reshape(row_count, heads_here * HEAD_SIZE)
    return running + jnp.einsum(
        "tf,df->td", query_flat, query_weights, preferred_element_type=jnp.float32
    )


def head_rows(row_block):
    return lax.all_gather(row_block, "head", axis=0, tiled=True)


def head_sums(partial_rows):
    return lax.psum_scatter(partial_rows, "head", scatter_dimension=0, tiled=True)


def to_experts(outgoing):
    return lax.all_to_all(outgoing, ("expert", "head"), split_axis=0, concat_axis=0, tiled=True)


def from_experts(results):
    return lax.all_to_all(results, ("expert", "head"), split_axis=0, concat_axis=0, tiled=True)


def body(
    hidden_in,
    out_grad,
    loss_mask,
    expert_ids,
    gate_weights,
    cache_lengths,
    key_cache,
    prefix_value_cache,
    attn_gain,
    moe_gain,
    w_query,
    key_value_weight,
    w_output,
    w_gate,
    w_up,
    w_down,
):
    highest_prec = lax.Precision.HIGHEST
    owned = hidden_in.shape[0]
    width = hidden_in.shape[1]
    normed_one, inverse_one = rms_forward(hidden_in, attn_gain)
    attn_rows = normed_one.astype(jnp.bfloat16)
    kv_full = lax.all_gather(key_value_weight, "head", axis=1, tiled=True)
    heads_here = w_query.shape[1] // HEAD_SIZE
    first_head = lax.axis_index("head") * heads_here
    gathered_rows = head_rows(attn_rows)
    attended, saved = attention_forward(
        gathered_rows, w_query, kv_full, key_value_weight, key_cache, prefix_value_cache, cache_lengths, first_head
    )
    mixed = head_sums(jnp.dot(attended, w_output, preferred_element_type=jnp.float32))
    hidden = (hidden_in.astype(jnp.float32) + mixed).astype(jnp.bfloat16)
    normed_two, inverse_two = rms_forward(hidden, moe_gain)
    moe_rows = normed_two.astype(jnp.bfloat16)
    device_count = lax.axis_size("expert") * lax.axis_size("head")
    capacity = (owned * TOP * 4 + 3 * device_count - 1) // (3 * device_count)
    slot_total = device_count * capacity
    flat_ids = expert_ids.reshape(-1)
    one_hot = (flat_ids[:, None] == jnp.arange(device_count, dtype=jnp.int32)[None, :]).astype(
        jnp.int32
    )
    earlier = jnp.cumsum(one_hot, axis=0) - one_hot
    position = jnp.sum(earlier * one_hot, axis=1)
    target = flat_ids * capacity + position
    matched = (jnp.arange(slot_total, dtype=jnp.int32)[:, None] == target[None, :]).reshape(
        device_count, capacity, owned, TOP
    )
    placement = jnp.any(matched, axis=3).astype(jnp.bfloat16)
    weighting = jnp.sum(jnp.where(matched, gate_weights[None, None, :, :], 0.0), axis=3)
    cotangent = out_grad.astype(jnp.float32) * loss_mask.astype(jnp.float32)[:, None]
    outgoing = jnp.einsum(
        "dct,tw->dcw", placement, moe_rows, preferred_element_type=jnp.float32
    ).astype(jnp.bfloat16)
    grad_out = jnp.einsum(
        "dct,tw->dcw", weighting, cotangent, precision=highest_prec
    ).astype(jnp.bfloat16)
    rows_in = to_experts(outgoing)
    grads_in = to_experts(grad_out)
    gate_matrix = w_gate[0]
    up_matrix = w_up[0]
    down_matrix = w_down[0]
    gate_pre = jnp.einsum("scw,wf->scf", rows_in, gate_matrix, preferred_element_type=jnp.float32)
    up_pre = jnp.einsum("scw,wf->scf", rows_in, up_matrix, preferred_element_type=jnp.float32)
    sigma = jax.nn.sigmoid(gate_pre)
    activated = (gate_pre * sigma * up_pre).astype(jnp.bfloat16)
    result = jnp.einsum(
        "scf,fw->scw", activated, down_matrix, preferred_element_type=jnp.float32
    ).astype(jnp.bfloat16)
    grad_act = jnp.einsum(
        "scw,fw->scf", grads_in, down_matrix, preferred_element_type=jnp.float32
    )
    grad_gate = (grad_act * up_pre * sigma * (1.0 + gate_pre * (1.0 - sigma))).astype(jnp.bfloat16)
    grad_up = (grad_act * gate_pre * sigma).astype(jnp.bfloat16)
    grad_back = jnp.einsum(
        "scf,wf->scw", grad_gate, gate_matrix, preferred_element_type=jnp.float32
    )
    grad_back = grad_back + jnp.einsum(
        "scf,wf->scw", grad_up, up_matrix, preferred_element_type=jnp.float32
    )
    grad_back = grad_back.astype(jnp.bfloat16)
    result_home = from_experts(result)
    grad_home = from_experts(grad_back)
    moe_sum = jnp.einsum(
        "dct,dcw->tw",
        weighting,
        result_home.astype(jnp.float32),
        precision=highest_prec,
    )
    layer_out = (hidden.astype(jnp.float32) + moe_sum).astype(jnp.bfloat16)
    grad_moe = jnp.einsum(
        "dct,dcw->tw", placement, grad_home, preferred_element_type=jnp.float32
    )
    grad_hidden = cotangent + rms_backward(hidden, moe_gain, inverse_two, grad_moe)
    grad_low = grad_hidden.astype(jnp.bfloat16)
    grad_gathered = head_rows(grad_low)
    grad_attn_rows = head_sums(attention_backward(grad_gathered, w_query, w_output, saved))
    input_grad = (
        grad_hidden + rms_backward(hidden_in, attn_gain, inverse_one, grad_attn_rows)
    ).astype(jnp.bfloat16)
    return (layer_out, input_grad)


def solution(mesh):
    in_specs = (
        P(("groups", "expert", "head"), None),
        P(("groups", "expert", "head"), None),
        P(("groups", "expert", "head")),
        P(("groups", "expert", "head"), None),
        P(("groups", "expert", "head"), None),
        P(("groups", "expert")),
        P(("groups", "expert"), None, None),
        P(("groups", "expert"), None, None),
        P(),
        P(),
        P(None, "head"),
        P(None, "head"),
        P("head", None),
        P(("expert", "head"), None, None),
        P(("expert", "head"), None, None),
        P(("expert", "head"), None, None),
    )
    out_specs = (P(("groups", "expert", "head"), None), P(("groups", "expert", "head"), None))
    return jax.shard_map(body, mesh=mesh, in_specs=in_specs, out_specs=out_specs, check_vma=False)
```

```python
import jax
import jax.numpy as jnp
from jax import lax
from jax.sharding import PartitionSpec as P

QUERY_HEADS = 16
KEY_VALUE_HEADS = 2
HEAD_SIZE = 128
TOP = 8
BLOCK = 16
PREFIX_SLOTS = 32


EPS = 1e-06
NEG_FILL = -1e30


def rms_forward(row_block, gain_vec):
    values = row_block.astype(jnp.float32)
    inverse = lax.rsqrt(jnp.mean(values * values, axis=-1, keepdims=True) + EPS)
    return (values * inverse * gain_vec, inverse)


def rms_backward(row_block, gain_vec, inverse, upstream):
    scaled_rows = row_block.astype(jnp.float32) * inverse
    weighted = upstream * gain_vec
    inner_mean = jnp.mean(weighted * scaled_rows, axis=-1, keepdims=True)
    return inverse * (weighted - scaled_rows * inner_mean)


def attend_forward(queries, key_rows, value_rows, usable):
    factor = queries.shape[-1] ** (-0.5)
    scores = (
        jnp.einsum("sbhd,skd->shbk", queries.astype(jnp.float32), key_rows.astype(jnp.float32))
        * factor
    )
    scores = jnp.where(usable[:, None, None, :], scores, NEG_FILL)
    highest = jnp.max(scores, axis=-1, keepdims=True)
    exponent_terms = jnp.exp(scores - highest)
    probabilities = exponent_terms / jnp.sum(exponent_terms, axis=-1, keepdims=True)
    probs_low = probabilities.astype(jnp.bfloat16)
    attended = jnp.einsum(
        "shbk,skd->sbhd", probs_low.astype(jnp.float32), value_rows.astype(jnp.float32)
    )
    return (probabilities, probs_low, attended.astype(jnp.bfloat16))


def attend_backward(queries, key_rows, value_rows, probabilities, probs_low, grad_attended):
    factor = queries.shape[-1] ** (-0.5)
    grad_probs = jnp.einsum(
        "sbhd,skd->shbk", grad_attended.astype(jnp.float32), value_rows.astype(jnp.float32)
    )
    inner_sum = jnp.sum(probabilities * grad_probs, axis=-1, keepdims=True)
    grad_scores = (probabilities * (grad_probs - inner_sum) * factor).astype(jnp.bfloat16)
    grad_queries = jnp.einsum(
        "shbk,skd->sbhd", grad_scores.astype(jnp.float32), key_rows.astype(jnp.float32)
    )
    grad_keys = jnp.einsum(
        "shbk,sbhd->skd", grad_scores.astype(jnp.float32), queries.astype(jnp.float32)
    )
    grad_values = jnp.einsum(
        "shbk,sbhd->skd", probs_low.astype(jnp.float32), grad_attended.astype(jnp.float32)
    )
    return (grad_queries.astype(jnp.bfloat16), grad_keys, grad_values)


def attention_forward(
    row_block,
    query_weights,
    own_kv_weights,
    key_cache,
    prefix_value_cache,
    lengths,
    first_head,
):
    heads_here = query_weights.shape[1] // HEAD_SIZE
    query_group_count = QUERY_HEADS // KEY_VALUE_HEADS
    row_count = row_block.shape[0]
    seq_count = row_count // BLOCK
    key_value_width = KEY_VALUE_HEADS * HEAD_SIZE
    kv_first = first_head // query_group_count
    queries = jnp.dot(row_block, query_weights, preferred_element_type=jnp.float32).astype(
        jnp.bfloat16
    )
    queries = queries.reshape(seq_count, BLOCK, heads_here, HEAD_SIZE)
    usable = jnp.concatenate(
        [
            jnp.arange(PREFIX_SLOTS)[None, :] < lengths[:, None],
            jnp.ones((seq_count, BLOCK), dtype=jnp.bool_),
        ],
        axis=1,
    )
    kv_now = kv_first + 0
    own_rows = jnp.dot(row_block, own_kv_weights, preferred_element_type=jnp.float32).astype(
        jnp.bfloat16
    )
    kv_rows = lax.all_gather(own_rows, "head", axis=1, tiled=True)
    pair_rows = jnp.concatenate(
        [
            lax.dynamic_slice_in_dim(kv_rows, kv_now * HEAD_SIZE, HEAD_SIZE, 1),
            lax.dynamic_slice_in_dim(kv_rows, key_value_width + kv_now * HEAD_SIZE, HEAD_SIZE, 1),
        ],
        axis=1,
    )
    key_rows = jnp.concatenate(
        [
            lax.dynamic_slice_in_dim(key_cache, kv_now * HEAD_SIZE, HEAD_SIZE, 2),
            pair_rows[:, :HEAD_SIZE].reshape(seq_count, BLOCK, HEAD_SIZE),
        ],
        axis=1,
    )
    value_rows = jnp.concatenate(
        [
            lax.dynamic_slice_in_dim(prefix_value_cache, kv_now * HEAD_SIZE, HEAD_SIZE, 2),
            pair_rows[:, HEAD_SIZE:].reshape(seq_count, BLOCK, HEAD_SIZE),
        ],
        axis=1,
    )
    probabilities, probs_low, attended = attend_forward(queries, key_rows, value_rows, usable)
    saved = [(queries, key_rows, value_rows, probabilities, probs_low)]
    joined = attended.reshape(row_count, heads_here * HEAD_SIZE)
    return (joined, saved)


def attention_backward(grad_rows, query_weights, output_weights, saved):
    heads_here = query_weights.shape[1] // HEAD_SIZE
    row_count = grad_rows.shape[0]
    seq_count = row_count // BLOCK
    grad_attn = jnp.einsum(
        "td,fd->tf", grad_rows, output_weights, preferred_element_type=jnp.float32
    ).astype(jnp.bfloat16)
    grad_attn = grad_attn.reshape(seq_count, BLOCK, heads_here, HEAD_SIZE)
    query_part, key_rows, value_rows, probabilities, probs_low, pair_weights = saved[0]
    grad_queries, grad_keys, grad_values = attend_backward(
        query_part, key_rows, value_rows, probabilities, probs_low, grad_attn
    )
    block_grads = jnp.concatenate(
        [
            grad_keys[:, PREFIX_SLOTS:].reshape(row_count, HEAD_SIZE),
            grad_values[:, PREFIX_SLOTS:].reshape(row_count, HEAD_SIZE),
        ],
        axis=1,
    )
    running = jnp.einsum(
        "tc,dc->td", block_grads, pair_weights.astype(jnp.float32), precision=lax.Precision.HIGHEST
    )
    query_flat = grad_queries.reshape(row_count, heads_here * HEAD_SIZE)
    return running + jnp.einsum(
        "tf,df->td", query_flat, query_weights, preferred_element_type=jnp.float32
    )


def head_rows(row_block):
    return lax.all_gather(row_block, "head", axis=0, tiled=True)


def head_sums(partial_rows):
    return lax.psum_scatter(partial_rows, "head", scatter_dimension=0, tiled=True)


def to_experts(outgoing):
    return lax.all_to_all(outgoing, ("expert", "head"), split_axis=0, concat_axis=0, tiled=True)


def from_experts(results):
    return lax.all_to_all(results, ("expert", "head"), split_axis=0, concat_axis=0, tiled=True)


def body(
    hidden_in,
    out_grad,
    loss_mask,
    expert_ids,
    gate_weights,
    cache_lengths,
    key_cache,
    prefix_value_cache,
    attn_gain,
    moe_gain,
    w_query,
    key_value_weight,
    w_output,
    w_gate,
    w_up,
    w_down,
):
    highest_prec = lax.Precision.HIGHEST
    owned = hidden_in.shape[0]
    width = hidden_in.shape[1]
    normed_one, inverse_one = rms_forward(hidden_in, attn_gain)
    attn_rows = normed_one.astype(jnp.bfloat16)
    kv_full = lax.all_gather(key_value_weight, "head", axis=1, tiled=True)
    heads_here = w_query.shape[1] // HEAD_SIZE
    first_head = lax.axis_index("head") * heads_here
    gathered_rows = head_rows(attn_rows)
    attended, saved = attention_forward(
        gathered_rows, w_query, key_value_weight, key_cache, prefix_value_cache, cache_lengths, first_head
    )
    partial_mixed = jnp.dot(attended, w_output, preferred_element_type=jnp.float32)
    partial_mixed, kv_full = lax.optimization_barrier((partial_mixed, kv_full))
    mixed = head_sums(partial_mixed)
    hidden = (hidden_in.astype(jnp.float32) + mixed).astype(jnp.bfloat16)
    normed_two, inverse_two = rms_forward(hidden, moe_gain)
    moe_rows = normed_two.astype(jnp.bfloat16)
    device_count = lax.axis_size("expert") * lax.axis_size("head")
    capacity = (owned * TOP * 4 + 3 * device_count - 1) // (3 * device_count)
    slot_total = device_count * capacity
    flat_ids = expert_ids.reshape(-1)
    one_hot = (flat_ids[:, None] == jnp.arange(device_count, dtype=jnp.int32)[None, :]).astype(
        jnp.int32
    )
    earlier = jnp.cumsum(one_hot, axis=0) - one_hot
    position = jnp.sum(earlier * one_hot, axis=1)
    target = flat_ids * capacity + position
    matched = (jnp.arange(slot_total, dtype=jnp.int32)[:, None] == target[None, :]).reshape(
        device_count, capacity, owned, TOP
    )
    placement = jnp.any(matched, axis=3).astype(jnp.bfloat16)
    weighting = jnp.sum(jnp.where(matched, gate_weights[None, None, :, :], 0.0), axis=3)
    cotangent = out_grad.astype(jnp.float32) * loss_mask.astype(jnp.float32)[:, None]
    outgoing = jnp.einsum(
        "dct,tw->dcw", placement, moe_rows, preferred_element_type=jnp.float32
    ).astype(jnp.bfloat16)
    grad_out = jnp.einsum(
        "dct,tw->dcw", weighting, cotangent, precision=highest_prec
    ).astype(jnp.bfloat16)
    rows_in = to_experts(outgoing)
    kv_now = first_head // (QUERY_HEADS // KEY_VALUE_HEADS)
    key_value_width = KEY_VALUE_HEADS * HEAD_SIZE
    pair_weights = jnp.concatenate(
        [
            lax.dynamic_slice_in_dim(kv_full, kv_now * HEAD_SIZE, HEAD_SIZE, 1),
            lax.dynamic_slice_in_dim(kv_full, key_value_width + kv_now * HEAD_SIZE, HEAD_SIZE, 1),
        ],
        axis=1,
    )
    saved = [saved[0][:5] + (pair_weights,)]
    grads_in = to_experts(grad_out)
    gate_matrix = w_gate[0]
    up_matrix = w_up[0]
    down_matrix = w_down[0]
    gate_pre = jnp.einsum("scw,wf->scf", rows_in, gate_matrix, preferred_element_type=jnp.float32)
    up_pre = jnp.einsum("scw,wf->scf", rows_in, up_matrix, preferred_element_type=jnp.float32)
    sigma = jax.nn.sigmoid(gate_pre)
    activated = (gate_pre * sigma * up_pre).astype(jnp.bfloat16)
    result = jnp.einsum(
        "scf,fw->scw", activated, down_matrix, preferred_element_type=jnp.float32
    ).astype(jnp.bfloat16)
    grad_act = jnp.einsum(
        "scw,fw->scf", grads_in, down_matrix, preferred_element_type=jnp.float32
    )
    grad_gate = (grad_act * up_pre * sigma * (1.0 + gate_pre * (1.0 - sigma))).astype(jnp.bfloat16)
    grad_up = (grad_act * gate_pre * sigma).astype(jnp.bfloat16)
    grad_back = jnp.einsum(
        "scf,wf->scw", grad_gate, gate_matrix, preferred_element_type=jnp.float32
    )
    grad_back = grad_back + jnp.einsum(
        "scf,wf->scw", grad_up, up_matrix, preferred_element_type=jnp.float32
    )
    grad_back = grad_back.astype(jnp.bfloat16)
    result_home = from_experts(result)
    grad_home = from_experts(grad_back)
    moe_sum = jnp.einsum(
        "dct,dcw->tw",
        weighting,
        result_home.astype(jnp.float32),
        precision=highest_prec,
    )
    layer_out = (hidden.astype(jnp.float32) + moe_sum).astype(jnp.bfloat16)
    grad_moe = jnp.einsum(
        "dct,dcw->tw", placement, grad_home, preferred_element_type=jnp.float32
    )
    grad_hidden = cotangent + rms_backward(hidden, moe_gain, inverse_two, grad_moe)
    grad_low = grad_hidden.astype(jnp.bfloat16)
    grad_gathered = head_rows(grad_low)
    grad_attn_rows = head_sums(attention_backward(grad_gathered, w_query, w_output, saved))
    input_grad = (
        grad_hidden + rms_backward(hidden_in, attn_gain, inverse_one, grad_attn_rows)
    ).astype(jnp.bfloat16)
    return (layer_out, input_grad)


def solution(mesh):
    in_specs = (
        P(("groups", "expert", "head"), None),
        P(("groups", "expert", "head"), None),
        P(("groups", "expert", "head")),
        P(("groups", "expert", "head"), None),
        P(("groups", "expert", "head"), None),
        P(("groups", "expert")),
        P(("groups", "expert"), None, None),
        P(("groups", "expert"), None, None),
        P(),
        P(),
        P(None, "head"),
        P(None, "head"),
        P("head", None),
        P(("expert", "head"), None, None),
        P(("expert", "head"), None, None),
        P(("expert", "head"), None, None),
    )
    out_specs = (P(("groups", "expert", "head"), None), P(("groups", "expert", "head"), None))
    return jax.shard_map(body, mesh=mesh, in_specs=in_specs, out_specs=out_specs, check_vma=False)
```

```python
import jax
import jax.numpy as jnp
from jax import lax
from jax.sharding import PartitionSpec as P

QUERY_HEADS = 16
KEY_VALUE_HEADS = 2
HEAD_SIZE = 128
TOP = 8
BLOCK = 16
PREFIX_SLOTS = 32


EPS = 1e-06
NEG_FILL = -1e30


def rms_forward(row_block, gain_vec):
    values = row_block.astype(jnp.float32)
    inverse = lax.rsqrt(jnp.mean(values * values, axis=-1, keepdims=True) + EPS)
    return (values * inverse * gain_vec, inverse)


def rms_backward(row_block, gain_vec, inverse, upstream):
    scaled_rows = row_block.astype(jnp.float32) * inverse
    weighted = upstream * gain_vec
    inner_mean = jnp.mean(weighted * scaled_rows, axis=-1, keepdims=True)
    return inverse * (weighted - scaled_rows * inner_mean)


def attend_forward(queries, key_rows, value_rows, usable):
    factor = queries.shape[-1] ** (-0.5)
    scores = (
        jnp.einsum("sbhd,skd->shbk", queries.astype(jnp.float32), key_rows.astype(jnp.float32))
        * factor
    )
    scores = jnp.where(usable[:, None, None, :], scores, NEG_FILL)
    highest = jnp.max(scores, axis=-1, keepdims=True)
    exponent_terms = jnp.exp(scores - highest)
    probabilities = exponent_terms / jnp.sum(exponent_terms, axis=-1, keepdims=True)
    probs_low = probabilities.astype(jnp.bfloat16)
    attended = jnp.einsum(
        "shbk,skd->sbhd", probs_low.astype(jnp.float32), value_rows.astype(jnp.float32)
    )
    return (probabilities, probs_low, attended.astype(jnp.bfloat16))


def attend_backward(queries, key_rows, value_rows, probabilities, probs_low, grad_attended):
    factor = queries.shape[-1] ** (-0.5)
    grad_probs = jnp.einsum(
        "sbhd,skd->shbk", grad_attended.astype(jnp.float32), value_rows.astype(jnp.float32)
    )
    inner_sum = jnp.sum(probabilities * grad_probs, axis=-1, keepdims=True)
    grad_scores = (probabilities * (grad_probs - inner_sum) * factor).astype(jnp.bfloat16)
    grad_queries = jnp.einsum(
        "shbk,skd->sbhd", grad_scores.astype(jnp.float32), key_rows.astype(jnp.float32)
    )
    grad_keys = jnp.einsum(
        "shbk,sbhd->skd", grad_scores.astype(jnp.float32), queries.astype(jnp.float32)
    )
    grad_values = jnp.einsum(
        "shbk,sbhd->skd", probs_low.astype(jnp.float32), grad_attended.astype(jnp.float32)
    )
    return (grad_queries.astype(jnp.bfloat16), grad_keys, grad_values)


def attention_forward(
    row_block,
    query_weights,
    own_kv_weights,
    key_cache,
    prefix_value_cache,
    lengths,
    first_head,
):
    heads_here = query_weights.shape[1] // HEAD_SIZE
    query_group_count = QUERY_HEADS // KEY_VALUE_HEADS
    row_count = row_block.shape[0]
    seq_count = row_count // BLOCK
    key_value_width = KEY_VALUE_HEADS * HEAD_SIZE
    kv_first = first_head // query_group_count
    queries = jnp.dot(row_block, query_weights, preferred_element_type=jnp.float32).astype(
        jnp.bfloat16
    )
    queries = queries.reshape(seq_count, BLOCK, heads_here, HEAD_SIZE)
    usable = jnp.concatenate(
        [
            jnp.arange(PREFIX_SLOTS)[None, :] < lengths[:, None],
            jnp.ones((seq_count, BLOCK), dtype=jnp.bool_),
        ],
        axis=1,
    )
    kv_now = kv_first + 0
    own_rows = jnp.dot(row_block, own_kv_weights, preferred_element_type=jnp.float32).astype(
        jnp.bfloat16
    )
    kv_rows = lax.all_gather(own_rows, "head", axis=1, tiled=True)
    pair_rows = jnp.concatenate(
        [
            lax.dynamic_slice_in_dim(kv_rows, kv_now * HEAD_SIZE, HEAD_SIZE, 1),
            lax.dynamic_slice_in_dim(kv_rows, key_value_width + kv_now * HEAD_SIZE, HEAD_SIZE, 1),
        ],
        axis=1,
    )
    key_rows = jnp.concatenate(
        [
            lax.dynamic_slice_in_dim(key_cache, kv_now * HEAD_SIZE, HEAD_SIZE, 2),
            pair_rows[:, :HEAD_SIZE].reshape(seq_count, BLOCK, HEAD_SIZE),
        ],
        axis=1,
    )
    value_rows = jnp.concatenate(
        [
            lax.dynamic_slice_in_dim(prefix_value_cache, kv_now * HEAD_SIZE, HEAD_SIZE, 2),
            pair_rows[:, HEAD_SIZE:].reshape(seq_count, BLOCK, HEAD_SIZE),
        ],
        axis=1,
    )
    probabilities, probs_low, attended = attend_forward(queries, key_rows, value_rows, usable)
    saved = [(queries, key_rows, value_rows, probabilities, probs_low)]
    joined = attended.reshape(row_count, heads_here * HEAD_SIZE)
    return (joined, saved)


def attention_backward(grad_rows, query_weights, output_weights, own_kv_weights, saved, kv_now):
    heads_here = query_weights.shape[1] // HEAD_SIZE
    row_count = grad_rows.shape[0]
    seq_count = row_count // BLOCK
    key_value_width = KEY_VALUE_HEADS * HEAD_SIZE
    grad_attn = jnp.einsum(
        "td,fd->tf", grad_rows, output_weights, preferred_element_type=jnp.float32
    ).astype(jnp.bfloat16)
    grad_attn = grad_attn.reshape(seq_count, BLOCK, heads_here, HEAD_SIZE)
    query_part, key_rows, value_rows, probabilities, probs_low = saved[0]
    grad_queries, grad_keys, grad_values = attend_backward(
        query_part, key_rows, value_rows, probabilities, probs_low, grad_attn
    )
    placed = jnp.zeros((row_count, 2 * key_value_width), jnp.float32)
    placed = lax.dynamic_update_slice_in_dim(
        placed, grad_keys[:, PREFIX_SLOTS:].reshape(row_count, HEAD_SIZE), kv_now * HEAD_SIZE, 1
    )
    placed = lax.dynamic_update_slice_in_dim(
        placed,
        grad_values[:, PREFIX_SLOTS:].reshape(row_count, HEAD_SIZE),
        key_value_width + kv_now * HEAD_SIZE,
        1,
    )
    own_grads = lax.psum_scatter(placed, "head", scatter_dimension=1, tiled=True)
    running = jnp.einsum(
        "tc,dc->td", own_grads, own_kv_weights.astype(jnp.float32), precision=lax.Precision.HIGHEST
    )
    query_flat = grad_queries.reshape(row_count, heads_here * HEAD_SIZE)
    return running + jnp.einsum(
        "tf,df->td", query_flat, query_weights, preferred_element_type=jnp.float32
    )


def head_rows(row_block):
    return lax.all_gather(row_block, "head", axis=0, tiled=True)


def head_sums(partial_rows):
    return lax.psum_scatter(partial_rows, "head", scatter_dimension=0, tiled=True)


def to_experts(outgoing):
    return lax.all_to_all(outgoing, ("expert", "head"), split_axis=0, concat_axis=0, tiled=True)


def from_experts(results):
    return lax.all_to_all(results, ("expert", "head"), split_axis=0, concat_axis=0, tiled=True)


def body(
    hidden_in,
    out_grad,
    loss_mask,
    expert_ids,
    gate_weights,
    cache_lengths,
    key_cache,
    prefix_value_cache,
    attn_gain,
    moe_gain,
    w_query,
    key_value_weight,
    w_output,
    w_gate,
    w_up,
    w_down,
):
    highest_prec = lax.Precision.HIGHEST
    owned = hidden_in.shape[0]
    width = hidden_in.shape[1]
    normed_one, inverse_one = rms_forward(hidden_in, attn_gain)
    attn_rows = normed_one.astype(jnp.bfloat16)
    heads_here = w_query.shape[1] // HEAD_SIZE
    first_head = lax.axis_index("head") * heads_here
    gathered_rows = head_rows(attn_rows)
    attended, saved = attention_forward(
        gathered_rows, w_query, key_value_weight, key_cache, prefix_value_cache, cache_lengths, first_head
    )
    mixed = head_sums(jnp.dot(attended, w_output, preferred_element_type=jnp.float32))
    hidden = (hidden_in.astype(jnp.float32) + mixed).astype(jnp.bfloat16)
    normed_two, inverse_two = rms_forward(hidden, moe_gain)
    moe_rows = normed_two.astype(jnp.bfloat16)
    device_count = lax.axis_size("expert") * lax.axis_size("head")
    capacity = (owned * TOP * 4 + 3 * device_count - 1) // (3 * device_count)
    slot_total = device_count * capacity
    flat_ids = expert_ids.reshape(-1)
    one_hot = (flat_ids[:, None] == jnp.arange(device_count, dtype=jnp.int32)[None, :]).astype(
        jnp.int32
    )
    earlier = jnp.cumsum(one_hot, axis=0) - one_hot
    position = jnp.sum(earlier * one_hot, axis=1)
    target = flat_ids * capacity + position
    matched = (jnp.arange(slot_total, dtype=jnp.int32)[:, None] == target[None, :]).reshape(
        device_count, capacity, owned, TOP
    )
    placement = jnp.any(matched, axis=3).astype(jnp.bfloat16)
    weighting = jnp.sum(jnp.where(matched, gate_weights[None, None, :, :], 0.0), axis=3)
    cotangent = out_grad.astype(jnp.float32) * loss_mask.astype(jnp.float32)[:, None]
    outgoing = jnp.einsum(
        "dct,tw->dcw", placement, moe_rows, preferred_element_type=jnp.float32
    ).astype(jnp.bfloat16)
    grad_out = jnp.einsum(
        "dct,tw->dcw", weighting, cotangent, precision=highest_prec
    ).astype(jnp.bfloat16)
    rows_in = to_experts(outgoing)
    grads_in = to_experts(grad_out)
    gate_matrix = w_gate[0]
    up_matrix = w_up[0]
    down_matrix = w_down[0]
    gate_pre = jnp.einsum("scw,wf->scf", rows_in, gate_matrix, preferred_element_type=jnp.float32)
    up_pre = jnp.einsum("scw,wf->scf", rows_in, up_matrix, preferred_element_type=jnp.float32)
    sigma = jax.nn.sigmoid(gate_pre)
    activated = (gate_pre * sigma * up_pre).astype(jnp.bfloat16)
    result = jnp.einsum(
        "scf,fw->scw", activated, down_matrix, preferred_element_type=jnp.float32
    ).astype(jnp.bfloat16)
    grad_act = jnp.einsum(
        "scw,fw->scf", grads_in, down_matrix, preferred_element_type=jnp.float32
    )
    grad_gate = (grad_act * up_pre * sigma * (1.0 + gate_pre * (1.0 - sigma))).astype(jnp.bfloat16)
    grad_up = (grad_act * gate_pre * sigma).astype(jnp.bfloat16)
    grad_back = jnp.einsum(
        "scf,wf->scw", grad_gate, gate_matrix, preferred_element_type=jnp.float32
    )
    grad_back = grad_back + jnp.einsum(
        "scf,wf->scw", grad_up, up_matrix, preferred_element_type=jnp.float32
    )
    grad_back = grad_back.astype(jnp.bfloat16)
    result_home = from_experts(result)
    grad_home = from_experts(grad_back)
    moe_sum = jnp.einsum(
        "dct,dcw->tw",
        weighting,
        result_home.astype(jnp.float32),
        precision=highest_prec,
    )
    layer_out = (hidden.astype(jnp.float32) + moe_sum).astype(jnp.bfloat16)
    grad_moe = jnp.einsum(
        "dct,dcw->tw", placement, grad_home, preferred_element_type=jnp.float32
    )
    grad_hidden = cotangent + rms_backward(hidden, moe_gain, inverse_two, grad_moe)
    grad_low = grad_hidden.astype(jnp.bfloat16)
    grad_gathered = head_rows(grad_low)
    grad_attn_rows = head_sums(
        attention_backward(
            grad_gathered,
            w_query,
            w_output,
            key_value_weight,
            saved,
            first_head // (QUERY_HEADS // KEY_VALUE_HEADS),
        )
    )
    input_grad = (
        grad_hidden + rms_backward(hidden_in, attn_gain, inverse_one, grad_attn_rows)
    ).astype(jnp.bfloat16)
    return (layer_out, input_grad)


def solution(mesh):
    in_specs = (
        P(("groups", "expert", "head"), None),
        P(("groups", "expert", "head"), None),
        P(("groups", "expert", "head")),
        P(("groups", "expert", "head"), None),
        P(("groups", "expert", "head"), None),
        P(("groups", "expert")),
        P(("groups", "expert"), None, None),
        P(("groups", "expert"), None, None),
        P(),
        P(),
        P(None, "head"),
        P(None, "head"),
        P("head", None),
        P(("expert", "head"), None, None),
        P(("expert", "head"), None, None),
        P(("expert", "head"), None, None),
    )
    out_specs = (P(("groups", "expert", "head"), None), P(("groups", "expert", "head"), None))
    return jax.shard_map(body, mesh=mesh, in_specs=in_specs, out_specs=out_specs, check_vma=False)
```

```python
import jax
import jax.numpy as jnp
from jax import lax
from jax.sharding import PartitionSpec as P

QUERY_HEADS = 16
KEY_VALUE_HEADS = 2
HEAD_SIZE = 128
TOP = 8
BLOCK = 16
PREFIX_SLOTS = 32


EPS = 1e-06
NEG_FILL = -1e30


def rms_forward(row_block, gain_vec):
    values = row_block.astype(jnp.float32)
    inverse = lax.rsqrt(jnp.mean(values * values, axis=-1, keepdims=True) + EPS)
    return (values * inverse * gain_vec, inverse)


def rms_backward(row_block, gain_vec, inverse, upstream):
    scaled_rows = row_block.astype(jnp.float32) * inverse
    weighted = upstream * gain_vec
    inner_mean = jnp.mean(weighted * scaled_rows, axis=-1, keepdims=True)
    return inverse * (weighted - scaled_rows * inner_mean)


def attend_forward(queries, key_rows, value_rows, usable):
    factor = queries.shape[-1] ** (-0.5)
    scores = (
        jnp.einsum("sbhd,skd->shbk", queries.astype(jnp.float32), key_rows.astype(jnp.float32))
        * factor
    )
    scores = jnp.where(usable[:, None, None, :], scores, NEG_FILL)
    highest = jnp.max(scores, axis=-1, keepdims=True)
    exponent_terms = jnp.exp(scores - highest)
    probabilities = exponent_terms / jnp.sum(exponent_terms, axis=-1, keepdims=True)
    probs_low = probabilities.astype(jnp.bfloat16)
    attended = jnp.einsum(
        "shbk,skd->sbhd", probs_low.astype(jnp.float32), value_rows.astype(jnp.float32)
    )
    return (probabilities, probs_low, attended.astype(jnp.bfloat16))


def attend_backward(queries, key_rows, value_rows, probabilities, probs_low, grad_attended):
    factor = queries.shape[-1] ** (-0.5)
    grad_probs = jnp.einsum(
        "sbhd,skd->shbk", grad_attended.astype(jnp.float32), value_rows.astype(jnp.float32)
    )
    inner_sum = jnp.sum(probabilities * grad_probs, axis=-1, keepdims=True)
    grad_scores = (probabilities * (grad_probs - inner_sum) * factor).astype(jnp.bfloat16)
    grad_queries = jnp.einsum(
        "shbk,skd->sbhd", grad_scores.astype(jnp.float32), key_rows.astype(jnp.float32)
    )
    grad_keys = jnp.einsum(
        "shbk,sbhd->skd", grad_scores.astype(jnp.float32), queries.astype(jnp.float32)
    )
    grad_values = jnp.einsum(
        "shbk,sbhd->skd", probs_low.astype(jnp.float32), grad_attended.astype(jnp.float32)
    )
    return (grad_queries.astype(jnp.bfloat16), grad_keys, grad_values)


def attention_forward(
    row_block,
    query_weights,
    own_kv_weights,
    key_cache,
    prefix_value_cache,
    lengths,
    first_head,
):
    heads_here = query_weights.shape[1] // HEAD_SIZE
    query_group_count = QUERY_HEADS // KEY_VALUE_HEADS
    row_count = row_block.shape[0]
    seq_count = row_count // BLOCK
    key_value_width = KEY_VALUE_HEADS * HEAD_SIZE
    kv_first = first_head // query_group_count
    queries = jnp.dot(row_block, query_weights, preferred_element_type=jnp.float32).astype(
        jnp.bfloat16
    )
    queries = queries.reshape(seq_count, BLOCK, heads_here, HEAD_SIZE)
    usable = jnp.concatenate(
        [
            jnp.arange(PREFIX_SLOTS)[None, :] < lengths[:, None],
            jnp.ones((seq_count, BLOCK), dtype=jnp.bool_),
        ],
        axis=1,
    )
    kv_now = kv_first + 0
    own_rows = jnp.dot(row_block, own_kv_weights, preferred_element_type=jnp.float32).astype(
        jnp.bfloat16
    )
    kv_rows = lax.all_gather(own_rows, "head", axis=1, tiled=True)
    pair_rows = jnp.concatenate(
        [
            lax.dynamic_slice_in_dim(kv_rows, kv_now * HEAD_SIZE, HEAD_SIZE, 1),
            lax.dynamic_slice_in_dim(kv_rows, key_value_width + kv_now * HEAD_SIZE, HEAD_SIZE, 1),
        ],
        axis=1,
    )
    key_rows = jnp.concatenate(
        [
            lax.dynamic_slice_in_dim(key_cache, kv_now * HEAD_SIZE, HEAD_SIZE, 2),
            pair_rows[:, :HEAD_SIZE].reshape(seq_count, BLOCK, HEAD_SIZE),
        ],
        axis=1,
    )
    value_rows = jnp.concatenate(
        [
            lax.dynamic_slice_in_dim(prefix_value_cache, kv_now * HEAD_SIZE, HEAD_SIZE, 2),
            pair_rows[:, HEAD_SIZE:].reshape(seq_count, BLOCK, HEAD_SIZE),
        ],
        axis=1,
    )
    probabilities, probs_low, attended = attend_forward(queries, key_rows, value_rows, usable)
    saved = [(queries, key_rows, value_rows, probabilities, probs_low)]
    joined = attended.reshape(row_count, heads_here * HEAD_SIZE)
    return (joined, saved)


def attention_backward(grad_rows, query_weights, output_weights, own_kv_weights, saved, kv_now):
    heads_here = query_weights.shape[1] // HEAD_SIZE
    row_count = grad_rows.shape[0]
    seq_count = row_count // BLOCK
    key_value_width = KEY_VALUE_HEADS * HEAD_SIZE
    grad_attn = jnp.einsum(
        "td,fd->tf", grad_rows, output_weights, preferred_element_type=jnp.float32
    ).astype(jnp.bfloat16)
    grad_attn = grad_attn.reshape(seq_count, BLOCK, heads_here, HEAD_SIZE)
    query_part, key_rows, value_rows, probabilities, probs_low = saved[0]
    grad_queries, grad_keys, grad_values = attend_backward(
        query_part, key_rows, value_rows, probabilities, probs_low, grad_attn
    )
    placed = jnp.zeros((row_count, 2 * key_value_width), jnp.float32)
    placed = lax.dynamic_update_slice_in_dim(
        placed, grad_keys[:, PREFIX_SLOTS:].reshape(row_count, HEAD_SIZE), kv_now * HEAD_SIZE, 1
    )
    placed = lax.dynamic_update_slice_in_dim(
        placed,
        grad_values[:, PREFIX_SLOTS:].reshape(row_count, HEAD_SIZE),
        key_value_width + kv_now * HEAD_SIZE,
        1,
    )
    own_grads = lax.psum_scatter(placed, "head", scatter_dimension=1, tiled=True)
    running = jnp.einsum(
        "tc,dc->td", own_grads, own_kv_weights.astype(jnp.float32), precision=lax.Precision.HIGHEST
    )
    query_flat = grad_queries.reshape(row_count, heads_here * HEAD_SIZE)
    return running + jnp.einsum(
        "tf,df->td", query_flat, query_weights, preferred_element_type=jnp.float32
    )


def head_rows(row_block):
    return lax.all_gather(row_block, "head", axis=0, tiled=True)


def head_sums(partial_rows):
    return lax.psum_scatter(partial_rows, "head", scatter_dimension=0, tiled=True)


def to_experts(outgoing):
    return lax.all_to_all(outgoing, ("expert", "head"), split_axis=0, concat_axis=0, tiled=True)


def from_experts(results):
    return lax.all_to_all(results, ("expert", "head"), split_axis=0, concat_axis=0, tiled=True)


def body(
    hidden_in,
    out_grad,
    loss_mask,
    expert_ids,
    gate_weights,
    cache_lengths,
    key_cache,
    prefix_value_cache,
    attn_gain,
    moe_gain,
    w_query,
    key_value_weight,
    w_output,
    w_gate,
    w_up,
    w_down,
):
    highest_prec = lax.Precision.HIGHEST
    owned = hidden_in.shape[0]
    width = hidden_in.shape[1]
    normed_one, inverse_one = rms_forward(hidden_in, attn_gain)
    attn_rows = normed_one.astype(jnp.bfloat16)
    heads_here = w_query.shape[1] // HEAD_SIZE
    first_head = lax.axis_index("head") * heads_here
    gathered_rows = head_rows(attn_rows)
    attended, saved = attention_forward(
        gathered_rows, w_query, key_value_weight, key_cache, prefix_value_cache, cache_lengths, first_head
    )
    mixed = head_sums(jnp.dot(attended, w_output, preferred_element_type=jnp.float32))
    hidden = (hidden_in.astype(jnp.float32) + mixed).astype(jnp.bfloat16)
    normed_two, inverse_two = rms_forward(hidden, moe_gain)
    moe_rows = normed_two.astype(jnp.bfloat16)
    device_count = lax.axis_size("expert") * lax.axis_size("head")
    capacity = (owned * TOP * 4 + 3 * device_count - 1) // (3 * device_count)
    slot_total = device_count * capacity
    flat_ids = expert_ids.reshape(-1)
    one_hot = (flat_ids[:, None] == jnp.arange(device_count, dtype=jnp.int32)[None, :]).astype(
        jnp.int32
    )
    earlier = jnp.cumsum(one_hot, axis=0) - one_hot
    position = jnp.sum(earlier * one_hot, axis=1)
    target = flat_ids * capacity + position
    matched = (jnp.arange(slot_total, dtype=jnp.int32)[:, None] == target[None, :]).reshape(
        device_count, capacity, owned, TOP
    )
    placement = jnp.any(matched, axis=3).astype(jnp.bfloat16)
    weighting = jnp.sum(jnp.where(matched, gate_weights[None, None, :, :], 0.0), axis=3)
    cotangent = out_grad.astype(jnp.float32) * loss_mask.astype(jnp.float32)[:, None]
    outgoing = jnp.einsum(
        "dct,tw->dcw", placement, moe_rows, preferred_element_type=jnp.float32
    ).astype(jnp.bfloat16)
    grad_out = jnp.einsum(
        "dct,tw->dcw", weighting, cotangent, precision=highest_prec
    ).astype(jnp.bfloat16)
    rows_in = to_experts(outgoing)
    grads_in = to_experts(grad_out)
    gate_matrix = w_gate[0]
    up_matrix = w_up[0]
    down_matrix = w_down[0]
    gate_pre = jnp.einsum("scw,wf->scf", rows_in, gate_matrix, preferred_element_type=jnp.float32)
    up_pre = jnp.einsum("scw,wf->scf", rows_in, up_matrix, preferred_element_type=jnp.float32)
    sigma = jax.nn.sigmoid(gate_pre)
    activated = (gate_pre * sigma * up_pre).astype(jnp.bfloat16)
    result = jnp.einsum(
        "scf,fw->scw", activated, down_matrix, preferred_element_type=jnp.float32
    ).astype(jnp.bfloat16)
    grad_act = jnp.einsum(
        "scw,fw->scf", grads_in, down_matrix, preferred_element_type=jnp.float32
    )
    grad_gate = (grad_act * up_pre * sigma * (1.0 + gate_pre * (1.0 - sigma))).astype(jnp.bfloat16)
    grad_up = (grad_act * gate_pre * sigma).astype(jnp.bfloat16)
    grad_back = jnp.einsum(
        "scf,wf->scw", grad_gate, gate_matrix, preferred_element_type=jnp.float32
    )
    grad_back = grad_back + jnp.einsum(
        "scf,wf->scw", grad_up, up_matrix, preferred_element_type=jnp.float32
    )
    grad_back = grad_back.astype(jnp.bfloat16)
    result_home = from_experts(result)
    grad_home = from_experts(grad_back)
    grad_moe = jnp.einsum(
        "dct,dcw->tw", placement, grad_home, preferred_element_type=jnp.float32
    )
    grad_hidden = cotangent + rms_backward(hidden, moe_gain, inverse_two, grad_moe)
    grad_low = grad_hidden.astype(jnp.bfloat16)
    grad_gathered = head_rows(grad_low)
    grad_partial = (
        attention_backward(
            grad_gathered,
            w_query,
            w_output,
            key_value_weight,
            saved,
            first_head // (QUERY_HEADS // KEY_VALUE_HEADS),
        )
    )
    grad_partial, result_home = lax.optimization_barrier((grad_partial, result_home))
    grad_attn_rows = head_sums(grad_partial)
    moe_sum = jnp.einsum(
        "dct,dcw->tw",
        weighting,
        result_home.astype(jnp.float32),
        precision=highest_prec,
    )
    layer_out = (hidden.astype(jnp.float32) + moe_sum).astype(jnp.bfloat16)

    input_grad = (
        grad_hidden + rms_backward(hidden_in, attn_gain, inverse_one, grad_attn_rows)
    ).astype(jnp.bfloat16)
    return (layer_out, input_grad)


def solution(mesh):
    in_specs = (
        P(("groups", "expert", "head"), None),
        P(("groups", "expert", "head"), None),
        P(("groups", "expert", "head")),
        P(("groups", "expert", "head"), None),
        P(("groups", "expert", "head"), None),
        P(("groups", "expert")),
        P(("groups", "expert"), None, None),
        P(("groups", "expert"), None, None),
        P(),
        P(),
        P(None, "head"),
        P(None, "head"),
        P("head", None),
        P(("expert", "head"), None, None),
        P(("expert", "head"), None, None),
        P(("expert", "head"), None, None),
    )
    out_specs = (P(("groups", "expert", "head"), None), P(("groups", "expert", "head"), None))
    return jax.shard_map(body, mesh=mesh, in_specs=in_specs, out_specs=out_specs, check_vma=False)
```

```python
import jax
import jax.numpy as jnp
from jax import lax
from jax.sharding import PartitionSpec as P

QUERY_HEADS = 16
KEY_VALUE_HEADS = 2
HEAD_SIZE = 128
TOP = 8
BLOCK = 16
PREFIX_SLOTS = 32


EPS = 1e-06
NEG_FILL = -1e30


def rms_forward(row_block, gain_vec):
    values = row_block.astype(jnp.float32)
    inverse = lax.rsqrt(jnp.mean(values * values, axis=-1, keepdims=True) + EPS)
    return (values * inverse * gain_vec, inverse)


def rms_backward(row_block, gain_vec, inverse, upstream):
    scaled_rows = row_block.astype(jnp.float32) * inverse
    weighted = upstream * gain_vec
    inner_mean = jnp.mean(weighted * scaled_rows, axis=-1, keepdims=True)
    return inverse * (weighted - scaled_rows * inner_mean)


def attend_forward(queries, key_rows, value_rows, usable):
    factor = queries.shape[-1] ** (-0.5)
    scores = (
        jnp.einsum("sbhd,skd->shbk", queries.astype(jnp.float32), key_rows.astype(jnp.float32))
        * factor
    )
    scores = jnp.where(usable[:, None, None, :], scores, NEG_FILL)
    highest = jnp.max(scores, axis=-1, keepdims=True)
    exponent_terms = jnp.exp(scores - highest)
    probabilities = exponent_terms / jnp.sum(exponent_terms, axis=-1, keepdims=True)
    probs_low = probabilities.astype(jnp.bfloat16)
    attended = jnp.einsum(
        "shbk,skd->sbhd", probs_low.astype(jnp.float32), value_rows.astype(jnp.float32)
    )
    return (probabilities, probs_low, attended.astype(jnp.bfloat16))


def attend_backward(queries, key_rows, value_rows, probabilities, probs_low, grad_attended):
    factor = queries.shape[-1] ** (-0.5)
    grad_probs = jnp.einsum(
        "sbhd,skd->shbk", grad_attended.astype(jnp.float32), value_rows.astype(jnp.float32)
    )
    inner_sum = jnp.sum(probabilities * grad_probs, axis=-1, keepdims=True)
    grad_scores = (probabilities * (grad_probs - inner_sum) * factor).astype(jnp.bfloat16)
    grad_queries = jnp.einsum(
        "shbk,skd->sbhd", grad_scores.astype(jnp.float32), key_rows.astype(jnp.float32)
    )
    grad_keys = jnp.einsum(
        "shbk,sbhd->skd", grad_scores.astype(jnp.float32), queries.astype(jnp.float32)
    )
    grad_values = jnp.einsum(
        "shbk,sbhd->skd", probs_low.astype(jnp.float32), grad_attended.astype(jnp.float32)
    )
    return (grad_queries.astype(jnp.bfloat16), grad_keys, grad_values)


def attention_forward(
    row_block,
    query_weights,
    own_kv_weights,
    key_cache,
    prefix_value_cache,
    lengths,
    first_head,
):
    heads_here = query_weights.shape[1] // HEAD_SIZE
    query_group_count = QUERY_HEADS // KEY_VALUE_HEADS
    row_count = row_block.shape[0]
    seq_count = row_count // BLOCK
    key_value_width = KEY_VALUE_HEADS * HEAD_SIZE
    kv_first = first_head // query_group_count
    queries = jnp.dot(row_block, query_weights, preferred_element_type=jnp.float32).astype(
        jnp.bfloat16
    )
    queries = queries.reshape(seq_count, BLOCK, heads_here, HEAD_SIZE)
    usable = jnp.concatenate(
        [
            jnp.arange(PREFIX_SLOTS)[None, :] < lengths[:, None],
            jnp.ones((seq_count, BLOCK), dtype=jnp.bool_),
        ],
        axis=1,
    )
    kv_now = kv_first + 0
    own_rows = jnp.dot(row_block, own_kv_weights, preferred_element_type=jnp.float32).astype(
        jnp.bfloat16
    )
    kv_rows = lax.all_gather(own_rows, "head", axis=1, tiled=True)
    pair_rows = jnp.concatenate(
        [
            lax.dynamic_slice_in_dim(kv_rows, kv_now * HEAD_SIZE, HEAD_SIZE, 1),
            lax.dynamic_slice_in_dim(kv_rows, key_value_width + kv_now * HEAD_SIZE, HEAD_SIZE, 1),
        ],
        axis=1,
    )
    key_rows = jnp.concatenate(
        [
            lax.dynamic_slice_in_dim(key_cache, kv_now * HEAD_SIZE, HEAD_SIZE, 2),
            pair_rows[:, :HEAD_SIZE].reshape(seq_count, BLOCK, HEAD_SIZE),
        ],
        axis=1,
    )
    value_rows = jnp.concatenate(
        [
            lax.dynamic_slice_in_dim(prefix_value_cache, kv_now * HEAD_SIZE, HEAD_SIZE, 2),
            pair_rows[:, HEAD_SIZE:].reshape(seq_count, BLOCK, HEAD_SIZE),
        ],
        axis=1,
    )
    probabilities, probs_low, attended = attend_forward(queries, key_rows, value_rows, usable)
    saved = [(queries, key_rows, value_rows, probabilities, probs_low)]
    joined = attended.reshape(row_count, heads_here * HEAD_SIZE)
    return (joined, saved)


def attention_backward(grad_rows, query_weights, output_weights, own_kv_weights, saved, kv_now):
    heads_here = query_weights.shape[1] // HEAD_SIZE
    row_count = grad_rows.shape[0]
    seq_count = row_count // BLOCK
    key_value_width = KEY_VALUE_HEADS * HEAD_SIZE
    grad_attn = jnp.einsum(
        "td,fd->tf", grad_rows, output_weights, preferred_element_type=jnp.float32
    ).astype(jnp.bfloat16)
    grad_attn = grad_attn.reshape(seq_count, BLOCK, heads_here, HEAD_SIZE)
    query_part, key_rows, value_rows, probabilities, probs_low = saved[0]
    grad_queries, grad_keys, grad_values = attend_backward(
        query_part, key_rows, value_rows, probabilities, probs_low, grad_attn
    )
    placed = jnp.zeros((row_count, 2 * key_value_width), jnp.float32)
    placed = lax.dynamic_update_slice_in_dim(
        placed, grad_keys[:, PREFIX_SLOTS:].reshape(row_count, HEAD_SIZE), kv_now * HEAD_SIZE, 1
    )
    placed = lax.dynamic_update_slice_in_dim(
        placed,
        grad_values[:, PREFIX_SLOTS:].reshape(row_count, HEAD_SIZE),
        key_value_width + kv_now * HEAD_SIZE,
        1,
    )
    own_grads = lax.psum_scatter(placed, "head", scatter_dimension=1, tiled=True)
    running = jnp.einsum(
        "tc,dc->td", own_grads, own_kv_weights.astype(jnp.float32), precision=lax.Precision.HIGHEST
    )
    query_flat = grad_queries.reshape(row_count, heads_here * HEAD_SIZE)
    return running + jnp.einsum(
        "tf,df->td", query_flat, query_weights, preferred_element_type=jnp.float32
    )


def head_rows(row_block):
    return lax.all_gather(row_block, "head", axis=0, tiled=True)


def head_sums(partial_rows):
    return lax.psum_scatter(partial_rows, "head", scatter_dimension=0, tiled=True)


def to_experts(outgoing):
    return lax.all_to_all(outgoing, ("expert", "head"), split_axis=0, concat_axis=0, tiled=True)


def from_experts(results):
    return lax.all_to_all(results, ("expert", "head"), split_axis=0, concat_axis=0, tiled=True)


def body(
    hidden_in,
    out_grad,
    loss_mask,
    expert_ids,
    gate_weights,
    cache_lengths,
    key_cache,
    prefix_value_cache,
    attn_gain,
    moe_gain,
    w_query,
    key_value_weight,
    w_output,
    w_gate,
    w_up,
    w_down,
):
    highest_prec = lax.Precision.HIGHEST
    owned = hidden_in.shape[0]
    width = hidden_in.shape[1]
    normed_one, inverse_one = rms_forward(hidden_in, attn_gain)
    attn_rows = normed_one.astype(jnp.bfloat16)
    heads_here = w_query.shape[1] // HEAD_SIZE
    first_head = lax.axis_index("head") * heads_here
    gathered_rows = head_rows(attn_rows)
    attended, saved = attention_forward(
        gathered_rows, w_query, key_value_weight, key_cache, prefix_value_cache, cache_lengths, first_head
    )
    mixed = head_sums(jnp.dot(attended, w_output, preferred_element_type=jnp.float32))
    hidden = (hidden_in.astype(jnp.float32) + mixed).astype(jnp.bfloat16)
    normed_two, inverse_two = rms_forward(hidden, moe_gain)
    moe_rows = normed_two.astype(jnp.bfloat16)
    device_count = lax.axis_size("expert") * lax.axis_size("head")
    capacity = (owned * TOP * 4 + 3 * device_count - 1) // (3 * device_count)
    slot_total = device_count * capacity
    flat_ids = expert_ids.reshape(-1)
    one_hot = (flat_ids[:, None] == jnp.arange(device_count, dtype=jnp.int32)[None, :]).astype(
        jnp.int32
    )
    earlier = jnp.cumsum(one_hot, axis=0) - one_hot
    position = jnp.sum(earlier * one_hot, axis=1)
    target = flat_ids * capacity + position
    matched = (jnp.arange(slot_total, dtype=jnp.int32)[:, None] == target[None, :]).reshape(
        device_count, capacity, owned, TOP
    )
    placement = jnp.any(matched, axis=3).astype(jnp.bfloat16)
    weighting = jnp.sum(jnp.where(matched, gate_weights[None, None, :, :], 0.0), axis=3)
    cotangent = out_grad.astype(jnp.float32) * loss_mask.astype(jnp.float32)[:, None]
    lanes = 128
    pieces = width // lanes
    outgoing = jnp.einsum(
        "dct,tkl->dckl",
        placement,
        moe_rows.reshape(owned, pieces, lanes),
        preferred_element_type=jnp.float32,
    ).astype(jnp.bfloat16)
    grad_out = jnp.einsum(
        "dct,tkl->dckl",
        weighting,
        cotangent.reshape(owned, pieces, lanes),
        precision=highest_prec,
    ).astype(jnp.bfloat16)
    flat_shape = (device_count, capacity * pieces, lanes)
    split_shape = (device_count, capacity, pieces, lanes)
    rows_in = to_experts(outgoing.reshape(flat_shape)).reshape(split_shape)
    grads_in = to_experts(grad_out.reshape(flat_shape)).reshape(split_shape)
    gate_matrix = w_gate[0].reshape(pieces, lanes, -1)
    up_matrix = w_up[0].reshape(pieces, lanes, -1)
    down_matrix = w_down[0].reshape(-1, pieces, lanes)
    gate_pre = jnp.einsum(
        "sckl,klf->scf", rows_in, gate_matrix, preferred_element_type=jnp.float32
    )
    up_pre = jnp.einsum("sckl,klf->scf", rows_in, up_matrix, preferred_element_type=jnp.float32)
    sigma = jax.nn.sigmoid(gate_pre)
    activated = (gate_pre * sigma * up_pre).astype(jnp.bfloat16)
    result = jnp.einsum(
        "scf,fkl->sckl", activated, down_matrix, preferred_element_type=jnp.float32
    ).astype(jnp.bfloat16)
    grad_act = jnp.einsum(
        "sckl,fkl->scf", grads_in, down_matrix, preferred_element_type=jnp.float32
    )
    grad_gate = (grad_act * up_pre * sigma * (1.0 + gate_pre * (1.0 - sigma))).astype(jnp.bfloat16)
    grad_up = (grad_act * gate_pre * sigma).astype(jnp.bfloat16)
    grad_back = jnp.einsum(
        "scf,klf->sckl", grad_gate, gate_matrix, preferred_element_type=jnp.float32
    )
    grad_back = grad_back + jnp.einsum(
        "scf,klf->sckl", grad_up, up_matrix, preferred_element_type=jnp.float32
    )
    grad_back = grad_back.astype(jnp.bfloat16)
    result_home = from_experts(result.reshape(flat_shape)).reshape(split_shape)
    grad_home = from_experts(grad_back.reshape(flat_shape)).reshape(split_shape)
    moe_sum = jnp.einsum(
        "dct,dckl->tkl",
        weighting,
        result_home.astype(jnp.float32),
        precision=highest_prec,
    ).reshape(owned, width)
    layer_out = (hidden.astype(jnp.float32) + moe_sum).astype(jnp.bfloat16)
    grad_moe = jnp.einsum(
        "dct,dckl->tkl", placement, grad_home, preferred_element_type=jnp.float32
    ).reshape(owned, width)
    grad_hidden = cotangent + rms_backward(hidden, moe_gain, inverse_two, grad_moe)
    grad_low = grad_hidden.astype(jnp.bfloat16)
    grad_gathered = head_rows(grad_low)
    grad_attn_rows = head_sums(
        attention_backward(
            grad_gathered,
            w_query,
            w_output,
            key_value_weight,
            saved,
            first_head // (QUERY_HEADS // KEY_VALUE_HEADS),
        )
    )
    input_grad = (
        grad_hidden + rms_backward(hidden_in, attn_gain, inverse_one, grad_attn_rows)
    ).astype(jnp.bfloat16)
    return (layer_out, input_grad)


def solution(mesh):
    in_specs = (
        P(("groups", "expert", "head"), None),
        P(("groups", "expert", "head"), None),
        P(("groups", "expert", "head")),
        P(("groups", "expert", "head"), None),
        P(("groups", "expert", "head"), None),
        P(("groups", "expert")),
        P(("groups", "expert"), None, None),
        P(("groups", "expert"), None, None),
        P(),
        P(),
        P(None, "head"),
        P(None, "head"),
        P("head", None),
        P(("expert", "head"), None, None),
        P(("expert", "head"), None, None),
        P(("expert", "head"), None, None),
    )
    out_specs = (P(("groups", "expert", "head"), None), P(("groups", "expert", "head"), None))
    return jax.shard_map(body, mesh=mesh, in_specs=in_specs, out_specs=out_specs, check_vma=False)
```

```python
import jax
import jax.numpy as jnp
from jax import lax
from jax.sharding import PartitionSpec as P

QUERY_HEADS = 16
KEY_VALUE_HEADS = 2
HEAD_SIZE = 128
TOP = 8
BLOCK = 16
PREFIX_SLOTS = 32


EPS = 1e-06
NEG_FILL = -1e30


def rms_forward(row_block, gain_vec):
    values = row_block.astype(jnp.float32)
    inverse = lax.rsqrt(jnp.mean(values * values, axis=-1, keepdims=True) + EPS)
    return (values * inverse * gain_vec, inverse)


def rms_backward(row_block, gain_vec, inverse, upstream):
    scaled_rows = row_block.astype(jnp.float32) * inverse
    weighted = upstream * gain_vec
    inner_mean = jnp.mean(weighted * scaled_rows, axis=-1, keepdims=True)
    return inverse * (weighted - scaled_rows * inner_mean)


def attend_forward(queries, key_rows, value_rows, usable):
    factor = queries.shape[-1] ** (-0.5)
    scores = (
        jnp.einsum("sbhd,skd->shbk", queries.astype(jnp.float32), key_rows.astype(jnp.float32))
        * factor
    )
    scores = jnp.where(usable[:, None, None, :], scores, NEG_FILL)
    highest = jnp.max(scores, axis=-1, keepdims=True)
    exponent_terms = jnp.exp(scores - highest)
    probabilities = exponent_terms / jnp.sum(exponent_terms, axis=-1, keepdims=True)
    probs_low = probabilities.astype(jnp.bfloat16)
    attended = jnp.einsum(
        "shbk,skd->sbhd", probs_low.astype(jnp.float32), value_rows.astype(jnp.float32)
    )
    return (probabilities, probs_low, attended.astype(jnp.bfloat16))


def attend_backward(queries, key_rows, value_rows, probabilities, probs_low, grad_attended):
    factor = queries.shape[-1] ** (-0.5)
    grad_probs = jnp.einsum(
        "sbhd,skd->shbk", grad_attended.astype(jnp.float32), value_rows.astype(jnp.float32)
    )
    inner_sum = jnp.sum(probabilities * grad_probs, axis=-1, keepdims=True)
    grad_scores = (probabilities * (grad_probs - inner_sum) * factor).astype(jnp.bfloat16)
    grad_queries = jnp.einsum(
        "shbk,skd->sbhd", grad_scores.astype(jnp.float32), key_rows.astype(jnp.float32)
    )
    grad_keys = jnp.einsum(
        "shbk,sbhd->skd", grad_scores.astype(jnp.float32), queries.astype(jnp.float32)
    )
    grad_values = jnp.einsum(
        "shbk,sbhd->skd", probs_low.astype(jnp.float32), grad_attended.astype(jnp.float32)
    )
    return (grad_queries.astype(jnp.bfloat16), grad_keys, grad_values)


def attention_forward(
    row_block,
    query_weights,
    own_kv_weights,
    key_cache,
    prefix_value_cache,
    lengths,
    first_head,
):
    heads_here = query_weights.shape[1] // HEAD_SIZE
    query_group_count = QUERY_HEADS // KEY_VALUE_HEADS
    row_count = row_block.shape[0]
    seq_count = row_count // BLOCK
    key_value_width = KEY_VALUE_HEADS * HEAD_SIZE
    kv_first = first_head // query_group_count
    queries = jnp.dot(row_block, query_weights, preferred_element_type=jnp.float32).astype(
        jnp.bfloat16
    )
    queries = queries.reshape(seq_count, BLOCK, heads_here, HEAD_SIZE)
    usable = jnp.concatenate(
        [
            jnp.arange(PREFIX_SLOTS)[None, :] < lengths[:, None],
            jnp.ones((seq_count, BLOCK), dtype=jnp.bool_),
        ],
        axis=1,
    )
    kv_now = kv_first + 0
    own_rows = jnp.dot(row_block, own_kv_weights, preferred_element_type=jnp.float32).astype(
        jnp.bfloat16
    )
    kv_rows = head_gather(own_rows, 1)
    pair_rows = jnp.concatenate(
        [
            lax.dynamic_slice_in_dim(kv_rows, kv_now * HEAD_SIZE, HEAD_SIZE, 1),
            lax.dynamic_slice_in_dim(kv_rows, key_value_width + kv_now * HEAD_SIZE, HEAD_SIZE, 1),
        ],
        axis=1,
    )
    key_rows = jnp.concatenate(
        [
            lax.dynamic_slice_in_dim(key_cache, kv_now * HEAD_SIZE, HEAD_SIZE, 2),
            pair_rows[:, :HEAD_SIZE].reshape(seq_count, BLOCK, HEAD_SIZE),
        ],
        axis=1,
    )
    value_rows = jnp.concatenate(
        [
            lax.dynamic_slice_in_dim(prefix_value_cache, kv_now * HEAD_SIZE, HEAD_SIZE, 2),
            pair_rows[:, HEAD_SIZE:].reshape(seq_count, BLOCK, HEAD_SIZE),
        ],
        axis=1,
    )
    probabilities, probs_low, attended = attend_forward(queries, key_rows, value_rows, usable)
    saved = [(queries, key_rows, value_rows, probabilities, probs_low)]
    joined = attended.reshape(row_count, heads_here * HEAD_SIZE)
    return (joined, saved)


def attention_backward(grad_rows, query_weights, output_weights, own_kv_weights, saved, kv_now):
    heads_here = query_weights.shape[1] // HEAD_SIZE
    row_count = grad_rows.shape[0]
    seq_count = row_count // BLOCK
    key_value_width = KEY_VALUE_HEADS * HEAD_SIZE
    grad_attn = jnp.einsum(
        "td,fd->tf", grad_rows, output_weights, preferred_element_type=jnp.float32
    ).astype(jnp.bfloat16)
    grad_attn = grad_attn.reshape(seq_count, BLOCK, heads_here, HEAD_SIZE)
    query_part, key_rows, value_rows, probabilities, probs_low = saved[0]
    grad_queries, grad_keys, grad_values = attend_backward(
        query_part, key_rows, value_rows, probabilities, probs_low, grad_attn
    )
    placed = jnp.zeros((row_count, 2 * key_value_width), jnp.float32)
    placed = lax.dynamic_update_slice_in_dim(
        placed, grad_keys[:, PREFIX_SLOTS:].reshape(row_count, HEAD_SIZE), kv_now * HEAD_SIZE, 1
    )
    placed = lax.dynamic_update_slice_in_dim(
        placed,
        grad_values[:, PREFIX_SLOTS:].reshape(row_count, HEAD_SIZE),
        key_value_width + kv_now * HEAD_SIZE,
        1,
    )
    own_grads = lax.psum_scatter(placed, "head", scatter_dimension=1, tiled=True)
    running = jnp.einsum(
        "tc,dc->td", own_grads, own_kv_weights.astype(jnp.float32), precision=lax.Precision.HIGHEST
    )
    query_flat = grad_queries.reshape(row_count, heads_here * HEAD_SIZE)
    return running + jnp.einsum(
        "tf,df->td", query_flat, query_weights, preferred_element_type=jnp.float32
    )


def head_gather(block, axis):
    count = lax.axis_size("head")
    me = lax.axis_index("head")
    parts = [block] + [
        lax.ppermute(block, "head", perm=[(j, (j + shift) % count) for j in range(count)])
        for shift in range(1, count)
    ]
    ordered = jnp.take(jnp.stack(parts), (me - jnp.arange(count)) % count, axis=0)
    ordered = jnp.moveaxis(ordered, 0, axis)
    merged = list(block.shape)
    merged[axis] = count * block.shape[axis]
    return ordered.reshape(merged)


def head_rows(row_block):
    return head_gather(row_block, 0)


def head_sums(partial_rows):
    return lax.psum_scatter(partial_rows, "head", scatter_dimension=0, tiled=True)


def to_experts(outgoing):
    return lax.all_to_all(outgoing, ("expert", "head"), split_axis=0, concat_axis=0, tiled=True)


def from_experts(results):
    return lax.all_to_all(results, ("expert", "head"), split_axis=0, concat_axis=0, tiled=True)


def body(
    hidden_in,
    out_grad,
    loss_mask,
    expert_ids,
    gate_weights,
    cache_lengths,
    key_cache,
    prefix_value_cache,
    attn_gain,
    moe_gain,
    w_query,
    key_value_weight,
    w_output,
    w_gate,
    w_up,
    w_down,
):
    highest_prec = lax.Precision.HIGHEST
    owned = hidden_in.shape[0]
    width = hidden_in.shape[1]
    normed_one, inverse_one = rms_forward(hidden_in, attn_gain)
    attn_rows = normed_one.astype(jnp.bfloat16)
    heads_here = w_query.shape[1] // HEAD_SIZE
    first_head = lax.axis_index("head") * heads_here
    gathered_rows = head_rows(attn_rows)
    attended, saved = attention_forward(
        gathered_rows, w_query, key_value_weight, key_cache, prefix_value_cache, cache_lengths, first_head
    )
    mixed = head_sums(jnp.dot(attended, w_output, preferred_element_type=jnp.float32))
    hidden = (hidden_in.astype(jnp.float32) + mixed).astype(jnp.bfloat16)
    normed_two, inverse_two = rms_forward(hidden, moe_gain)
    moe_rows = normed_two.astype(jnp.bfloat16)
    device_count = lax.axis_size("expert") * lax.axis_size("head")
    capacity = (owned * TOP * 4 + 3 * device_count - 1) // (3 * device_count)
    slot_total = device_count * capacity
    flat_ids = expert_ids.reshape(-1)
    one_hot = (flat_ids[:, None] == jnp.arange(device_count, dtype=jnp.int32)[None, :]).astype(
        jnp.int32
    )
    earlier = jnp.cumsum(one_hot, axis=0) - one_hot
    position = jnp.sum(earlier * one_hot, axis=1)
    target = flat_ids * capacity + position
    matched = (jnp.arange(slot_total, dtype=jnp.int32)[:, None] == target[None, :]).reshape(
        device_count, capacity, owned, TOP
    )
    placement = jnp.any(matched, axis=3).astype(jnp.bfloat16)
    weighting = jnp.sum(jnp.where(matched, gate_weights[None, None, :, :], 0.0), axis=3)
    cotangent = out_grad.astype(jnp.float32) * loss_mask.astype(jnp.float32)[:, None]
    lanes = 128
    pieces = width // lanes
    outgoing = jnp.einsum(
        "dct,tkl->dckl",
        placement,
        moe_rows.reshape(owned, pieces, lanes),
        preferred_element_type=jnp.float32,
    ).astype(jnp.bfloat16)
    grad_out = jnp.einsum(
        "dct,tkl->dckl",
        weighting,
        cotangent.reshape(owned, pieces, lanes),
        precision=highest_prec,
    ).astype(jnp.bfloat16)
    flat_shape = (device_count, capacity * pieces, lanes)
    split_shape = (device_count, capacity, pieces, lanes)
    rows_in = to_experts(outgoing.reshape(flat_shape)).reshape(split_shape)
    grads_in = to_experts(grad_out.reshape(flat_shape)).reshape(split_shape)
    gate_matrix = w_gate[0].reshape(pieces, lanes, -1)
    up_matrix = w_up[0].reshape(pieces, lanes, -1)
    down_matrix = w_down[0].reshape(-1, pieces, lanes)
    gate_pre = jnp.einsum(
        "sckl,klf->scf", rows_in, gate_matrix, preferred_element_type=jnp.float32
    )
    up_pre = jnp.einsum("sckl,klf->scf", rows_in, up_matrix, preferred_element_type=jnp.float32)
    sigma = jax.nn.sigmoid(gate_pre)
    activated = (gate_pre * sigma * up_pre).astype(jnp.bfloat16)
    result = jnp.einsum(
        "scf,fkl->sckl", activated, down_matrix, preferred_element_type=jnp.float32
    ).astype(jnp.bfloat16)
    grad_act = jnp.einsum(
        "sckl,fkl->scf", grads_in, down_matrix, preferred_element_type=jnp.float32
    )
    grad_gate = (grad_act * up_pre * sigma * (1.0 + gate_pre * (1.0 - sigma))).astype(jnp.bfloat16)
    grad_up = (grad_act * gate_pre * sigma).astype(jnp.bfloat16)
    grad_back = jnp.einsum(
        "scf,klf->sckl", grad_gate, gate_matrix, preferred_element_type=jnp.float32
    )
    grad_back = grad_back + jnp.einsum(
        "scf,klf->sckl", grad_up, up_matrix, preferred_element_type=jnp.float32
    )
    grad_back = grad_back.astype(jnp.bfloat16)
    result_home = from_experts(result.reshape(flat_shape)).reshape(split_shape)
    grad_home = from_experts(grad_back.reshape(flat_shape)).reshape(split_shape)
    moe_sum = jnp.einsum(
        "dct,dckl->tkl",
        weighting,
        result_home.astype(jnp.float32),
        precision=highest_prec,
    ).reshape(owned, width)
    layer_out = (hidden.astype(jnp.float32) + moe_sum).astype(jnp.bfloat16)
    grad_moe = jnp.einsum(
        "dct,dckl->tkl", placement, grad_home, preferred_element_type=jnp.float32
    ).reshape(owned, width)
    grad_hidden = cotangent + rms_backward(hidden, moe_gain, inverse_two, grad_moe)
    grad_low = grad_hidden.astype(jnp.bfloat16)
    grad_gathered = head_rows(grad_low)
    grad_attn_rows = head_sums(
        attention_backward(
            grad_gathered,
            w_query,
            w_output,
            key_value_weight,
            saved,
            first_head // (QUERY_HEADS // KEY_VALUE_HEADS),
        )
    )
    input_grad = (
        grad_hidden + rms_backward(hidden_in, attn_gain, inverse_one, grad_attn_rows)
    ).astype(jnp.bfloat16)
    return (layer_out, input_grad)


def solution(mesh):
    in_specs = (
        P(("groups", "expert", "head"), None),
        P(("groups", "expert", "head"), None),
        P(("groups", "expert", "head")),
        P(("groups", "expert", "head"), None),
        P(("groups", "expert", "head"), None),
        P(("groups", "expert")),
        P(("groups", "expert"), None, None),
        P(("groups", "expert"), None, None),
        P(),
        P(),
        P(None, "head"),
        P(None, "head"),
        P("head", None),
        P(("expert", "head"), None, None),
        P(("expert", "head"), None, None),
        P(("expert", "head"), None, None),
    )
    out_specs = (P(("groups", "expert", "head"), None), P(("groups", "expert", "head"), None))
    return jax.shard_map(body, mesh=mesh, in_specs=in_specs, out_specs=out_specs, check_vma=False)
```

```python
import jax
import jax.numpy as jnp
from jax import lax
from jax.sharding import PartitionSpec as P

QUERY_HEADS = 16
KEY_VALUE_HEADS = 2
HEAD_SIZE = 128
TOP = 8
BLOCK = 16
PREFIX_SLOTS = 32


EPS = 1e-06
NEG_FILL = -1e30


def rms_forward(row_block, gain_vec):
    values = row_block.astype(jnp.float32)
    inverse = lax.rsqrt(jnp.mean(values * values, axis=-1, keepdims=True) + EPS)
    return (values * inverse * gain_vec, inverse)


def rms_backward(row_block, gain_vec, inverse, upstream):
    scaled_rows = row_block.astype(jnp.float32) * inverse
    weighted = upstream * gain_vec
    inner_mean = jnp.mean(weighted * scaled_rows, axis=-1, keepdims=True)
    return inverse * (weighted - scaled_rows * inner_mean)


def attend_forward(queries, key_rows, value_rows, usable):
    factor = queries.shape[-1] ** (-0.5)
    scores = (
        jnp.einsum("sbhd,skd->shbk", queries.astype(jnp.float32), key_rows.astype(jnp.float32))
        * factor
    )
    scores = jnp.where(usable[:, None, None, :], scores, NEG_FILL)
    highest = jnp.max(scores, axis=-1, keepdims=True)
    exponent_terms = jnp.exp(scores - highest)
    probabilities = exponent_terms / jnp.sum(exponent_terms, axis=-1, keepdims=True)
    probs_low = probabilities.astype(jnp.bfloat16)
    attended = jnp.einsum(
        "shbk,skd->sbhd", probs_low.astype(jnp.float32), value_rows.astype(jnp.float32)
    )
    return (probabilities, probs_low, attended.astype(jnp.bfloat16))


def attend_backward(queries, key_rows, value_rows, probabilities, probs_low, grad_attended):
    factor = queries.shape[-1] ** (-0.5)
    grad_probs = jnp.einsum(
        "sbhd,skd->shbk", grad_attended.astype(jnp.float32), value_rows.astype(jnp.float32)
    )
    inner_sum = jnp.sum(probabilities * grad_probs, axis=-1, keepdims=True)
    grad_scores = (probabilities * (grad_probs - inner_sum) * factor).astype(jnp.bfloat16)
    grad_queries = jnp.einsum(
        "shbk,skd->sbhd", grad_scores.astype(jnp.float32), key_rows.astype(jnp.float32)
    )
    grad_keys = jnp.einsum(
        "shbk,sbhd->skd", grad_scores.astype(jnp.float32), queries.astype(jnp.float32)
    )
    grad_values = jnp.einsum(
        "shbk,sbhd->skd", probs_low.astype(jnp.float32), grad_attended.astype(jnp.float32)
    )
    return (grad_queries.astype(jnp.bfloat16), grad_keys, grad_values)


def attention_forward(
    row_block,
    query_weights,
    own_kv_weights,
    key_cache,
    prefix_value_cache,
    lengths,
    first_head,
):
    heads_here = query_weights.shape[1] // HEAD_SIZE
    query_group_count = QUERY_HEADS // KEY_VALUE_HEADS
    row_count = row_block.shape[0]
    seq_count = row_count // BLOCK
    key_value_width = KEY_VALUE_HEADS * HEAD_SIZE
    kv_first = first_head // query_group_count
    queries = jnp.dot(row_block, query_weights, preferred_element_type=jnp.float32).astype(
        jnp.bfloat16
    )
    queries = queries.reshape(seq_count, BLOCK, heads_here, HEAD_SIZE)
    usable = jnp.concatenate(
        [
            jnp.arange(PREFIX_SLOTS)[None, :] < lengths[:, None],
            jnp.ones((seq_count, BLOCK), dtype=jnp.bool_),
        ],
        axis=1,
    )
    kv_now = kv_first + 0
    own_rows = jnp.dot(row_block, own_kv_weights, preferred_element_type=jnp.float32).astype(
        jnp.bfloat16
    )
    kv_rows = head_gather(own_rows, 1)
    pair_rows = jnp.concatenate(
        [
            lax.dynamic_slice_in_dim(kv_rows, kv_now * HEAD_SIZE, HEAD_SIZE, 1),
            lax.dynamic_slice_in_dim(kv_rows, key_value_width + kv_now * HEAD_SIZE, HEAD_SIZE, 1),
        ],
        axis=1,
    )
    key_rows = jnp.concatenate(
        [
            lax.dynamic_slice_in_dim(key_cache, kv_now * HEAD_SIZE, HEAD_SIZE, 2),
            pair_rows[:, :HEAD_SIZE].reshape(seq_count, BLOCK, HEAD_SIZE),
        ],
        axis=1,
    )
    value_rows = jnp.concatenate(
        [
            lax.dynamic_slice_in_dim(prefix_value_cache, kv_now * HEAD_SIZE, HEAD_SIZE, 2),
            pair_rows[:, HEAD_SIZE:].reshape(seq_count, BLOCK, HEAD_SIZE),
        ],
        axis=1,
    )
    probabilities, probs_low, attended = attend_forward(queries, key_rows, value_rows, usable)
    saved = [(queries, key_rows, value_rows, probabilities, probs_low)]
    joined = attended.reshape(row_count, heads_here * HEAD_SIZE)
    return (joined, saved)


def attention_backward(grad_rows, query_weights, output_weights, own_kv_weights, saved, kv_now):
    heads_here = query_weights.shape[1] // HEAD_SIZE
    row_count = grad_rows.shape[0]
    seq_count = row_count // BLOCK
    key_value_width = KEY_VALUE_HEADS * HEAD_SIZE
    grad_attn = jnp.einsum(
        "td,fd->tf", grad_rows, output_weights, preferred_element_type=jnp.float32
    ).astype(jnp.bfloat16)
    grad_attn = grad_attn.reshape(seq_count, BLOCK, heads_here, HEAD_SIZE)
    query_part, key_rows, value_rows, probabilities, probs_low = saved[0]
    grad_queries, grad_keys, grad_values = attend_backward(
        query_part, key_rows, value_rows, probabilities, probs_low, grad_attn
    )
    placed = jnp.zeros((row_count, 2 * key_value_width), jnp.float32)
    placed = lax.dynamic_update_slice_in_dim(
        placed, grad_keys[:, PREFIX_SLOTS:].reshape(row_count, HEAD_SIZE), kv_now * HEAD_SIZE, 1
    )
    placed = lax.dynamic_update_slice_in_dim(
        placed,
        grad_values[:, PREFIX_SLOTS:].reshape(row_count, HEAD_SIZE),
        key_value_width + kv_now * HEAD_SIZE,
        1,
    )
    own_grads = lax.psum_scatter(placed, "head", scatter_dimension=1, tiled=True)
    running = jnp.einsum(
        "tc,dc->td", own_grads, own_kv_weights.astype(jnp.float32), precision=lax.Precision.HIGHEST
    )
    query_flat = grad_queries.reshape(row_count, heads_here * HEAD_SIZE)
    return running + jnp.einsum(
        "tf,df->td", query_flat, query_weights, preferred_element_type=jnp.float32
    )


def head_gather(block, axis):
    count = lax.axis_size("head")
    me = lax.axis_index("head")
    parts = [block] + [
        lax.ppermute(block, "head", perm=[(j, (j + shift) % count) for j in range(count)])
        for shift in range(1, count)
    ]
    ordered = jnp.take(jnp.stack(parts), (me - jnp.arange(count)) % count, axis=0)
    ordered = jnp.moveaxis(ordered, 0, axis)
    merged = list(block.shape)
    merged[axis] = count * block.shape[axis]
    return ordered.reshape(merged)


def head_rows(row_block):
    return head_gather(row_block, 0)


def head_sums(partial_rows):
    count = lax.axis_size("head")
    me = lax.axis_index("head")
    chunks = partial_rows.reshape((count, -1) + partial_rows.shape[1:])
    total = chunks[me]
    for shift in range(1, count):
        total = total + lax.ppermute(
            chunks[(me + shift) % count],
            "head",
            perm=[(j, (j + shift) % count) for j in range(count)],
        )
    return total


def to_experts(outgoing):
    return lax.all_to_all(outgoing, ("expert", "head"), split_axis=0, concat_axis=0, tiled=True)


def from_experts(results):
    return lax.all_to_all(results, ("expert", "head"), split_axis=0, concat_axis=0, tiled=True)


def body(
    hidden_in,
    out_grad,
    loss_mask,
    expert_ids,
    gate_weights,
    cache_lengths,
    key_cache,
    prefix_value_cache,
    attn_gain,
    moe_gain,
    w_query,
    key_value_weight,
    w_output,
    w_gate,
    w_up,
    w_down,
):
    highest_prec = lax.Precision.HIGHEST
    owned = hidden_in.shape[0]
    width = hidden_in.shape[1]
    normed_one, inverse_one = rms_forward(hidden_in, attn_gain)
    attn_rows = normed_one.astype(jnp.bfloat16)
    heads_here = w_query.shape[1] // HEAD_SIZE
    first_head = lax.axis_index("head") * heads_here
    gathered_rows = head_rows(attn_rows)
    attended, saved = attention_forward(
        gathered_rows, w_query, key_value_weight, key_cache, prefix_value_cache, cache_lengths, first_head
    )
    mixed = head_sums(jnp.dot(attended, w_output, preferred_element_type=jnp.float32))
    hidden = (hidden_in.astype(jnp.float32) + mixed).astype(jnp.bfloat16)
    normed_two, inverse_two = rms_forward(hidden, moe_gain)
    moe_rows = normed_two.astype(jnp.bfloat16)
    device_count = lax.axis_size("expert") * lax.axis_size("head")
    capacity = (owned * TOP * 4 + 3 * device_count - 1) // (3 * device_count)
    slot_total = device_count * capacity
    flat_ids = expert_ids.reshape(-1)
    one_hot = (flat_ids[:, None] == jnp.arange(device_count, dtype=jnp.int32)[None, :]).astype(
        jnp.int32
    )
    earlier = jnp.cumsum(one_hot, axis=0) - one_hot
    position = jnp.sum(earlier * one_hot, axis=1)
    target = flat_ids * capacity + position
    matched = (jnp.arange(slot_total, dtype=jnp.int32)[:, None] == target[None, :]).reshape(
        device_count, capacity, owned, TOP
    )
    placement = jnp.any(matched, axis=3).astype(jnp.bfloat16)
    weighting = jnp.sum(jnp.where(matched, gate_weights[None, None, :, :], 0.0), axis=3)
    cotangent = out_grad.astype(jnp.float32) * loss_mask.astype(jnp.float32)[:, None]
    lanes = 128
    pieces = width // lanes
    outgoing = jnp.einsum(
        "dct,tkl->dckl",
        placement,
        moe_rows.reshape(owned, pieces, lanes),
        preferred_element_type=jnp.float32,
    ).astype(jnp.bfloat16)
    grad_out = jnp.einsum(
        "dct,tkl->dckl",
        weighting,
        cotangent.reshape(owned, pieces, lanes),
        precision=highest_prec,
    ).astype(jnp.bfloat16)
    flat_shape = (device_count, capacity * pieces, lanes)
    split_shape = (device_count, capacity, pieces, lanes)
    rows_in = to_experts(outgoing.reshape(flat_shape)).reshape(split_shape)
    grads_in = to_experts(grad_out.reshape(flat_shape)).reshape(split_shape)
    gate_matrix = w_gate[0].reshape(pieces, lanes, -1)
    up_matrix = w_up[0].reshape(pieces, lanes, -1)
    down_matrix = w_down[0].reshape(-1, pieces, lanes)
    gate_pre = jnp.einsum(
        "sckl,klf->scf", rows_in, gate_matrix, preferred_element_type=jnp.float32
    )
    up_pre = jnp.einsum("sckl,klf->scf", rows_in, up_matrix, preferred_element_type=jnp.float32)
    sigma = jax.nn.sigmoid(gate_pre)
    activated = (gate_pre * sigma * up_pre).astype(jnp.bfloat16)
    result = jnp.einsum(
        "scf,fkl->sckl", activated, down_matrix, preferred_element_type=jnp.float32
    ).astype(jnp.bfloat16)
    grad_act = jnp.einsum(
        "sckl,fkl->scf", grads_in, down_matrix, preferred_element_type=jnp.float32
    )
    grad_gate = (grad_act * up_pre * sigma * (1.0 + gate_pre * (1.0 - sigma))).astype(jnp.bfloat16)
    grad_up = (grad_act * gate_pre * sigma).astype(jnp.bfloat16)
    grad_back = jnp.einsum(
        "scf,klf->sckl", grad_gate, gate_matrix, preferred_element_type=jnp.float32
    )
    grad_back = grad_back + jnp.einsum(
        "scf,klf->sckl", grad_up, up_matrix, preferred_element_type=jnp.float32
    )
    grad_back = grad_back.astype(jnp.bfloat16)
    result_home = from_experts(result.reshape(flat_shape)).reshape(split_shape)
    grad_home = from_experts(grad_back.reshape(flat_shape)).reshape(split_shape)
    moe_sum = jnp.einsum(
        "dct,dckl->tkl",
        weighting,
        result_home.astype(jnp.float32),
        precision=highest_prec,
    ).reshape(owned, width)
    layer_out = (hidden.astype(jnp.float32) + moe_sum).astype(jnp.bfloat16)
    grad_moe = jnp.einsum(
        "dct,dckl->tkl", placement, grad_home, preferred_element_type=jnp.float32
    ).reshape(owned, width)
    grad_hidden = cotangent + rms_backward(hidden, moe_gain, inverse_two, grad_moe)
    grad_low = grad_hidden.astype(jnp.bfloat16)
    grad_gathered = head_rows(grad_low)
    grad_attn_rows = head_sums(
        attention_backward(
            grad_gathered,
            w_query,
            w_output,
            key_value_weight,
            saved,
            first_head // (QUERY_HEADS // KEY_VALUE_HEADS),
        )
    )
    input_grad = (
        grad_hidden + rms_backward(hidden_in, attn_gain, inverse_one, grad_attn_rows)
    ).astype(jnp.bfloat16)
    return (layer_out, input_grad)


def solution(mesh):
    in_specs = (
        P(("groups", "expert", "head"), None),
        P(("groups", "expert", "head"), None),
        P(("groups", "expert", "head")),
        P(("groups", "expert", "head"), None),
        P(("groups", "expert", "head"), None),
        P(("groups", "expert")),
        P(("groups", "expert"), None, None),
        P(("groups", "expert"), None, None),
        P(),
        P(),
        P(None, "head"),
        P(None, "head"),
        P("head", None),
        P(("expert", "head"), None, None),
        P(("expert", "head"), None, None),
        P(("expert", "head"), None, None),
    )
    out_specs = (P(("groups", "expert", "head"), None), P(("groups", "expert", "head"), None))
    return jax.shard_map(body, mesh=mesh, in_specs=in_specs, out_specs=out_specs, check_vma=False)
```

```python
import jax
import jax.numpy as jnp
from jax import lax
from jax.sharding import PartitionSpec as P

QUERY_HEADS = 16
KEY_VALUE_HEADS = 2
HEAD_SIZE = 128
TOP = 8
BLOCK = 16
PREFIX_SLOTS = 32


EPS = 1e-06
NEG_FILL = -1e30


def rms_forward(row_block, gain_vec):
    values = row_block.astype(jnp.float32)
    inverse = lax.rsqrt(jnp.mean(values * values, axis=-1, keepdims=True) + EPS)
    return (values * inverse * gain_vec, inverse)


def rms_backward(row_block, gain_vec, inverse, upstream):
    scaled_rows = row_block.astype(jnp.float32) * inverse
    weighted = upstream * gain_vec
    inner_mean = jnp.mean(weighted * scaled_rows, axis=-1, keepdims=True)
    return inverse * (weighted - scaled_rows * inner_mean)


def attend_forward(queries, key_rows, value_rows, usable):
    factor = queries.shape[-1] ** (-0.5)
    scores = (
        jnp.einsum("sbhd,skd->shbk", queries.astype(jnp.float32), key_rows.astype(jnp.float32))
        * factor
    )
    scores = jnp.where(usable[:, None, None, :], scores, NEG_FILL)
    highest = jnp.max(scores, axis=-1, keepdims=True)
    exponent_terms = jnp.exp(scores - highest)
    probabilities = exponent_terms / jnp.sum(exponent_terms, axis=-1, keepdims=True)
    probs_low = probabilities.astype(jnp.bfloat16)
    attended = jnp.einsum(
        "shbk,skd->sbhd", probs_low.astype(jnp.float32), value_rows.astype(jnp.float32)
    )
    return (probabilities, probs_low, attended.astype(jnp.bfloat16))


def attend_backward(queries, key_rows, value_rows, probabilities, probs_low, grad_attended):
    factor = queries.shape[-1] ** (-0.5)
    grad_probs = jnp.einsum(
        "sbhd,skd->shbk", grad_attended.astype(jnp.float32), value_rows.astype(jnp.float32)
    )
    inner_sum = jnp.sum(probabilities * grad_probs, axis=-1, keepdims=True)
    grad_scores = (probabilities * (grad_probs - inner_sum) * factor).astype(jnp.bfloat16)
    grad_queries = jnp.einsum(
        "shbk,skd->sbhd", grad_scores.astype(jnp.float32), key_rows.astype(jnp.float32)
    )
    grad_keys = jnp.einsum(
        "shbk,sbhd->skd", grad_scores.astype(jnp.float32), queries.astype(jnp.float32)
    )
    grad_values = jnp.einsum(
        "shbk,sbhd->skd", probs_low.astype(jnp.float32), grad_attended.astype(jnp.float32)
    )
    return (grad_queries.astype(jnp.bfloat16), grad_keys, grad_values)


def attention_forward(
    row_block,
    query_weights,
    own_kv_weights,
    key_cache,
    prefix_value_cache,
    lengths,
    first_head,
):
    heads_here = query_weights.shape[1] // HEAD_SIZE
    query_group_count = QUERY_HEADS // KEY_VALUE_HEADS
    row_count = row_block.shape[0]
    seq_count = row_count // BLOCK
    key_value_width = KEY_VALUE_HEADS * HEAD_SIZE
    kv_first = first_head // query_group_count
    queries = jnp.dot(row_block, query_weights, preferred_element_type=jnp.float32).astype(
        jnp.bfloat16
    )
    queries = queries.reshape(seq_count, BLOCK, heads_here, HEAD_SIZE)
    usable = jnp.concatenate(
        [
            jnp.arange(PREFIX_SLOTS)[None, :] < lengths[:, None],
            jnp.ones((seq_count, BLOCK), dtype=jnp.bool_),
        ],
        axis=1,
    )
    kv_now = kv_first + 0
    own_rows = jnp.dot(row_block, own_kv_weights, preferred_element_type=jnp.float32).astype(
        jnp.bfloat16
    )
    kv_rows = head_gather(own_rows, 1)
    pair_rows = jnp.concatenate(
        [
            lax.dynamic_slice_in_dim(kv_rows, kv_now * HEAD_SIZE, HEAD_SIZE, 1),
            lax.dynamic_slice_in_dim(kv_rows, key_value_width + kv_now * HEAD_SIZE, HEAD_SIZE, 1),
        ],
        axis=1,
    )
    key_rows = jnp.concatenate(
        [
            lax.dynamic_slice_in_dim(key_cache, kv_now * HEAD_SIZE, HEAD_SIZE, 2),
            pair_rows[:, :HEAD_SIZE].reshape(seq_count, BLOCK, HEAD_SIZE),
        ],
        axis=1,
    )
    value_rows = jnp.concatenate(
        [
            lax.dynamic_slice_in_dim(prefix_value_cache, kv_now * HEAD_SIZE, HEAD_SIZE, 2),
            pair_rows[:, HEAD_SIZE:].reshape(seq_count, BLOCK, HEAD_SIZE),
        ],
        axis=1,
    )
    probabilities, probs_low, attended = attend_forward(queries, key_rows, value_rows, usable)
    saved = [(queries, key_rows, value_rows, probabilities, probs_low)]
    joined = attended.reshape(row_count, heads_here * HEAD_SIZE)
    return (joined, saved)


def attention_backward(grad_rows, query_weights, output_weights, own_kv_weights, saved, kv_now):
    heads_here = query_weights.shape[1] // HEAD_SIZE
    row_count = grad_rows.shape[0]
    seq_count = row_count // BLOCK
    key_value_width = KEY_VALUE_HEADS * HEAD_SIZE
    grad_attn = jnp.einsum(
        "td,fd->tf", grad_rows, output_weights, preferred_element_type=jnp.float32
    ).astype(jnp.bfloat16)
    grad_attn = grad_attn.reshape(seq_count, BLOCK, heads_here, HEAD_SIZE)
    query_part, key_rows, value_rows, probabilities, probs_low = saved[0]
    grad_queries, grad_keys, grad_values = attend_backward(
        query_part, key_rows, value_rows, probabilities, probs_low, grad_attn
    )
    placed = jnp.zeros((row_count, 2 * key_value_width), jnp.float32)
    placed = lax.dynamic_update_slice_in_dim(
        placed, grad_keys[:, PREFIX_SLOTS:].reshape(row_count, HEAD_SIZE), kv_now * HEAD_SIZE, 1
    )
    placed = lax.dynamic_update_slice_in_dim(
        placed,
        grad_values[:, PREFIX_SLOTS:].reshape(row_count, HEAD_SIZE),
        key_value_width + kv_now * HEAD_SIZE,
        1,
    )
    own_grads = lax.psum_scatter(placed, "head", scatter_dimension=1, tiled=True)
    running = jnp.einsum(
        "tc,dc->td", own_grads, own_kv_weights.astype(jnp.float32), precision=lax.Precision.HIGHEST
    )
    query_flat = grad_queries.reshape(row_count, heads_here * HEAD_SIZE)
    return running + jnp.einsum(
        "tf,df->td", query_flat, query_weights, preferred_element_type=jnp.float32
    )


def head_gather(block, axis):
    count = lax.axis_size("head")
    me = lax.axis_index("head")
    parts = [block] + [
        lax.ppermute(block, "head", perm=[(j, (j + shift) % count) for j in range(count)])
        for shift in range(1, count)
    ]
    reversed_parts = parts[::-1]
    doubled = jnp.stack(reversed_parts + reversed_parts)
    ordered = lax.dynamic_slice_in_dim(doubled, count - 1 - me, count, 0)
    ordered = jnp.moveaxis(ordered, 0, axis)
    merged = list(block.shape)
    merged[axis] = count * block.shape[axis]
    return ordered.reshape(merged)


def head_rows(row_block):
    return head_gather(row_block, 0)


def head_sums(partial_rows):
    count = lax.axis_size("head")
    me = lax.axis_index("head")
    chunks = partial_rows.reshape((count, -1) + partial_rows.shape[1:])
    total = chunks[me]
    for shift in range(1, count):
        total = total + lax.ppermute(
            chunks[(me + shift) % count],
            "head",
            perm=[(j, (j + shift) % count) for j in range(count)],
        )
    return total


def to_experts(outgoing):
    return lax.all_to_all(outgoing, ("expert", "head"), split_axis=0, concat_axis=0, tiled=True)


def from_experts(results):
    return lax.all_to_all(results, ("expert", "head"), split_axis=0, concat_axis=0, tiled=True)


def body(
    hidden_in,
    out_grad,
    loss_mask,
    expert_ids,
    gate_weights,
    cache_lengths,
    key_cache,
    prefix_value_cache,
    attn_gain,
    moe_gain,
    w_query,
    key_value_weight,
    w_output,
    w_gate,
    w_up,
    w_down,
):
    highest_prec = lax.Precision.HIGHEST
    owned = hidden_in.shape[0]
    width = hidden_in.shape[1]
    normed_one, inverse_one = rms_forward(hidden_in, attn_gain)
    attn_rows = normed_one.astype(jnp.bfloat16)
    heads_here = w_query.shape[1] // HEAD_SIZE
    first_head = lax.axis_index("head") * heads_here
    gathered_rows = head_rows(attn_rows)
    attended, saved = attention_forward(
        gathered_rows, w_query, key_value_weight, key_cache, prefix_value_cache, cache_lengths, first_head
    )
    mixed = head_sums(jnp.dot(attended, w_output, preferred_element_type=jnp.float32))
    hidden = (hidden_in.astype(jnp.float32) + mixed).astype(jnp.bfloat16)
    normed_two, inverse_two = rms_forward(hidden, moe_gain)
    moe_rows = normed_two.astype(jnp.bfloat16)
    device_count = lax.axis_size("expert") * lax.axis_size("head")
    capacity = (owned * TOP * 4 + 3 * device_count - 1) // (3 * device_count)
    slot_total = device_count * capacity
    flat_ids = expert_ids.reshape(-1)
    one_hot = (flat_ids[:, None] == jnp.arange(device_count, dtype=jnp.int32)[None, :]).astype(
        jnp.int32
    )
    earlier = jnp.cumsum(one_hot, axis=0) - one_hot
    position = jnp.sum(earlier * one_hot, axis=1)
    target = flat_ids * capacity + position
    matched = (jnp.arange(slot_total, dtype=jnp.int32)[:, None] == target[None, :]).reshape(
        device_count, capacity, owned, TOP
    )
    placement = jnp.any(matched, axis=3).astype(jnp.bfloat16)
    weighting = jnp.sum(jnp.where(matched, gate_weights[None, None, :, :], 0.0), axis=3)
    cotangent = out_grad.astype(jnp.float32) * loss_mask.astype(jnp.float32)[:, None]
    lanes = 128
    pieces = width // lanes
    outgoing = jnp.einsum(
        "dct,tkl->dckl",
        placement,
        moe_rows.reshape(owned, pieces, lanes),
        preferred_element_type=jnp.float32,
    ).astype(jnp.bfloat16)
    grad_out = jnp.einsum(
        "dct,tkl->dckl",
        weighting,
        cotangent.reshape(owned, pieces, lanes),
        precision=highest_prec,
    ).astype(jnp.bfloat16)
    flat_shape = (device_count, capacity * pieces, lanes)
    split_shape = (device_count, capacity, pieces, lanes)
    rows_in = to_experts(outgoing.reshape(flat_shape)).reshape(split_shape)
    grads_in = to_experts(grad_out.reshape(flat_shape)).reshape(split_shape)
    gate_matrix = w_gate[0].reshape(pieces, lanes, -1)
    up_matrix = w_up[0].reshape(pieces, lanes, -1)
    down_matrix = w_down[0]
    gate_pre = jnp.einsum(
        "sckl,klf->scf", rows_in, gate_matrix, preferred_element_type=jnp.float32
    )
    up_pre = jnp.einsum("sckl,klf->scf", rows_in, up_matrix, preferred_element_type=jnp.float32)
    sigma = jax.nn.sigmoid(gate_pre)
    activated = (gate_pre * sigma * up_pre).astype(jnp.bfloat16)
    result = jnp.einsum(
        "scf,fw->scw", activated, down_matrix, preferred_element_type=jnp.float32
    ).astype(jnp.bfloat16)
    grad_act = jnp.einsum(
        "scw,fw->scf",
        grads_in.reshape(device_count, capacity, width),
        down_matrix,
        preferred_element_type=jnp.float32,
    )
    grad_gate = (grad_act * up_pre * sigma * (1.0 + gate_pre * (1.0 - sigma))).astype(jnp.bfloat16)
    grad_up = (grad_act * gate_pre * sigma).astype(jnp.bfloat16)
    grad_back = jnp.einsum(
        "scf,klf->sckl", grad_gate, gate_matrix, preferred_element_type=jnp.float32
    )
    grad_back = grad_back + jnp.einsum(
        "scf,klf->sckl", grad_up, up_matrix, preferred_element_type=jnp.float32
    )
    grad_back = grad_back.astype(jnp.bfloat16)
    result_home = from_experts(result.reshape(flat_shape)).reshape(split_shape)
    grad_home = from_experts(grad_back.reshape(flat_shape)).reshape(split_shape)
    moe_sum = jnp.einsum(
        "dct,dckl->tkl",
        weighting,
        result_home.astype(jnp.float32),
        precision=highest_prec,
    ).reshape(owned, width)
    layer_out = (hidden.astype(jnp.float32) + moe_sum).astype(jnp.bfloat16)
    grad_moe = jnp.einsum(
        "dct,dckl->tkl", placement, grad_home, preferred_element_type=jnp.float32
    ).reshape(owned, width)
    grad_hidden = cotangent + rms_backward(hidden, moe_gain, inverse_two, grad_moe)
    grad_low = grad_hidden.astype(jnp.bfloat16)
    grad_gathered = head_rows(grad_low)
    grad_attn_rows = head_sums(
        attention_backward(
            grad_gathered,
            w_query,
            w_output,
            key_value_weight,
            saved,
            first_head // (QUERY_HEADS // KEY_VALUE_HEADS),
        )
    )
    input_grad = (
        grad_hidden + rms_backward(hidden_in, attn_gain, inverse_one, grad_attn_rows)
    ).astype(jnp.bfloat16)
    return (layer_out, input_grad)


def solution(mesh):
    in_specs = (
        P(("groups", "expert", "head"), None),
        P(("groups", "expert", "head"), None),
        P(("groups", "expert", "head")),
        P(("groups", "expert", "head"), None),
        P(("groups", "expert", "head"), None),
        P(("groups", "expert")),
        P(("groups", "expert"), None, None),
        P(("groups", "expert"), None, None),
        P(),
        P(),
        P(None, "head"),
        P(None, "head"),
        P("head", None),
        P(("expert", "head"), None, None),
        P(("expert", "head"), None, None),
        P(("expert", "head"), None, None),
    )
    out_specs = (P(("groups", "expert", "head"), None), P(("groups", "expert", "head"), None))
    return jax.shard_map(body, mesh=mesh, in_specs=in_specs, out_specs=out_specs, check_vma=False)
```

```python
import jax
import jax.numpy as jnp
from jax import lax
from jax.sharding import PartitionSpec as P

QUERY_HEADS = 16
KEY_VALUE_HEADS = 2
HEAD_SIZE = 128
TOP = 8
BLOCK = 16
PREFIX_SLOTS = 32


EPS = 1e-06
NEG_FILL = -1e30


def rms_forward(row_block, gain_vec):
    values = row_block.astype(jnp.float32)
    inverse = lax.rsqrt(jnp.mean(values * values, axis=-1, keepdims=True) + EPS)
    return (values * inverse * gain_vec, inverse)


def rms_backward(row_block, gain_vec, inverse, upstream):
    scaled_rows = row_block.astype(jnp.float32) * inverse
    weighted = upstream * gain_vec
    inner_mean = jnp.mean(weighted * scaled_rows, axis=-1, keepdims=True)
    return inverse * (weighted - scaled_rows * inner_mean)


def attend_forward(queries, key_rows, value_rows, usable):
    factor = queries.shape[-1] ** (-0.5)
    scores = (
        jnp.einsum("sbhd,skd->shbk", queries.astype(jnp.float32), key_rows.astype(jnp.float32))
        * factor
    )
    scores = jnp.where(usable[:, None, None, :], scores, NEG_FILL)
    highest = jnp.max(scores, axis=-1, keepdims=True)
    exponent_terms = jnp.exp(scores - highest)
    probabilities = exponent_terms / jnp.sum(exponent_terms, axis=-1, keepdims=True)
    probs_low = probabilities.astype(jnp.bfloat16)
    attended = jnp.einsum(
        "shbk,skd->sbhd", probs_low.astype(jnp.float32), value_rows.astype(jnp.float32)
    )
    return (probabilities, probs_low, attended.astype(jnp.bfloat16))


def attend_backward(queries, key_rows, value_rows, probabilities, probs_low, grad_attended):
    factor = queries.shape[-1] ** (-0.5)
    grad_probs = jnp.einsum(
        "sbhd,skd->shbk", grad_attended.astype(jnp.float32), value_rows.astype(jnp.float32)
    )
    inner_sum = jnp.sum(probabilities * grad_probs, axis=-1, keepdims=True)
    grad_scores = (probabilities * (grad_probs - inner_sum) * factor).astype(jnp.bfloat16)
    grad_queries = jnp.einsum(
        "shbk,skd->sbhd", grad_scores.astype(jnp.float32), key_rows.astype(jnp.float32)
    )
    grad_keys = jnp.einsum(
        "shbk,sbhd->skd", grad_scores.astype(jnp.float32), queries.astype(jnp.float32)
    )
    grad_values = jnp.einsum(
        "shbk,sbhd->skd", probs_low.astype(jnp.float32), grad_attended.astype(jnp.float32)
    )
    return (grad_queries.astype(jnp.bfloat16), grad_keys, grad_values)


def attention_forward(
    row_block,
    query_weights,
    own_kv_weights,
    key_cache,
    prefix_value_cache,
    lengths,
    first_head,
):
    heads_here = query_weights.shape[1] // HEAD_SIZE
    query_group_count = QUERY_HEADS // KEY_VALUE_HEADS
    row_count = row_block.shape[0]
    seq_count = row_count // BLOCK
    key_value_width = KEY_VALUE_HEADS * HEAD_SIZE
    kv_first = first_head // query_group_count
    queries = jnp.dot(row_block, query_weights, preferred_element_type=jnp.float32).astype(
        jnp.bfloat16
    )
    queries = queries.reshape(seq_count, BLOCK, heads_here, HEAD_SIZE)
    usable = jnp.concatenate(
        [
            jnp.arange(PREFIX_SLOTS)[None, :] < lengths[:, None],
            jnp.ones((seq_count, BLOCK), dtype=jnp.bool_),
        ],
        axis=1,
    )
    kv_now = kv_first + 0
    own_rows = jnp.dot(row_block, own_kv_weights, preferred_element_type=jnp.float32).astype(
        jnp.bfloat16
    )
    kv_rows = head_gather(own_rows, 1)
    pair_rows = jnp.concatenate(
        [
            lax.dynamic_slice_in_dim(kv_rows, kv_now * HEAD_SIZE, HEAD_SIZE, 1),
            lax.dynamic_slice_in_dim(kv_rows, key_value_width + kv_now * HEAD_SIZE, HEAD_SIZE, 1),
        ],
        axis=1,
    )
    key_rows = jnp.concatenate(
        [
            lax.dynamic_slice_in_dim(key_cache, kv_now * HEAD_SIZE, HEAD_SIZE, 2),
            pair_rows[:, :HEAD_SIZE].reshape(seq_count, BLOCK, HEAD_SIZE),
        ],
        axis=1,
    )
    value_rows = jnp.concatenate(
        [
            lax.dynamic_slice_in_dim(prefix_value_cache, kv_now * HEAD_SIZE, HEAD_SIZE, 2),
            pair_rows[:, HEAD_SIZE:].reshape(seq_count, BLOCK, HEAD_SIZE),
        ],
        axis=1,
    )
    probabilities, probs_low, attended = attend_forward(queries, key_rows, value_rows, usable)
    saved = [(queries, key_rows, value_rows, probabilities, probs_low)]
    joined = attended.reshape(row_count, heads_here * HEAD_SIZE)
    return (joined, saved)


def attention_backward(
    grad_rows, query_weights, output_weights, own_kv_weights, saved, kv_now, carried
):
    heads_here = query_weights.shape[1] // HEAD_SIZE
    row_count = grad_rows.shape[0]
    seq_count = row_count // BLOCK
    key_value_width = KEY_VALUE_HEADS * HEAD_SIZE
    grad_attn = jnp.einsum(
        "td,fd->tf", grad_rows, output_weights, preferred_element_type=jnp.float32
    ).astype(jnp.bfloat16)
    grad_attn = grad_attn.reshape(seq_count, BLOCK, heads_here, HEAD_SIZE)
    query_part, key_rows, value_rows, probabilities, probs_low = saved[0]
    grad_queries, grad_keys, grad_values = attend_backward(
        query_part, key_rows, value_rows, probabilities, probs_low, grad_attn
    )
    placed = jnp.zeros((row_count, 2 * key_value_width), jnp.float32)
    placed = lax.dynamic_update_slice_in_dim(
        placed, grad_keys[:, PREFIX_SLOTS:].reshape(row_count, HEAD_SIZE), kv_now * HEAD_SIZE, 1
    )
    placed = lax.dynamic_update_slice_in_dim(
        placed,
        grad_values[:, PREFIX_SLOTS:].reshape(row_count, HEAD_SIZE),
        key_value_width + kv_now * HEAD_SIZE,
        1,
    )
    placed, carried = lax.optimization_barrier((placed, carried))
    own_grads = lax.psum_scatter(placed, "head", scatter_dimension=1, tiled=True)
    running = jnp.einsum(
        "tc,dc->td", own_grads, own_kv_weights.astype(jnp.float32), precision=lax.Precision.HIGHEST
    )
    query_flat = grad_queries.reshape(row_count, heads_here * HEAD_SIZE)
    total = running + jnp.einsum(
        "tf,df->td", query_flat, query_weights, preferred_element_type=jnp.float32
    )
    return (total, carried)


def head_gather(block, axis):
    count = lax.axis_size("head")
    me = lax.axis_index("head")
    parts = [block] + [
        lax.ppermute(block, "head", perm=[(j, (j + shift) % count) for j in range(count)])
        for shift in range(1, count)
    ]
    reversed_parts = parts[::-1]
    doubled = jnp.stack(reversed_parts + reversed_parts)
    ordered = lax.dynamic_slice_in_dim(doubled, count - 1 - me, count, 0)
    ordered = jnp.moveaxis(ordered, 0, axis)
    merged = list(block.shape)
    merged[axis] = count * block.shape[axis]
    return ordered.reshape(merged)


def head_rows(row_block):
    return head_gather(row_block, 0)


def head_sums(partial_rows):
    count = lax.axis_size("head")
    me = lax.axis_index("head")
    chunks = partial_rows.reshape((count, -1) + partial_rows.shape[1:])
    total = chunks[me]
    for shift in range(1, count):
        total = total + lax.ppermute(
            chunks[(me + shift) % count],
            "head",
            perm=[(j, (j + shift) % count) for j in range(count)],
        )
    return total


def to_experts(outgoing):
    return lax.all_to_all(outgoing, ("expert", "head"), split_axis=0, concat_axis=0, tiled=True)


def from_experts(results):
    return lax.all_to_all(results, ("expert", "head"), split_axis=0, concat_axis=0, tiled=True)


def body(
    hidden_in,
    out_grad,
    loss_mask,
    expert_ids,
    gate_weights,
    cache_lengths,
    key_cache,
    prefix_value_cache,
    attn_gain,
    moe_gain,
    w_query,
    key_value_weight,
    w_output,
    w_gate,
    w_up,
    w_down,
):
    highest_prec = lax.Precision.HIGHEST
    owned = hidden_in.shape[0]
    width = hidden_in.shape[1]
    normed_one, inverse_one = rms_forward(hidden_in, attn_gain)
    attn_rows = normed_one.astype(jnp.bfloat16)
    heads_here = w_query.shape[1] // HEAD_SIZE
    first_head = lax.axis_index("head") * heads_here
    gathered_rows = head_rows(attn_rows)
    attended, saved = attention_forward(
        gathered_rows, w_query, key_value_weight, key_cache, prefix_value_cache, cache_lengths, first_head
    )
    mixed = head_sums(jnp.dot(attended, w_output, preferred_element_type=jnp.float32))
    hidden = (hidden_in.astype(jnp.float32) + mixed).astype(jnp.bfloat16)
    normed_two, inverse_two = rms_forward(hidden, moe_gain)
    moe_rows = normed_two.astype(jnp.bfloat16)
    device_count = lax.axis_size("expert") * lax.axis_size("head")
    capacity = (owned * TOP * 4 + 3 * device_count - 1) // (3 * device_count)
    slot_total = device_count * capacity
    flat_ids = expert_ids.reshape(-1)
    one_hot = (flat_ids[:, None] == jnp.arange(device_count, dtype=jnp.int32)[None, :]).astype(
        jnp.int32
    )
    earlier = jnp.cumsum(one_hot, axis=0) - one_hot
    position = jnp.sum(earlier * one_hot, axis=1)
    target = flat_ids * capacity + position
    matched = (jnp.arange(slot_total, dtype=jnp.int32)[:, None] == target[None, :]).reshape(
        device_count, capacity, owned, TOP
    )
    placement = jnp.any(matched, axis=3).astype(jnp.bfloat16)
    weighting = jnp.sum(jnp.where(matched, gate_weights[None, None, :, :], 0.0), axis=3)
    cotangent = out_grad.astype(jnp.float32) * loss_mask.astype(jnp.float32)[:, None]
    lanes = 128
    pieces = width // lanes
    outgoing = jnp.einsum(
        "dct,tkl->dckl",
        placement,
        moe_rows.reshape(owned, pieces, lanes),
        preferred_element_type=jnp.float32,
    ).astype(jnp.bfloat16)
    grad_out = jnp.einsum(
        "dct,tkl->dckl",
        weighting,
        cotangent.reshape(owned, pieces, lanes),
        precision=highest_prec,
    ).astype(jnp.bfloat16)
    flat_shape = (device_count, capacity * pieces, lanes)
    split_shape = (device_count, capacity, pieces, lanes)
    rows_in = to_experts(outgoing.reshape(flat_shape)).reshape(split_shape)
    grads_in = to_experts(grad_out.reshape(flat_shape)).reshape(split_shape)
    gate_matrix = w_gate[0].reshape(pieces, lanes, -1)
    up_matrix = w_up[0].reshape(pieces, lanes, -1)
    down_matrix = w_down[0].reshape(-1, pieces, lanes)
    gate_pre = jnp.einsum(
        "sckl,klf->scf", rows_in, gate_matrix, preferred_element_type=jnp.float32
    )
    up_pre = jnp.einsum("sckl,klf->scf", rows_in, up_matrix, preferred_element_type=jnp.float32)
    sigma = jax.nn.sigmoid(gate_pre)
    activated = (gate_pre * sigma * up_pre).astype(jnp.bfloat16)
    result = jnp.einsum(
        "scf,fkl->sckl", activated, down_matrix, preferred_element_type=jnp.float32
    ).astype(jnp.bfloat16)
    grad_act = jnp.einsum(
        "sckl,fkl->scf", grads_in, down_matrix, preferred_element_type=jnp.float32
    )
    grad_gate = (grad_act * up_pre * sigma * (1.0 + gate_pre * (1.0 - sigma))).astype(jnp.bfloat16)
    grad_up = (grad_act * gate_pre * sigma).astype(jnp.bfloat16)
    grad_back = jnp.einsum(
        "scf,klf->sckl", grad_gate, gate_matrix, preferred_element_type=jnp.float32
    )
    grad_back = grad_back + jnp.einsum(
        "scf,klf->sckl", grad_up, up_matrix, preferred_element_type=jnp.float32
    )
    grad_back = grad_back.astype(jnp.bfloat16)
    grad_home = from_experts(grad_back.reshape(flat_shape)).reshape(split_shape)
    grad_moe = jnp.einsum(
        "dct,dckl->tkl", placement, grad_home, preferred_element_type=jnp.float32
    ).reshape(owned, width)
    grad_hidden = cotangent + rms_backward(hidden, moe_gain, inverse_two, grad_moe)
    grad_low = grad_hidden.astype(jnp.bfloat16)
    grad_gathered = head_rows(grad_low)
    result, grad_gathered = lax.optimization_barrier((result, grad_gathered))
    result_home = from_experts(result.reshape(flat_shape)).reshape(split_shape)
    grad_partial, result_home = attention_backward(
        grad_gathered,
        w_query,
        w_output,
        key_value_weight,
        saved,
        first_head // (QUERY_HEADS // KEY_VALUE_HEADS),
        result_home,
    )
    grad_attn_rows = head_sums(grad_partial)
    input_grad = (
        grad_hidden + rms_backward(hidden_in, attn_gain, inverse_one, grad_attn_rows)
    ).astype(jnp.bfloat16)
    moe_sum = jnp.einsum(
        "dct,dckl->tkl",
        weighting,
        result_home.astype(jnp.float32),
        precision=highest_prec,
    ).reshape(owned, width)
    layer_out = (hidden.astype(jnp.float32) + moe_sum).astype(jnp.bfloat16)
    return (layer_out, input_grad)


def solution(mesh):
    in_specs = (
        P(("groups", "expert", "head"), None),
        P(("groups", "expert", "head"), None),
        P(("groups", "expert", "head")),
        P(("groups", "expert", "head"), None),
        P(("groups", "expert", "head"), None),
        P(("groups", "expert")),
        P(("groups", "expert"), None, None),
        P(("groups", "expert"), None, None),
        P(),
        P(),
        P(None, "head"),
        P(None, "head"),
        P("head", None),
        P(("expert", "head"), None, None),
        P(("expert", "head"), None, None),
        P(("expert", "head"), None, None),
    )
    out_specs = (P(("groups", "expert", "head"), None), P(("groups", "expert", "head"), None))
    return jax.shard_map(body, mesh=mesh, in_specs=in_specs, out_specs=out_specs, check_vma=False)
```

```python
import jax
import jax.numpy as jnp
from jax import lax
from jax.sharding import PartitionSpec as P

QUERY_HEADS = 16
KEY_VALUE_HEADS = 2
HEAD_SIZE = 128
TOP = 8
BLOCK = 16
PREFIX_SLOTS = 32


EPS = 1e-06
NEG_FILL = -1e30


def rms_forward(row_block, gain_vec):
    values = row_block.astype(jnp.float32)
    inverse = lax.rsqrt(jnp.mean(values * values, axis=-1, keepdims=True) + EPS)
    return (values * inverse * gain_vec, inverse)


def rms_backward(row_block, gain_vec, inverse, upstream):
    scaled_rows = row_block.astype(jnp.float32) * inverse
    weighted = upstream * gain_vec
    inner_mean = jnp.mean(weighted * scaled_rows, axis=-1, keepdims=True)
    return inverse * (weighted - scaled_rows * inner_mean)


def attend_forward(queries, key_rows, value_rows, usable):
    factor = queries.shape[-1] ** (-0.5)
    scores = (
        jnp.einsum("sbhd,skd->shbk", queries.astype(jnp.float32), key_rows.astype(jnp.float32))
        * factor
    )
    scores = jnp.where(usable[:, None, None, :], scores, NEG_FILL)
    highest = jnp.max(scores, axis=-1, keepdims=True)
    exponent_terms = jnp.exp(scores - highest)
    probabilities = exponent_terms / jnp.sum(exponent_terms, axis=-1, keepdims=True)
    probs_low = probabilities.astype(jnp.bfloat16)
    attended = jnp.einsum(
        "shbk,skd->sbhd", probs_low.astype(jnp.float32), value_rows.astype(jnp.float32)
    )
    return (probabilities, probs_low, attended.astype(jnp.bfloat16))


def attend_backward(queries, key_rows, value_rows, probabilities, probs_low, grad_attended):
    factor = queries.shape[-1] ** (-0.5)
    grad_probs = jnp.einsum(
        "sbhd,skd->shbk", grad_attended.astype(jnp.float32), value_rows.astype(jnp.float32)
    )
    inner_sum = jnp.sum(probabilities * grad_probs, axis=-1, keepdims=True)
    grad_scores = (probabilities * (grad_probs - inner_sum) * factor).astype(jnp.bfloat16)
    grad_queries = jnp.einsum(
        "shbk,skd->sbhd", grad_scores.astype(jnp.float32), key_rows.astype(jnp.float32)
    )
    grad_keys = jnp.einsum(
        "shbk,sbhd->skd", grad_scores.astype(jnp.float32), queries.astype(jnp.float32)
    )
    grad_values = jnp.einsum(
        "shbk,sbhd->skd", probs_low.astype(jnp.float32), grad_attended.astype(jnp.float32)
    )
    return (grad_queries.astype(jnp.bfloat16), grad_keys, grad_values)


def attention_forward(
    row_block,
    query_weights,
    own_kv_weights,
    key_cache,
    prefix_value_cache,
    lengths,
    first_head,
):
    heads_here = query_weights.shape[1] // HEAD_SIZE
    query_group_count = QUERY_HEADS // KEY_VALUE_HEADS
    row_count = row_block.shape[0]
    seq_count = row_count // BLOCK
    key_value_width = KEY_VALUE_HEADS * HEAD_SIZE
    kv_first = first_head // query_group_count
    queries = jnp.dot(row_block, query_weights, preferred_element_type=jnp.float32).astype(
        jnp.bfloat16
    )
    queries = queries.reshape(seq_count, BLOCK, heads_here, HEAD_SIZE)
    usable = jnp.concatenate(
        [
            jnp.arange(PREFIX_SLOTS)[None, :] < lengths[:, None],
            jnp.ones((seq_count, BLOCK), dtype=jnp.bool_),
        ],
        axis=1,
    )
    kv_now = kv_first + 0
    own_rows = jnp.dot(row_block, own_kv_weights, preferred_element_type=jnp.float32).astype(
        jnp.bfloat16
    )
    kv_rows = head_gather(own_rows, 1)
    pair_rows = jnp.concatenate(
        [
            lax.dynamic_slice_in_dim(kv_rows, kv_now * HEAD_SIZE, HEAD_SIZE, 1),
            lax.dynamic_slice_in_dim(kv_rows, key_value_width + kv_now * HEAD_SIZE, HEAD_SIZE, 1),
        ],
        axis=1,
    )
    key_rows = jnp.concatenate(
        [
            lax.dynamic_slice_in_dim(key_cache, kv_now * HEAD_SIZE, HEAD_SIZE, 2),
            pair_rows[:, :HEAD_SIZE].reshape(seq_count, BLOCK, HEAD_SIZE),
        ],
        axis=1,
    )
    value_rows = jnp.concatenate(
        [
            lax.dynamic_slice_in_dim(prefix_value_cache, kv_now * HEAD_SIZE, HEAD_SIZE, 2),
            pair_rows[:, HEAD_SIZE:].reshape(seq_count, BLOCK, HEAD_SIZE),
        ],
        axis=1,
    )
    probabilities, probs_low, attended = attend_forward(queries, key_rows, value_rows, usable)
    saved = [(queries, key_rows, value_rows, probabilities, probs_low)]
    joined = attended.reshape(row_count, heads_here * HEAD_SIZE)
    return (joined, saved)


def attention_backward(grad_rows, query_weights, output_weights, own_kv_weights, saved, kv_now):
    heads_here = query_weights.shape[1] // HEAD_SIZE
    row_count = grad_rows.shape[0]
    seq_count = row_count // BLOCK
    key_value_width = KEY_VALUE_HEADS * HEAD_SIZE
    grad_attn = jnp.einsum(
        "td,fd->tf", grad_rows, output_weights, preferred_element_type=jnp.float32
    ).astype(jnp.bfloat16)
    grad_attn = grad_attn.reshape(seq_count, BLOCK, heads_here, HEAD_SIZE)
    query_part, key_rows, value_rows, probabilities, probs_low = saved[0]
    grad_queries, grad_keys, grad_values = attend_backward(
        query_part, key_rows, value_rows, probabilities, probs_low, grad_attn
    )
    placed = jnp.zeros((row_count, 2 * key_value_width), jnp.float32)
    placed = lax.dynamic_update_slice_in_dim(
        placed, grad_keys[:, PREFIX_SLOTS:].reshape(row_count, HEAD_SIZE), kv_now * HEAD_SIZE, 1
    )
    placed = lax.dynamic_update_slice_in_dim(
        placed,
        grad_values[:, PREFIX_SLOTS:].reshape(row_count, HEAD_SIZE),
        key_value_width + kv_now * HEAD_SIZE,
        1,
    )
    own_grads = lax.psum_scatter(placed, "head", scatter_dimension=1, tiled=True)
    running = jnp.einsum(
        "tc,dc->td", own_grads, own_kv_weights.astype(jnp.float32), precision=lax.Precision.HIGHEST
    )
    query_flat = grad_queries.reshape(row_count, heads_here * HEAD_SIZE)
    return running + jnp.einsum(
        "tf,df->td", query_flat, query_weights, preferred_element_type=jnp.float32
    )


def head_gather(block, axis):
    count = lax.axis_size("head")
    me = lax.axis_index("head")
    parts = [block] + [
        lax.ppermute(block, "head", perm=[(j, (j + shift) % count) for j in range(count)])
        for shift in range(1, count)
    ]
    reversed_parts = parts[::-1]
    doubled = jnp.stack(reversed_parts + reversed_parts)
    ordered = lax.dynamic_slice_in_dim(doubled, count - 1 - me, count, 0)
    ordered = jnp.moveaxis(ordered, 0, axis)
    merged = list(block.shape)
    merged[axis] = count * block.shape[axis]
    return ordered.reshape(merged)


def head_rows(row_block):
    return head_gather(row_block, 0)


def head_sums(partial_rows):
    count = lax.axis_size("head")
    me = lax.axis_index("head")
    chunks = partial_rows.reshape((count, -1) + partial_rows.shape[1:])
    total = chunks[me]
    for shift in range(1, count):
        total = total + lax.ppermute(
            chunks[(me + shift) % count],
            "head",
            perm=[(j, (j + shift) % count) for j in range(count)],
        )
    return total


def to_experts(outgoing):
    return lax.all_to_all(outgoing, ("expert", "head"), split_axis=0, concat_axis=0, tiled=True)


def from_experts(results):
    return lax.all_to_all(results, ("expert", "head"), split_axis=0, concat_axis=0, tiled=True)


def body(
    hidden_in,
    out_grad,
    loss_mask,
    expert_ids,
    gate_weights,
    cache_lengths,
    key_cache,
    prefix_value_cache,
    attn_gain,
    moe_gain,
    w_query,
    key_value_weight,
    w_output,
    w_gate,
    w_up,
    w_down,
):
    highest_prec = lax.Precision.HIGHEST
    owned = hidden_in.shape[0]
    width = hidden_in.shape[1]
    normed_one, inverse_one = rms_forward(hidden_in, attn_gain)
    attn_rows = normed_one.astype(jnp.bfloat16)
    heads_here = w_query.shape[1] // HEAD_SIZE
    first_head = lax.axis_index("head") * heads_here
    gathered_rows = head_rows(attn_rows)
    attended, saved = attention_forward(
        gathered_rows, w_query, key_value_weight, key_cache, prefix_value_cache, cache_lengths, first_head
    )
    mixed = head_sums(jnp.dot(attended, w_output, preferred_element_type=jnp.float32))
    hidden = (hidden_in.astype(jnp.float32) + mixed).astype(jnp.bfloat16)
    normed_two, inverse_two = rms_forward(hidden, moe_gain)
    moe_rows = normed_two.astype(jnp.bfloat16)
    device_count = lax.axis_size("expert") * lax.axis_size("head")
    capacity = (owned * TOP * 4 + 3 * device_count - 1) // (3 * device_count)
    slot_total = device_count * capacity
    flat_ids = expert_ids.reshape(-1)
    one_hot = (flat_ids[:, None] == jnp.arange(device_count, dtype=jnp.int32)[None, :]).astype(
        jnp.int32
    )
    earlier = jnp.cumsum(one_hot, axis=0) - one_hot
    position = jnp.sum(earlier * one_hot, axis=1)
    target = flat_ids * capacity + position
    matched = (jnp.arange(slot_total, dtype=jnp.int32)[:, None] == target[None, :]).reshape(
        device_count, capacity, owned, TOP
    )
    placement = jnp.any(matched, axis=3).astype(jnp.bfloat16)
    weighting = jnp.sum(jnp.where(matched, gate_weights[None, None, :, :], 0.0), axis=3)
    cotangent = out_grad.astype(jnp.float32) * loss_mask.astype(jnp.float32)[:, None]
    lanes = 128
    pieces = width // lanes
    outgoing = jnp.einsum(
        "dct,tkl->dckl",
        placement,
        moe_rows.reshape(owned, pieces, lanes),
        preferred_element_type=jnp.float32,
    ).astype(jnp.bfloat16)
    grad_out = jnp.einsum(
        "dct,tkl->dckl",
        weighting,
        cotangent.reshape(owned, pieces, lanes),
        precision=highest_prec,
    ).astype(jnp.bfloat16)
    flat_shape = (device_count, capacity * pieces, lanes)
    split_shape = (device_count, capacity, pieces, lanes)
    rows_in = to_experts(outgoing.reshape(flat_shape)).reshape(split_shape)
    grads_in = to_experts(grad_out.reshape(flat_shape)).reshape(split_shape)
    gate_matrix = w_gate[0].reshape(pieces, lanes, -1)
    up_matrix = w_up[0].reshape(pieces, lanes, -1)
    down_matrix = w_down[0].reshape(-1, pieces, lanes)
    gate_pre = jnp.einsum(
        "sckl,klf->scf", rows_in, gate_matrix, preferred_element_type=jnp.float32
    )
    up_pre = jnp.einsum("sckl,klf->scf", rows_in, up_matrix, preferred_element_type=jnp.float32)
    sigma = jax.nn.sigmoid(gate_pre)
    activated = (gate_pre * sigma * up_pre).astype(jnp.bfloat16)
    result = jnp.einsum(
        "scf,fkl->sckl", activated, down_matrix, preferred_element_type=jnp.float32
    ).astype(jnp.bfloat16)
    grad_act = jnp.einsum(
        "sckl,fkl->scf", grads_in, down_matrix, preferred_element_type=jnp.float32
    )
    grad_gate = (grad_act * up_pre * sigma * (1.0 + gate_pre * (1.0 - sigma))).astype(jnp.bfloat16)
    grad_up = (grad_act * gate_pre * sigma).astype(jnp.bfloat16)
    grad_back = jnp.einsum(
        "scf,klf->sckl", grad_gate, gate_matrix, preferred_element_type=jnp.float32
    )
    grad_back = grad_back + jnp.einsum(
        "scf,klf->sckl", grad_up, up_matrix, preferred_element_type=jnp.float32
    )
    grad_back = grad_back.astype(jnp.bfloat16)
    result_home = from_experts(result.reshape(flat_shape)).reshape(split_shape)
    grad_home = from_experts(grad_back.reshape(flat_shape)).reshape(split_shape)
    moe_sum = jnp.einsum(
        "dct,dckl->tkl",
        weighting,
        result_home.astype(jnp.float32),
        precision=highest_prec,
    ).reshape(owned, width)
    layer_out = (hidden.astype(jnp.float32) + moe_sum).astype(jnp.bfloat16)
    grad_moe = jnp.einsum(
        "dct,dckl->tkl", placement, grad_home, preferred_element_type=jnp.float32
    ).reshape(owned, width)
    grad_hidden = cotangent + rms_backward(hidden, moe_gain, inverse_two, grad_moe)
    grad_low = grad_hidden.astype(jnp.bfloat16)
    grad_gathered = head_rows(grad_low)
    grad_attn_rows = head_sums(
        attention_backward(
            grad_gathered,
            w_query,
            w_output,
            key_value_weight,
            saved,
            first_head // (QUERY_HEADS // KEY_VALUE_HEADS),
        )
    )
    input_grad = (
        grad_hidden + rms_backward(hidden_in, attn_gain, inverse_one, grad_attn_rows)
    ).astype(jnp.bfloat16)
    return (layer_out, input_grad)


def solution(mesh):
    in_specs = (
        P(("groups", "expert", "head"), None),
        P(("groups", "expert", "head"), None),
        P(("groups", "expert", "head")),
        P(("groups", "expert", "head"), None),
        P(("groups", "expert", "head"), None),
        P(("groups", "expert")),
        P(("groups", "expert"), None, None),
        P(("groups", "expert"), None, None),
        P(),
        P(),
        P(None, "head"),
        P(None, "head"),
        P("head", None),
        P(("expert", "head"), None, None),
        P(("expert", "head"), None, None),
        P(("expert", "head"), None, None),
    )
    out_specs = (P(("groups", "expert", "head"), None), P(("groups", "expert", "head"), None))
    return jax.shard_map(body, mesh=mesh, in_specs=in_specs, out_specs=out_specs, check_vma=False)
```

```python
import jax
import jax.numpy as jnp
from jax import lax
from jax.sharding import PartitionSpec as P

QUERY_HEADS = 16
KEY_VALUE_HEADS = 2
HEAD_SIZE = 128
TOP = 8
BLOCK = 16
PREFIX_SLOTS = 32


EPS = 1e-06
NEG_FILL = -1e30


def rms_forward(row_block, gain_vec):
    values = row_block.astype(jnp.float32)
    inverse = lax.rsqrt(jnp.mean(values * values, axis=-1, keepdims=True) + EPS)
    return (values * inverse * gain_vec, inverse)


def rms_backward(row_block, gain_vec, inverse, upstream):
    scaled_rows = row_block.astype(jnp.float32) * inverse
    weighted = upstream * gain_vec
    inner_mean = jnp.mean(weighted * scaled_rows, axis=-1, keepdims=True)
    return inverse * (weighted - scaled_rows * inner_mean)


def attend_forward(queries, key_rows, value_rows, usable):
    factor = queries.shape[-1] ** (-0.5)
    scores = (
        jnp.einsum("sbhd,skd->shbk", queries.astype(jnp.float32), key_rows.astype(jnp.float32))
        * factor
    )
    scores = jnp.where(usable[:, None, None, :], scores, NEG_FILL)
    highest = jnp.max(scores, axis=-1, keepdims=True)
    exponent_terms = jnp.exp(scores - highest)
    probabilities = exponent_terms / jnp.sum(exponent_terms, axis=-1, keepdims=True)
    probs_low = probabilities.astype(jnp.bfloat16)
    attended = jnp.einsum(
        "shbk,skd->sbhd", probs_low.astype(jnp.float32), value_rows.astype(jnp.float32)
    )
    return (probabilities, probs_low, attended.astype(jnp.bfloat16))


def attend_backward(queries, key_rows, value_rows, probabilities, probs_low, grad_attended):
    factor = queries.shape[-1] ** (-0.5)
    grad_probs = jnp.einsum(
        "sbhd,skd->shbk", grad_attended.astype(jnp.float32), value_rows.astype(jnp.float32)
    )
    inner_sum = jnp.sum(probabilities * grad_probs, axis=-1, keepdims=True)
    grad_scores = (probabilities * (grad_probs - inner_sum) * factor).astype(jnp.bfloat16)
    grad_queries = jnp.einsum(
        "shbk,skd->sbhd", grad_scores.astype(jnp.float32), key_rows.astype(jnp.float32)
    )
    grad_keys = jnp.einsum(
        "shbk,sbhd->skd", grad_scores.astype(jnp.float32), queries.astype(jnp.float32)
    )
    grad_values = jnp.einsum(
        "shbk,sbhd->skd", probs_low.astype(jnp.float32), grad_attended.astype(jnp.float32)
    )
    return (grad_queries.astype(jnp.bfloat16), grad_keys, grad_values)


def attention_forward(
    row_block,
    query_weights,
    own_kv_weights,
    key_cache,
    prefix_value_cache,
    lengths,
    first_head,
):
    heads_here = query_weights.shape[1] // HEAD_SIZE
    query_group_count = QUERY_HEADS // KEY_VALUE_HEADS
    row_count = row_block.shape[0]
    seq_count = row_count // BLOCK
    key_value_width = KEY_VALUE_HEADS * HEAD_SIZE
    kv_first = first_head // query_group_count
    queries = jnp.dot(row_block, query_weights, preferred_element_type=jnp.float32).astype(
        jnp.bfloat16
    )
    queries = queries.reshape(seq_count, BLOCK, heads_here, HEAD_SIZE)
    usable = jnp.concatenate(
        [
            jnp.arange(PREFIX_SLOTS)[None, :] < lengths[:, None],
            jnp.ones((seq_count, BLOCK), dtype=jnp.bool_),
        ],
        axis=1,
    )
    kv_now = kv_first + 0
    own_rows = jnp.dot(row_block, own_kv_weights, preferred_element_type=jnp.float32).astype(
        jnp.bfloat16
    )
    kv_rows = head_gather(own_rows, 1)
    pair_rows = jnp.concatenate(
        [
            lax.dynamic_slice_in_dim(kv_rows, kv_now * HEAD_SIZE, HEAD_SIZE, 1),
            lax.dynamic_slice_in_dim(kv_rows, key_value_width + kv_now * HEAD_SIZE, HEAD_SIZE, 1),
        ],
        axis=1,
    )
    key_rows = jnp.concatenate(
        [
            lax.dynamic_slice_in_dim(key_cache, kv_now * HEAD_SIZE, HEAD_SIZE, 2),
            pair_rows[:, :HEAD_SIZE].reshape(seq_count, BLOCK, HEAD_SIZE),
        ],
        axis=1,
    )
    value_rows = jnp.concatenate(
        [
            lax.dynamic_slice_in_dim(prefix_value_cache, kv_now * HEAD_SIZE, HEAD_SIZE, 2),
            pair_rows[:, HEAD_SIZE:].reshape(seq_count, BLOCK, HEAD_SIZE),
        ],
        axis=1,
    )
    probabilities, probs_low, attended = attend_forward(queries, key_rows, value_rows, usable)
    saved = [(queries, key_rows, value_rows, probabilities, probs_low)]
    joined = attended.reshape(row_count, heads_here * HEAD_SIZE)
    return (joined, saved)


def attention_backward(grad_rows, query_weights, output_weights, own_kv_weights, saved, kv_now):
    heads_here = query_weights.shape[1] // HEAD_SIZE
    row_count = grad_rows.shape[0]
    seq_count = row_count // BLOCK
    key_value_width = KEY_VALUE_HEADS * HEAD_SIZE
    grad_attn = jnp.einsum(
        "td,fd->tf", grad_rows, output_weights, preferred_element_type=jnp.float32
    ).astype(jnp.bfloat16)
    grad_attn = grad_attn.reshape(seq_count, BLOCK, heads_here, HEAD_SIZE)
    query_part, key_rows, value_rows, probabilities, probs_low = saved[0]
    grad_queries, grad_keys, grad_values = attend_backward(
        query_part, key_rows, value_rows, probabilities, probs_low, grad_attn
    )
    placed = jnp.zeros((row_count, 2 * key_value_width), jnp.float32)
    placed = lax.dynamic_update_slice_in_dim(
        placed, grad_keys[:, PREFIX_SLOTS:].reshape(row_count, HEAD_SIZE), kv_now * HEAD_SIZE, 1
    )
    placed = lax.dynamic_update_slice_in_dim(
        placed,
        grad_values[:, PREFIX_SLOTS:].reshape(row_count, HEAD_SIZE),
        key_value_width + kv_now * HEAD_SIZE,
        1,
    )
    own_grads = head_sums(placed, axis=1)
    running = jnp.einsum(
        "tc,dc->td", own_grads, own_kv_weights.astype(jnp.float32), precision=lax.Precision.HIGHEST
    )
    query_flat = grad_queries.reshape(row_count, heads_here * HEAD_SIZE)
    return running + jnp.einsum(
        "tf,df->td", query_flat, query_weights, preferred_element_type=jnp.float32
    )


def head_gather(block, axis):
    count = lax.axis_size("head")
    me = lax.axis_index("head")
    parts = [block] + [
        lax.ppermute(block, "head", perm=[(j, (j + shift) % count) for j in range(count)])
        for shift in range(1, count)
    ]
    return head_order(parts, axis)


def head_order(parts, axis):
    count = lax.axis_size("head")
    me = lax.axis_index("head")
    block = parts[0]
    ordered = jnp.take(jnp.stack(parts), (me - jnp.arange(count)) % count, axis=0)
    ordered = jnp.moveaxis(ordered, 0, axis)
    merged = list(block.shape)
    merged[axis] = count * block.shape[axis]
    return ordered.reshape(merged)


def head_rows(row_block):
    return head_gather(row_block, 0)


def after_first_hop(block, waiting):
    count = lax.axis_size("head")
    first = lax.ppermute(block, "head", perm=[(j, (j + 1) % count) for j in range(count)])
    return lax.optimization_barrier((waiting, first))


def head_sums(partial_rows, axis=0):
    count = lax.axis_size("head")
    me = lax.axis_index("head")
    size = partial_rows.shape[axis] // count

    def chunk(index):
        return lax.dynamic_slice_in_dim(partial_rows, index * size, size, axis)

    total = chunk(me)
    for shift in range(1, count):
        total = total + lax.ppermute(
            chunk((me + shift) % count),
            "head",
            perm=[(j, (j + shift) % count) for j in range(count)],
        )
    return total


def to_experts(outgoing):
    return lax.all_to_all(outgoing, ("expert", "head"), split_axis=0, concat_axis=0, tiled=True)


def from_experts(results):
    return lax.all_to_all(results, ("expert", "head"), split_axis=0, concat_axis=0, tiled=True)


def body(
    hidden_in,
    out_grad,
    loss_mask,
    expert_ids,
    gate_weights,
    cache_lengths,
    key_cache,
    prefix_value_cache,
    attn_gain,
    moe_gain,
    w_query,
    key_value_weight,
    w_output,
    w_gate,
    w_up,
    w_down,
):
    highest_prec = lax.Precision.HIGHEST
    owned = hidden_in.shape[0]
    width = hidden_in.shape[1]
    normed_one, inverse_one = rms_forward(hidden_in, attn_gain)
    attn_rows = normed_one.astype(jnp.bfloat16)
    heads_here = w_query.shape[1] // HEAD_SIZE
    first_head = lax.axis_index("head") * heads_here
    gathered_rows = head_rows(attn_rows)
    attended, saved = attention_forward(
        gathered_rows, w_query, key_value_weight, key_cache, prefix_value_cache, cache_lengths, first_head
    )
    mixed = head_sums(jnp.dot(attended, w_output, preferred_element_type=jnp.float32))
    hidden = (hidden_in.astype(jnp.float32) + mixed).astype(jnp.bfloat16)
    normed_two, inverse_two = rms_forward(hidden, moe_gain)
    moe_rows = normed_two.astype(jnp.bfloat16)
    device_count = lax.axis_size("expert") * lax.axis_size("head")
    capacity = (owned * TOP * 4 + 3 * device_count - 1) // (3 * device_count)
    slot_total = device_count * capacity
    flat_ids = expert_ids.reshape(-1)
    one_hot = (flat_ids[:, None] == jnp.arange(device_count, dtype=jnp.int32)[None, :]).astype(
        jnp.int32
    )
    earlier = jnp.cumsum(one_hot, axis=0) - one_hot
    position = jnp.sum(earlier * one_hot, axis=1)
    target = flat_ids * capacity + position
    matched = (jnp.arange(slot_total, dtype=jnp.int32)[:, None] == target[None, :]).reshape(
        device_count, capacity, owned, TOP
    )
    placement = jnp.any(matched, axis=3).astype(jnp.bfloat16)
    weighting = jnp.sum(jnp.where(matched, gate_weights[None, None, :, :], 0.0), axis=3)
    cotangent = out_grad.astype(jnp.float32) * loss_mask.astype(jnp.float32)[:, None]
    lanes = 128
    pieces = width // lanes
    outgoing = jnp.einsum(
        "dct,tkl->dckl",
        placement,
        moe_rows.reshape(owned, pieces, lanes),
        preferred_element_type=jnp.float32,
    ).astype(jnp.bfloat16)
    grad_out = jnp.einsum(
        "dct,tkl->dckl",
        weighting,
        cotangent.reshape(owned, pieces, lanes),
        precision=highest_prec,
    ).astype(jnp.bfloat16)
    flat_shape = (device_count, capacity * pieces, lanes)
    split_shape = (device_count, capacity, pieces, lanes)
    rows_in = to_experts(outgoing.reshape(flat_shape)).reshape(split_shape)
    grads_in = to_experts(grad_out.reshape(flat_shape)).reshape(split_shape)
    gate_matrix = w_gate[0].reshape(pieces, lanes, -1)
    up_matrix = w_up[0].reshape(pieces, lanes, -1)
    down_matrix = w_down[0].reshape(-1, pieces, lanes)
    gate_pre = jnp.einsum(
        "sckl,klf->scf", rows_in, gate_matrix, preferred_element_type=jnp.float32
    )
    up_pre = jnp.einsum("sckl,klf->scf", rows_in, up_matrix, preferred_element_type=jnp.float32)
    sigma = jax.nn.sigmoid(gate_pre)
    activated = (gate_pre * sigma * up_pre).astype(jnp.bfloat16)
    result = jnp.einsum(
        "scf,fkl->sckl", activated, down_matrix, preferred_element_type=jnp.float32
    ).astype(jnp.bfloat16)
    grad_act = jnp.einsum(
        "sckl,fkl->scf", grads_in, down_matrix, preferred_element_type=jnp.float32
    )
    grad_gate = (grad_act * up_pre * sigma * (1.0 + gate_pre * (1.0 - sigma))).astype(jnp.bfloat16)
    grad_up = (grad_act * gate_pre * sigma).astype(jnp.bfloat16)
    grad_back = jnp.einsum(
        "scf,klf->sckl", grad_gate, gate_matrix, preferred_element_type=jnp.float32
    )
    grad_back = grad_back + jnp.einsum(
        "scf,klf->sckl", grad_up, up_matrix, preferred_element_type=jnp.float32
    )
    grad_back = grad_back.astype(jnp.bfloat16)
    grad_home = from_experts(grad_back.reshape(flat_shape)).reshape(split_shape)
    grad_moe = jnp.einsum(
        "dct,dckl->tkl", placement, grad_home, preferred_element_type=jnp.float32
    ).reshape(owned, width)
    grad_hidden = cotangent + rms_backward(hidden, moe_gain, inverse_two, grad_moe)
    grad_low = grad_hidden.astype(jnp.bfloat16)
    count = lax.axis_size("head")
    (result, first_hop) = after_first_hop(grad_low, result)
    grad_parts = [grad_low, first_hop] + [
        lax.ppermute(grad_low, "head", perm=[(j, (j + shift) % count) for j in range(count)])
        for shift in range(2, count)
    ]
    grad_gathered = head_order(grad_parts, 0)
    result_home = from_experts(result.reshape(flat_shape)).reshape(split_shape)
    grad_attn_rows = head_sums(
        attention_backward(
            grad_gathered,
            w_query,
            w_output,
            key_value_weight,
            saved,
            first_head // (QUERY_HEADS // KEY_VALUE_HEADS),
        )
    )
    input_grad = (
        grad_hidden + rms_backward(hidden_in, attn_gain, inverse_one, grad_attn_rows)
    ).astype(jnp.bfloat16)
    moe_sum = jnp.einsum(
        "dct,dckl->tkl",
        weighting,
        result_home.astype(jnp.float32),
        precision=highest_prec,
    ).reshape(owned, width)
    layer_out = (hidden.astype(jnp.float32) + moe_sum).astype(jnp.bfloat16)
    return (layer_out, input_grad)


def solution(mesh):
    in_specs = (
        P(("groups", "expert", "head"), None),
        P(("groups", "expert", "head"), None),
        P(("groups", "expert", "head")),
        P(("groups", "expert", "head"), None),
        P(("groups", "expert", "head"), None),
        P(("groups", "expert")),
        P(("groups", "expert"), None, None),
        P(("groups", "expert"), None, None),
        P(),
        P(),
        P(None, "head"),
        P(None, "head"),
        P("head", None),
        P(("expert", "head"), None, None),
        P(("expert", "head"), None, None),
        P(("expert", "head"), None, None),
    )
    out_specs = (P(("groups", "expert", "head"), None), P(("groups", "expert", "head"), None))
    return jax.shard_map(body, mesh=mesh, in_specs=in_specs, out_specs=out_specs, check_vma=False)
```

```python
import jax
import jax.numpy as jnp
from jax import lax
from jax.sharding import PartitionSpec as P

QUERY_HEADS = 16
KEY_VALUE_HEADS = 2
HEAD_SIZE = 128
TOP = 8
BLOCK = 16
PREFIX_SLOTS = 32


EPS = 1e-06
NEG_FILL = -1e30


def rms_forward(row_block, gain_vec):
    values = row_block.astype(jnp.float32)
    inverse = lax.rsqrt(jnp.mean(values * values, axis=-1, keepdims=True) + EPS)
    return (values * inverse * gain_vec, inverse)


def rms_backward(row_block, gain_vec, inverse, upstream):
    scaled_rows = row_block.astype(jnp.float32) * inverse
    weighted = upstream * gain_vec
    inner_mean = jnp.mean(weighted * scaled_rows, axis=-1, keepdims=True)
    return inverse * (weighted - scaled_rows * inner_mean)


def attend_forward(queries, key_rows, value_rows, usable):
    factor = queries.shape[-1] ** (-0.5)
    scores = (
        jnp.einsum("sbhd,skd->shbk", queries.astype(jnp.float32), key_rows.astype(jnp.float32))
        * factor
    )
    scores = jnp.where(usable[:, None, None, :], scores, NEG_FILL)
    highest = jnp.max(scores, axis=-1, keepdims=True)
    exponent_terms = jnp.exp(scores - highest)
    probabilities = exponent_terms / jnp.sum(exponent_terms, axis=-1, keepdims=True)
    probs_low = probabilities.astype(jnp.bfloat16)
    attended = jnp.einsum(
        "shbk,skd->sbhd", probs_low.astype(jnp.float32), value_rows.astype(jnp.float32)
    )
    return (probabilities, probs_low, attended.astype(jnp.bfloat16))


def attend_backward(queries, key_rows, value_rows, probabilities, probs_low, grad_attended):
    factor = queries.shape[-1] ** (-0.5)
    grad_probs = jnp.einsum(
        "sbhd,skd->shbk", grad_attended.astype(jnp.float32), value_rows.astype(jnp.float32)
    )
    inner_sum = jnp.sum(probabilities * grad_probs, axis=-1, keepdims=True)
    grad_scores = (probabilities * (grad_probs - inner_sum) * factor).astype(jnp.bfloat16)
    grad_queries = jnp.einsum(
        "shbk,skd->sbhd", grad_scores.astype(jnp.float32), key_rows.astype(jnp.float32)
    )
    grad_keys = jnp.einsum(
        "shbk,sbhd->skd", grad_scores.astype(jnp.float32), queries.astype(jnp.float32)
    )
    grad_values = jnp.einsum(
        "shbk,sbhd->skd", probs_low.astype(jnp.float32), grad_attended.astype(jnp.float32)
    )
    return (grad_queries.astype(jnp.bfloat16), grad_keys, grad_values)


def attention_forward(
    row_block,
    query_weights,
    own_kv_weights,
    key_cache,
    prefix_value_cache,
    lengths,
    first_head,
):
    heads_here = query_weights.shape[1] // HEAD_SIZE
    query_group_count = QUERY_HEADS // KEY_VALUE_HEADS
    row_count = row_block.shape[0]
    seq_count = row_count // BLOCK
    key_value_width = KEY_VALUE_HEADS * HEAD_SIZE
    kv_first = first_head // query_group_count
    queries = jnp.dot(row_block, query_weights, preferred_element_type=jnp.float32).astype(
        jnp.bfloat16
    )
    queries = queries.reshape(seq_count, BLOCK, heads_here, HEAD_SIZE)
    usable = jnp.concatenate(
        [
            jnp.arange(PREFIX_SLOTS)[None, :] < lengths[:, None],
            jnp.ones((seq_count, BLOCK), dtype=jnp.bool_),
        ],
        axis=1,
    )
    kv_now = kv_first + 0
    own_rows = jnp.dot(row_block, own_kv_weights, preferred_element_type=jnp.float32).astype(
        jnp.bfloat16
    )
    kv_rows = head_gather(own_rows, 1)
    pair_rows = jnp.concatenate(
        [
            lax.dynamic_slice_in_dim(kv_rows, kv_now * HEAD_SIZE, HEAD_SIZE, 1),
            lax.dynamic_slice_in_dim(kv_rows, key_value_width + kv_now * HEAD_SIZE, HEAD_SIZE, 1),
        ],
        axis=1,
    )
    key_rows = jnp.concatenate(
        [
            lax.dynamic_slice_in_dim(key_cache, kv_now * HEAD_SIZE, HEAD_SIZE, 2),
            pair_rows[:, :HEAD_SIZE].reshape(seq_count, BLOCK, HEAD_SIZE),
        ],
        axis=1,
    )
    value_rows = jnp.concatenate(
        [
            lax.dynamic_slice_in_dim(prefix_value_cache, kv_now * HEAD_SIZE, HEAD_SIZE, 2),
            pair_rows[:, HEAD_SIZE:].reshape(seq_count, BLOCK, HEAD_SIZE),
        ],
        axis=1,
    )
    probabilities, probs_low, attended = attend_forward(queries, key_rows, value_rows, usable)
    saved = [(queries, key_rows, value_rows, probabilities, probs_low)]
    joined = attended.reshape(row_count, heads_here * HEAD_SIZE)
    return (joined, saved)


def attention_backward(
    grad_rows, query_weights, output_weights, own_kv_weights, saved, kv_now, carried
):
    heads_here = query_weights.shape[1] // HEAD_SIZE
    row_count = grad_rows.shape[0]
    seq_count = row_count // BLOCK
    key_value_width = KEY_VALUE_HEADS * HEAD_SIZE
    grad_attn = jnp.einsum(
        "td,fd->tf", grad_rows, output_weights, preferred_element_type=jnp.float32
    ).astype(jnp.bfloat16)
    grad_attn = grad_attn.reshape(seq_count, BLOCK, heads_here, HEAD_SIZE)
    query_part, key_rows, value_rows, probabilities, probs_low = saved[0]
    grad_queries, grad_keys, grad_values = attend_backward(
        query_part, key_rows, value_rows, probabilities, probs_low, grad_attn
    )
    placed = jnp.zeros((row_count, 2 * key_value_width), jnp.float32)
    placed = lax.dynamic_update_slice_in_dim(
        placed, grad_keys[:, PREFIX_SLOTS:].reshape(row_count, HEAD_SIZE), kv_now * HEAD_SIZE, 1
    )
    placed = lax.dynamic_update_slice_in_dim(
        placed,
        grad_values[:, PREFIX_SLOTS:].reshape(row_count, HEAD_SIZE),
        key_value_width + kv_now * HEAD_SIZE,
        1,
    )
    placed, carried = lax.optimization_barrier((placed, carried))
    own_grads = head_sums(placed, axis=1)
    running = jnp.einsum(
        "tc,dc->td", own_grads, own_kv_weights.astype(jnp.float32), precision=lax.Precision.HIGHEST
    )
    query_flat = grad_queries.reshape(row_count, heads_here * HEAD_SIZE)
    total = running + jnp.einsum(
        "tf,df->td", query_flat, query_weights, preferred_element_type=jnp.float32
    )
    return (total, carried)


def head_gather(block, axis):
    count = lax.axis_size("head")
    me = lax.axis_index("head")
    parts = [block] + [
        lax.ppermute(block, "head", perm=[(j, (j + shift) % count) for j in range(count)])
        for shift in range(1, count)
    ]
    return head_order(parts, axis)


def head_order(parts, axis):
    count = lax.axis_size("head")
    me = lax.axis_index("head")
    block = parts[0]
    ordered = jnp.take(jnp.stack(parts), (me - jnp.arange(count)) % count, axis=0)
    ordered = jnp.moveaxis(ordered, 0, axis)
    merged = list(block.shape)
    merged[axis] = count * block.shape[axis]
    return ordered.reshape(merged)


def head_rows(row_block):
    return head_gather(row_block, 0)


def after_first_hop(block, waiting):
    count = lax.axis_size("head")
    first = lax.ppermute(block, "head", perm=[(j, (j + 1) % count) for j in range(count)])
    return lax.optimization_barrier((waiting, first))


def head_sums(partial_rows, axis=0):
    count = lax.axis_size("head")
    me = lax.axis_index("head")
    size = partial_rows.shape[axis] // count

    def chunk(index):
        return lax.dynamic_slice_in_dim(partial_rows, index * size, size, axis)

    total = chunk(me)
    for shift in range(1, count):
        total = total + lax.ppermute(
            chunk((me + shift) % count),
            "head",
            perm=[(j, (j + shift) % count) for j in range(count)],
        )
    return total


def to_experts(outgoing):
    return lax.all_to_all(outgoing, ("expert", "head"), split_axis=0, concat_axis=0, tiled=True)


def from_experts(results):
    return lax.all_to_all(results, ("expert", "head"), split_axis=0, concat_axis=0, tiled=True)


def body(
    hidden_in,
    out_grad,
    loss_mask,
    expert_ids,
    gate_weights,
    cache_lengths,
    key_cache,
    prefix_value_cache,
    attn_gain,
    moe_gain,
    w_query,
    key_value_weight,
    w_output,
    w_gate,
    w_up,
    w_down,
):
    highest_prec = lax.Precision.HIGHEST
    owned = hidden_in.shape[0]
    width = hidden_in.shape[1]
    normed_one, inverse_one = rms_forward(hidden_in, attn_gain)
    attn_rows = normed_one.astype(jnp.bfloat16)
    heads_here = w_query.shape[1] // HEAD_SIZE
    first_head = lax.axis_index("head") * heads_here
    gathered_rows = head_rows(attn_rows)
    attended, saved = attention_forward(
        gathered_rows, w_query, key_value_weight, key_cache, prefix_value_cache, cache_lengths, first_head
    )
    mixed = head_sums(jnp.dot(attended, w_output, preferred_element_type=jnp.float32))
    hidden = (hidden_in.astype(jnp.float32) + mixed).astype(jnp.bfloat16)
    normed_two, inverse_two = rms_forward(hidden, moe_gain)
    moe_rows = normed_two.astype(jnp.bfloat16)
    device_count = lax.axis_size("expert") * lax.axis_size("head")
    capacity = (owned * TOP * 4 + 3 * device_count - 1) // (3 * device_count)
    slot_total = device_count * capacity
    flat_ids = expert_ids.reshape(-1)
    one_hot = (flat_ids[:, None] == jnp.arange(device_count, dtype=jnp.int32)[None, :]).astype(
        jnp.int32
    )
    earlier = jnp.cumsum(one_hot, axis=0) - one_hot
    position = jnp.sum(earlier * one_hot, axis=1)
    target = flat_ids * capacity + position
    matched = (jnp.arange(slot_total, dtype=jnp.int32)[:, None] == target[None, :]).reshape(
        device_count, capacity, owned, TOP
    )
    placement = jnp.any(matched, axis=3).astype(jnp.bfloat16)
    weighting = jnp.sum(jnp.where(matched, gate_weights[None, None, :, :], 0.0), axis=3)
    cotangent = out_grad.astype(jnp.float32) * loss_mask.astype(jnp.float32)[:, None]
    lanes = 128
    pieces = width // lanes
    outgoing = jnp.einsum(
        "dct,tkl->dckl",
        placement,
        moe_rows.reshape(owned, pieces, lanes),
        preferred_element_type=jnp.float32,
    ).astype(jnp.bfloat16)
    grad_out = jnp.einsum(
        "dct,tkl->dckl",
        weighting,
        cotangent.reshape(owned, pieces, lanes),
        precision=highest_prec,
    ).astype(jnp.bfloat16)
    flat_shape = (device_count, capacity * pieces, lanes)
    split_shape = (device_count, capacity, pieces, lanes)
    rows_in = to_experts(outgoing.reshape(flat_shape)).reshape(split_shape)
    grads_in = to_experts(grad_out.reshape(flat_shape)).reshape(split_shape)
    gate_matrix = w_gate[0].reshape(pieces, lanes, -1)
    up_matrix = w_up[0].reshape(pieces, lanes, -1)
    down_matrix = w_down[0].reshape(-1, pieces, lanes)
    gate_pre = jnp.einsum(
        "sckl,klf->scf", rows_in, gate_matrix, preferred_element_type=jnp.float32
    )
    up_pre = jnp.einsum("sckl,klf->scf", rows_in, up_matrix, preferred_element_type=jnp.float32)
    sigma = jax.nn.sigmoid(gate_pre)
    activated = (gate_pre * sigma * up_pre).astype(jnp.bfloat16)
    result = jnp.einsum(
        "scf,fkl->sckl", activated, down_matrix, preferred_element_type=jnp.float32
    ).astype(jnp.bfloat16)
    grad_act = jnp.einsum(
        "sckl,fkl->scf", grads_in, down_matrix, preferred_element_type=jnp.float32
    )
    grad_gate = (grad_act * up_pre * sigma * (1.0 + gate_pre * (1.0 - sigma))).astype(jnp.bfloat16)
    grad_up = (grad_act * gate_pre * sigma).astype(jnp.bfloat16)
    grad_back = jnp.einsum(
        "scf,klf->sckl", grad_gate, gate_matrix, preferred_element_type=jnp.float32
    )
    grad_back = grad_back + jnp.einsum(
        "scf,klf->sckl", grad_up, up_matrix, preferred_element_type=jnp.float32
    )
    grad_back = grad_back.astype(jnp.bfloat16)
    grad_home = from_experts(grad_back.reshape(flat_shape)).reshape(split_shape)
    grad_moe = jnp.einsum(
        "dct,dckl->tkl", placement, grad_home, preferred_element_type=jnp.float32
    ).reshape(owned, width)
    grad_hidden = cotangent + rms_backward(hidden, moe_gain, inverse_two, grad_moe)
    grad_low = grad_hidden.astype(jnp.bfloat16)
    count = lax.axis_size("head")
    grad_low, result = lax.optimization_barrier((grad_low, result))
    grad_parts = [grad_low] + [
        lax.ppermute(grad_low, "head", perm=[(j, (j + shift) % count) for j in range(count)])
        for shift in range(1, count)
    ]
    result_home = from_experts(result.reshape(flat_shape)).reshape(split_shape)
    grad_parts = list(lax.optimization_barrier(tuple(grad_parts)))
    grad_gathered = head_order(grad_parts, 0)
    grad_partial, result_home = attention_backward(
        grad_gathered,
        w_query,
        w_output,
        key_value_weight,
        saved,
        first_head // (QUERY_HEADS // KEY_VALUE_HEADS),
        result_home,
    )
    grad_attn_rows = head_sums(grad_partial)
    input_grad = (
        grad_hidden + rms_backward(hidden_in, attn_gain, inverse_one, grad_attn_rows)
    ).astype(jnp.bfloat16)
    moe_sum = jnp.einsum(
        "dct,dckl->tkl",
        weighting,
        result_home.astype(jnp.float32),
        precision=highest_prec,
    ).reshape(owned, width)
    layer_out = (hidden.astype(jnp.float32) + moe_sum).astype(jnp.bfloat16)
    return (layer_out, input_grad)


def solution(mesh):
    in_specs = (
        P(("groups", "expert", "head"), None),
        P(("groups", "expert", "head"), None),
        P(("groups", "expert", "head")),
        P(("groups", "expert", "head"), None),
        P(("groups", "expert", "head"), None),
        P(("groups", "expert")),
        P(("groups", "expert"), None, None),
        P(("groups", "expert"), None, None),
        P(),
        P(),
        P(None, "head"),
        P(None, "head"),
        P("head", None),
        P(("expert", "head"), None, None),
        P(("expert", "head"), None, None),
        P(("expert", "head"), None, None),
    )
    out_specs = (P(("groups", "expert", "head"), None), P(("groups", "expert", "head"), None))
    return jax.shard_map(body, mesh=mesh, in_specs=in_specs, out_specs=out_specs, check_vma=False)
```

```python
import jax
import jax.numpy as jnp
from jax import lax
from jax.sharding import PartitionSpec as P

QUERY_HEADS = 16
KEY_VALUE_HEADS = 2
HEAD_SIZE = 128
TOP = 8
BLOCK = 16
PREFIX_SLOTS = 32


EPS = 1e-06
NEG_FILL = -1e30


def rms_forward(row_block, gain_vec):
    values = row_block.astype(jnp.float32)
    inverse = lax.rsqrt(jnp.mean(values * values, axis=-1, keepdims=True) + EPS)
    return (values * inverse * gain_vec, inverse)


def rms_backward(row_block, gain_vec, inverse, upstream):
    scaled_rows = row_block.astype(jnp.float32) * inverse
    weighted = upstream * gain_vec
    inner_mean = jnp.mean(weighted * scaled_rows, axis=-1, keepdims=True)
    return inverse * (weighted - scaled_rows * inner_mean)


def attend_forward(queries, key_rows, value_rows, usable):
    factor = queries.shape[-1] ** (-0.5)
    scores = (
        jnp.einsum("sbhd,skd->shbk", queries.astype(jnp.float32), key_rows.astype(jnp.float32))
        * factor
    )
    scores = jnp.where(usable[:, None, None, :], scores, NEG_FILL)
    highest = jnp.max(scores, axis=-1, keepdims=True)
    exponent_terms = jnp.exp(scores - highest)
    probabilities = exponent_terms / jnp.sum(exponent_terms, axis=-1, keepdims=True)
    probs_low = probabilities.astype(jnp.bfloat16)
    attended = jnp.einsum(
        "shbk,skd->sbhd", probs_low.astype(jnp.float32), value_rows.astype(jnp.float32)
    )
    return (probabilities, probs_low, attended.astype(jnp.bfloat16))


def attend_backward(queries, key_rows, value_rows, probabilities, probs_low, grad_attended):
    factor = queries.shape[-1] ** (-0.5)
    grad_probs = jnp.einsum(
        "sbhd,skd->shbk", grad_attended.astype(jnp.float32), value_rows.astype(jnp.float32)
    )
    inner_sum = jnp.sum(probabilities * grad_probs, axis=-1, keepdims=True)
    grad_scores = (probabilities * (grad_probs - inner_sum) * factor).astype(jnp.bfloat16)
    grad_queries = jnp.einsum(
        "shbk,skd->sbhd", grad_scores.astype(jnp.float32), key_rows.astype(jnp.float32)
    )
    grad_keys = jnp.einsum(
        "shbk,sbhd->skd", grad_scores.astype(jnp.float32), queries.astype(jnp.float32)
    )
    grad_values = jnp.einsum(
        "shbk,sbhd->skd", probs_low.astype(jnp.float32), grad_attended.astype(jnp.float32)
    )
    return (grad_queries.astype(jnp.bfloat16), grad_keys, grad_values)


def attention_forward(
    row_block,
    query_weights,
    own_kv_weights,
    key_cache,
    prefix_value_cache,
    lengths,
    first_head,
):
    heads_here = query_weights.shape[1] // HEAD_SIZE
    query_group_count = QUERY_HEADS // KEY_VALUE_HEADS
    row_count = row_block.shape[0]
    seq_count = row_count // BLOCK
    key_value_width = KEY_VALUE_HEADS * HEAD_SIZE
    kv_first = first_head // query_group_count
    queries = jnp.dot(row_block, query_weights, preferred_element_type=jnp.float32).astype(
        jnp.bfloat16
    )
    queries = queries.reshape(seq_count, BLOCK, heads_here, HEAD_SIZE)
    usable = jnp.concatenate(
        [
            jnp.arange(PREFIX_SLOTS)[None, :] < lengths[:, None],
            jnp.ones((seq_count, BLOCK), dtype=jnp.bool_),
        ],
        axis=1,
    )
    kv_now = kv_first + 0
    own_rows = jnp.dot(row_block, own_kv_weights, preferred_element_type=jnp.float32).astype(
        jnp.bfloat16
    )
    kv_rows = head_gather(own_rows, 1)
    pair_rows = jnp.concatenate(
        [
            lax.dynamic_slice_in_dim(kv_rows, kv_now * HEAD_SIZE, HEAD_SIZE, 1),
            lax.dynamic_slice_in_dim(kv_rows, key_value_width + kv_now * HEAD_SIZE, HEAD_SIZE, 1),
        ],
        axis=1,
    )
    key_rows = jnp.concatenate(
        [
            lax.dynamic_slice_in_dim(key_cache, kv_now * HEAD_SIZE, HEAD_SIZE, 2),
            pair_rows[:, :HEAD_SIZE].reshape(seq_count, BLOCK, HEAD_SIZE),
        ],
        axis=1,
    )
    value_rows = jnp.concatenate(
        [
            lax.dynamic_slice_in_dim(prefix_value_cache, kv_now * HEAD_SIZE, HEAD_SIZE, 2),
            pair_rows[:, HEAD_SIZE:].reshape(seq_count, BLOCK, HEAD_SIZE),
        ],
        axis=1,
    )
    probabilities, probs_low, attended = attend_forward(queries, key_rows, value_rows, usable)
    saved = [(queries, key_rows, value_rows, probabilities, probs_low)]
    joined = attended.reshape(row_count, heads_here * HEAD_SIZE)
    return (joined, saved)


def attention_backward(
    grad_rows, query_weights, output_weights, own_kv_weights, saved, kv_now, carried
):
    heads_here = query_weights.shape[1] // HEAD_SIZE
    row_count = grad_rows.shape[0]
    seq_count = row_count // BLOCK
    key_value_width = KEY_VALUE_HEADS * HEAD_SIZE
    grad_attn = jnp.einsum(
        "td,fd->tf", grad_rows, output_weights, preferred_element_type=jnp.float32
    ).astype(jnp.bfloat16)
    grad_attn = grad_attn.reshape(seq_count, BLOCK, heads_here, HEAD_SIZE)
    query_part, key_rows, value_rows, probabilities, probs_low = saved[0]
    grad_queries, grad_keys, grad_values = attend_backward(
        query_part, key_rows, value_rows, probabilities, probs_low, grad_attn
    )
    placed = jnp.zeros((row_count, 2 * key_value_width), jnp.float32)
    placed = lax.dynamic_update_slice_in_dim(
        placed, grad_keys[:, PREFIX_SLOTS:].reshape(row_count, HEAD_SIZE), kv_now * HEAD_SIZE, 1
    )
    placed = lax.dynamic_update_slice_in_dim(
        placed,
        grad_values[:, PREFIX_SLOTS:].reshape(row_count, HEAD_SIZE),
        key_value_width + kv_now * HEAD_SIZE,
        1,
    )
    placed, carried = lax.optimization_barrier((placed, carried))
    own_grads = head_sums(placed, axis=1)
    running = jnp.einsum(
        "tc,dc->td", own_grads, own_kv_weights.astype(jnp.float32), precision=lax.Precision.HIGHEST
    )
    query_flat = grad_queries.reshape(row_count, heads_here * HEAD_SIZE)
    total = running + jnp.einsum(
        "tf,df->td", query_flat, query_weights, preferred_element_type=jnp.float32
    )
    return (total, carried)


def head_gather(block, axis):
    count = lax.axis_size("head")
    me = lax.axis_index("head")
    parts = [block] + [
        lax.ppermute(block, "head", perm=[(j, (j + shift) % count) for j in range(count)])
        for shift in range(1, count)
    ]
    return head_order(parts, axis)


def head_order(parts, axis):
    count = lax.axis_size("head")
    me = lax.axis_index("head")
    block = parts[0]
    ordered = jnp.take(jnp.stack(parts), (me - jnp.arange(count)) % count, axis=0)
    ordered = jnp.moveaxis(ordered, 0, axis)
    merged = list(block.shape)
    merged[axis] = count * block.shape[axis]
    return ordered.reshape(merged)


def head_rows(row_block):
    return head_gather(row_block, 0)


def after_first_hop(block, waiting):
    count = lax.axis_size("head")
    first = lax.ppermute(block, "head", perm=[(j, (j + 1) % count) for j in range(count)])
    return lax.optimization_barrier((waiting, first))


def head_sums(partial_rows, axis=0):
    count = lax.axis_size("head")
    me = lax.axis_index("head")
    size = partial_rows.shape[axis] // count

    def chunk(index):
        return lax.dynamic_slice_in_dim(partial_rows, index * size, size, axis)

    total = chunk(me)
    for shift in range(1, count):
        total = total + lax.ppermute(
            chunk((me + shift) % count),
            "head",
            perm=[(j, (j + shift) % count) for j in range(count)],
        )
    return total


def to_experts(outgoing):
    return lax.all_to_all(outgoing, ("expert", "head"), split_axis=0, concat_axis=0, tiled=True)


def from_experts(results):
    return lax.all_to_all(results, ("expert", "head"), split_axis=0, concat_axis=0, tiled=True)


def body(
    hidden_in,
    out_grad,
    loss_mask,
    expert_ids,
    gate_weights,
    cache_lengths,
    key_cache,
    prefix_value_cache,
    attn_gain,
    moe_gain,
    w_query,
    key_value_weight,
    w_output,
    w_gate,
    w_up,
    w_down,
):
    highest_prec = lax.Precision.HIGHEST
    owned = hidden_in.shape[0]
    width = hidden_in.shape[1]
    normed_one, inverse_one = rms_forward(hidden_in, attn_gain)
    attn_rows = normed_one.astype(jnp.bfloat16)
    heads_here = w_query.shape[1] // HEAD_SIZE
    first_head = lax.axis_index("head") * heads_here
    gathered_rows = head_rows(attn_rows)
    attended, saved = attention_forward(
        gathered_rows, w_query, key_value_weight, key_cache, prefix_value_cache, cache_lengths, first_head
    )
    device_count = lax.axis_size("expert") * lax.axis_size("head")
    capacity = (owned * TOP * 4 + 3 * device_count - 1) // (3 * device_count)
    slot_total = device_count * capacity
    flat_ids = expert_ids.reshape(-1)
    one_hot = (flat_ids[:, None] == jnp.arange(device_count, dtype=jnp.int32)[None, :]).astype(
        jnp.int32
    )
    earlier = jnp.cumsum(one_hot, axis=0) - one_hot
    position = jnp.sum(earlier * one_hot, axis=1)
    target = flat_ids * capacity + position
    matched = (jnp.arange(slot_total, dtype=jnp.int32)[:, None] == target[None, :]).reshape(
        device_count, capacity, owned, TOP
    )
    placement = jnp.any(matched, axis=3).astype(jnp.bfloat16)
    weighting = jnp.sum(jnp.where(matched, gate_weights[None, None, :, :], 0.0), axis=3)
    cotangent = out_grad.astype(jnp.float32) * loss_mask.astype(jnp.float32)[:, None]
    lanes = 128
    pieces = width // lanes
    grad_out = jnp.einsum(
        "dct,tkl->dckl",
        weighting,
        cotangent.reshape(owned, pieces, lanes),
        precision=highest_prec,
    ).astype(jnp.bfloat16)
    partial_mixed = jnp.dot(attended, w_output, preferred_element_type=jnp.float32)
    partial_mixed, grad_out = lax.optimization_barrier((partial_mixed, grad_out))
    mixed = head_sums(partial_mixed)
    hidden = (hidden_in.astype(jnp.float32) + mixed).astype(jnp.bfloat16)
    normed_two, inverse_two = rms_forward(hidden, moe_gain)
    moe_rows = normed_two.astype(jnp.bfloat16)
    outgoing = jnp.einsum(
        "dct,tkl->dckl",
        placement,
        moe_rows.reshape(owned, pieces, lanes),
        preferred_element_type=jnp.float32,
    ).astype(jnp.bfloat16)
    flat_shape = (device_count, capacity * pieces, lanes)
    split_shape = (device_count, capacity, pieces, lanes)
    rows_in = to_experts(outgoing.reshape(flat_shape)).reshape(split_shape)
    grads_in = to_experts(grad_out.reshape(flat_shape)).reshape(split_shape)
    gate_matrix = w_gate[0].reshape(pieces, lanes, -1)
    up_matrix = w_up[0].reshape(pieces, lanes, -1)
    down_matrix = w_down[0].reshape(-1, pieces, lanes)
    gate_pre = jnp.einsum(
        "sckl,klf->scf", rows_in, gate_matrix, preferred_element_type=jnp.float32
    )
    up_pre = jnp.einsum("sckl,klf->scf", rows_in, up_matrix, preferred_element_type=jnp.float32)
    sigma = jax.nn.sigmoid(gate_pre)
    activated = (gate_pre * sigma * up_pre).astype(jnp.bfloat16)
    result = jnp.einsum(
        "scf,fkl->sckl", activated, down_matrix, preferred_element_type=jnp.float32
    ).astype(jnp.bfloat16)
    grad_act = jnp.einsum(
        "sckl,fkl->scf", grads_in, down_matrix, preferred_element_type=jnp.float32
    )
    grad_gate = (grad_act * up_pre * sigma * (1.0 + gate_pre * (1.0 - sigma))).astype(jnp.bfloat16)
    grad_up = (grad_act * gate_pre * sigma).astype(jnp.bfloat16)
    grad_back = jnp.einsum(
        "scf,klf->sckl", grad_gate, gate_matrix, preferred_element_type=jnp.float32
    )
    grad_back = grad_back + jnp.einsum(
        "scf,klf->sckl", grad_up, up_matrix, preferred_element_type=jnp.float32
    )
    grad_back = grad_back.astype(jnp.bfloat16)
    grad_home = from_experts(grad_back.reshape(flat_shape)).reshape(split_shape)
    grad_moe = jnp.einsum(
        "dct,dckl->tkl", placement, grad_home, preferred_element_type=jnp.float32
    ).reshape(owned, width)
    grad_hidden = cotangent + rms_backward(hidden, moe_gain, inverse_two, grad_moe)
    grad_low = grad_hidden.astype(jnp.bfloat16)
    count = lax.axis_size("head")
    grad_low, result = lax.optimization_barrier((grad_low, result))
    grad_parts = [grad_low] + [
        lax.ppermute(grad_low, "head", perm=[(j, (j + shift) % count) for j in range(count)])
        for shift in range(1, count)
    ]
    result_home = from_experts(result.reshape(flat_shape)).reshape(split_shape)
    grad_parts = list(lax.optimization_barrier(tuple(grad_parts)))
    grad_gathered = head_order(grad_parts, 0)
    grad_partial, result_home = attention_backward(
        grad_gathered,
        w_query,
        w_output,
        key_value_weight,
        saved,
        first_head // (QUERY_HEADS // KEY_VALUE_HEADS),
        result_home,
    )
    grad_attn_rows = head_sums(grad_partial)
    input_grad = (
        grad_hidden + rms_backward(hidden_in, attn_gain, inverse_one, grad_attn_rows)
    ).astype(jnp.bfloat16)
    moe_sum = jnp.einsum(
        "dct,dckl->tkl",
        weighting,
        result_home.astype(jnp.float32),
        precision=highest_prec,
    ).reshape(owned, width)
    layer_out = (hidden.astype(jnp.float32) + moe_sum).astype(jnp.bfloat16)
    return (layer_out, input_grad)


def solution(mesh):
    in_specs = (
        P(("groups", "expert", "head"), None),
        P(("groups", "expert", "head"), None),
        P(("groups", "expert", "head")),
        P(("groups", "expert", "head"), None),
        P(("groups", "expert", "head"), None),
        P(("groups", "expert")),
        P(("groups", "expert"), None, None),
        P(("groups", "expert"), None, None),
        P(),
        P(),
        P(None, "head"),
        P(None, "head"),
        P("head", None),
        P(("expert", "head"), None, None),
        P(("expert", "head"), None, None),
        P(("expert", "head"), None, None),
    )
    out_specs = (P(("groups", "expert", "head"), None), P(("groups", "expert", "head"), None))
    return jax.shard_map(body, mesh=mesh, in_specs=in_specs, out_specs=out_specs, check_vma=False)
```

```python
import jax
import jax.numpy as jnp
from jax import lax
from jax.sharding import PartitionSpec as P

QUERY_HEADS = 16
KEY_VALUE_HEADS = 2
HEAD_SIZE = 128
TOP = 8
BLOCK = 16
PREFIX_SLOTS = 32


EPS = 1e-06
NEG_FILL = -1e30


def rms_forward(row_block, gain_vec):
    values = row_block.astype(jnp.float32)
    inverse = lax.rsqrt(jnp.mean(values * values, axis=-1, keepdims=True) + EPS)
    return (values * inverse * gain_vec, inverse)


def rms_backward(row_block, gain_vec, inverse, upstream):
    scaled_rows = row_block.astype(jnp.float32) * inverse
    weighted = upstream * gain_vec
    inner_mean = jnp.mean(weighted * scaled_rows, axis=-1, keepdims=True)
    return inverse * (weighted - scaled_rows * inner_mean)


def attend_forward(queries, key_rows, value_rows, usable):
    factor = queries.shape[-1] ** (-0.5)
    scores = (
        jnp.einsum("sbhd,skd->shbk", queries.astype(jnp.float32), key_rows.astype(jnp.float32))
        * factor
    )
    scores = jnp.where(usable[:, None, None, :], scores, NEG_FILL)
    highest = jnp.max(scores, axis=-1, keepdims=True)
    exponent_terms = jnp.exp(scores - highest)
    probabilities = exponent_terms / jnp.sum(exponent_terms, axis=-1, keepdims=True)
    probs_low = probabilities.astype(jnp.bfloat16)
    attended = jnp.einsum(
        "shbk,skd->sbhd", probs_low.astype(jnp.float32), value_rows.astype(jnp.float32)
    )
    return (probabilities, probs_low, attended.astype(jnp.bfloat16))


def attend_backward(queries, key_rows, value_rows, probabilities, probs_low, grad_attended):
    factor = queries.shape[-1] ** (-0.5)
    grad_probs = jnp.einsum(
        "sbhd,skd->shbk", grad_attended.astype(jnp.float32), value_rows.astype(jnp.float32)
    )
    inner_sum = jnp.sum(probabilities * grad_probs, axis=-1, keepdims=True)
    grad_scores = (probabilities * (grad_probs - inner_sum) * factor).astype(jnp.bfloat16)
    grad_queries = jnp.einsum(
        "shbk,skd->sbhd", grad_scores.astype(jnp.float32), key_rows.astype(jnp.float32)
    )
    grad_keys = jnp.einsum(
        "shbk,sbhd->skd", grad_scores.astype(jnp.float32), queries.astype(jnp.float32)
    )
    grad_values = jnp.einsum(
        "shbk,sbhd->skd", probs_low.astype(jnp.float32), grad_attended.astype(jnp.float32)
    )
    return (grad_queries.astype(jnp.bfloat16), grad_keys, grad_values)


def attention_forward(
    row_block,
    query_weights,
    own_kv_weights,
    key_cache,
    prefix_value_cache,
    lengths,
    first_head,
):
    heads_here = query_weights.shape[1] // HEAD_SIZE
    query_group_count = QUERY_HEADS // KEY_VALUE_HEADS
    row_count = row_block.shape[0]
    seq_count = row_count // BLOCK
    key_value_width = KEY_VALUE_HEADS * HEAD_SIZE
    kv_first = first_head // query_group_count
    queries = jnp.dot(row_block, query_weights, preferred_element_type=jnp.float32).astype(
        jnp.bfloat16
    )
    queries = queries.reshape(seq_count, BLOCK, heads_here, HEAD_SIZE)
    usable = jnp.concatenate(
        [
            jnp.arange(PREFIX_SLOTS)[None, :] < lengths[:, None],
            jnp.ones((seq_count, BLOCK), dtype=jnp.bool_),
        ],
        axis=1,
    )
    kv_now = kv_first + 0
    own_rows = jnp.dot(row_block, own_kv_weights, preferred_element_type=jnp.float32).astype(
        jnp.bfloat16
    )
    kv_rows = head_gather(own_rows, 1)
    pair_rows = jnp.concatenate(
        [
            lax.dynamic_slice_in_dim(kv_rows, kv_now * HEAD_SIZE, HEAD_SIZE, 1),
            lax.dynamic_slice_in_dim(kv_rows, key_value_width + kv_now * HEAD_SIZE, HEAD_SIZE, 1),
        ],
        axis=1,
    )
    key_rows = jnp.concatenate(
        [
            lax.dynamic_slice_in_dim(key_cache, kv_now * HEAD_SIZE, HEAD_SIZE, 2),
            pair_rows[:, :HEAD_SIZE].reshape(seq_count, BLOCK, HEAD_SIZE),
        ],
        axis=1,
    )
    value_rows = jnp.concatenate(
        [
            lax.dynamic_slice_in_dim(prefix_value_cache, kv_now * HEAD_SIZE, HEAD_SIZE, 2),
            pair_rows[:, HEAD_SIZE:].reshape(seq_count, BLOCK, HEAD_SIZE),
        ],
        axis=1,
    )
    probabilities, probs_low, attended = attend_forward(queries, key_rows, value_rows, usable)
    saved = [(queries, key_rows, value_rows, probabilities, probs_low)]
    joined = attended.reshape(row_count, heads_here * HEAD_SIZE)
    return (joined, saved)


def attention_backward(
    grad_rows, query_weights, output_weights, own_kv_weights, saved, kv_now, carried
):
    heads_here = query_weights.shape[1] // HEAD_SIZE
    row_count = grad_rows.shape[0]
    seq_count = row_count // BLOCK
    key_value_width = KEY_VALUE_HEADS * HEAD_SIZE
    grad_attn = jnp.einsum(
        "td,fd->tf", grad_rows, output_weights, preferred_element_type=jnp.float32
    ).astype(jnp.bfloat16)
    grad_attn = grad_attn.reshape(seq_count, BLOCK, heads_here, HEAD_SIZE)
    query_part, key_rows, value_rows, probabilities, probs_low = saved[0]
    grad_queries, grad_keys, grad_values = attend_backward(
        query_part, key_rows, value_rows, probabilities, probs_low, grad_attn
    )
    placed = jnp.zeros((row_count, 2 * key_value_width), jnp.float32)
    placed = lax.dynamic_update_slice_in_dim(
        placed, grad_keys[:, PREFIX_SLOTS:].reshape(row_count, HEAD_SIZE), kv_now * HEAD_SIZE, 1
    )
    placed = lax.dynamic_update_slice_in_dim(
        placed,
        grad_values[:, PREFIX_SLOTS:].reshape(row_count, HEAD_SIZE),
        key_value_width + kv_now * HEAD_SIZE,
        1,
    )
    placed, carried = lax.optimization_barrier((placed, carried))
    own_grads = head_sums(placed, axis=1)
    running = jnp.einsum(
        "tc,dc->td", own_grads, own_kv_weights.astype(jnp.float32), precision=lax.Precision.HIGHEST
    )
    query_flat = grad_queries.reshape(row_count, heads_here * HEAD_SIZE)
    total = running + jnp.einsum(
        "tf,df->td", query_flat, query_weights, preferred_element_type=jnp.float32
    )
    return (total, carried)


def head_gather(block, axis):
    count = lax.axis_size("head")
    me = lax.axis_index("head")
    parts = [block] + [
        lax.ppermute(block, "head", perm=[(j, (j + shift) % count) for j in range(count)])
        for shift in range(1, count)
    ]
    return head_order(parts, axis)


def head_order(parts, axis):
    count = lax.axis_size("head")
    me = lax.axis_index("head")
    block = parts[0]
    ordered = jnp.take(jnp.stack(parts), (me - jnp.arange(count)) % count, axis=0)
    ordered = jnp.moveaxis(ordered, 0, axis)
    merged = list(block.shape)
    merged[axis] = count * block.shape[axis]
    return ordered.reshape(merged)


def head_rows(row_block):
    return head_gather(row_block, 0)


def after_first_hop(block, waiting):
    count = lax.axis_size("head")
    first = lax.ppermute(block, "head", perm=[(j, (j + 1) % count) for j in range(count)])
    return lax.optimization_barrier((waiting, first))


def head_sums(partial_rows, axis=0):
    count = lax.axis_size("head")
    me = lax.axis_index("head")
    size = partial_rows.shape[axis] // count

    def chunk(index):
        return lax.dynamic_slice_in_dim(partial_rows, index * size, size, axis)

    total = chunk(me)
    for shift in range(1, count):
        total = total + lax.ppermute(
            chunk((me + shift) % count),
            "head",
            perm=[(j, (j + shift) % count) for j in range(count)],
        )
    return total


def to_experts(outgoing):
    return lax.all_to_all(outgoing, ("expert", "head"), split_axis=0, concat_axis=0, tiled=True)


def from_experts(results):
    return lax.all_to_all(results, ("expert", "head"), split_axis=0, concat_axis=0, tiled=True)


def body(
    hidden_in,
    out_grad,
    loss_mask,
    expert_ids,
    gate_weights,
    cache_lengths,
    key_cache,
    prefix_value_cache,
    attn_gain,
    moe_gain,
    w_query,
    key_value_weight,
    w_output,
    w_gate,
    w_up,
    w_down,
):
    highest_prec = lax.Precision.HIGHEST
    owned = hidden_in.shape[0]
    width = hidden_in.shape[1]
    normed_one, inverse_one = rms_forward(hidden_in, attn_gain)
    attn_rows = normed_one.astype(jnp.bfloat16)
    heads_here = w_query.shape[1] // HEAD_SIZE
    first_head = lax.axis_index("head") * heads_here
    gathered_rows = head_rows(attn_rows)
    attended, saved = attention_forward(
        gathered_rows, w_query, key_value_weight, key_cache, prefix_value_cache, cache_lengths, first_head
    )
    mixed = head_sums(jnp.dot(attended, w_output, preferred_element_type=jnp.float32))
    hidden = (hidden_in.astype(jnp.float32) + mixed).astype(jnp.bfloat16)
    normed_two, inverse_two = rms_forward(hidden, moe_gain)
    moe_rows = normed_two.astype(jnp.bfloat16)
    device_count = lax.axis_size("expert") * lax.axis_size("head")
    capacity = (owned * TOP * 4 + 3 * device_count - 1) // (3 * device_count)
    slot_total = device_count * capacity
    flat_ids = expert_ids.reshape(-1)
    one_hot = (flat_ids[:, None] == jnp.arange(device_count, dtype=jnp.int32)[None, :]).astype(
        jnp.int32
    )
    earlier = jnp.cumsum(one_hot, axis=0) - one_hot
    position = jnp.sum(earlier * one_hot, axis=1)
    target = flat_ids * capacity + position
    matched = (jnp.arange(slot_total, dtype=jnp.int32)[:, None] == target[None, :]).reshape(
        device_count, capacity, owned, TOP
    )
    placement = jnp.any(matched, axis=3).astype(jnp.bfloat16)
    weighting = jnp.sum(jnp.where(matched, gate_weights[None, None, :, :], 0.0), axis=3)
    cotangent = out_grad.astype(jnp.float32) * loss_mask.astype(jnp.float32)[:, None]
    lanes = 128
    pieces = width // lanes
    outgoing = jnp.einsum(
        "dct,tkl->dckl",
        placement,
        moe_rows.reshape(owned, pieces, lanes),
        preferred_element_type=jnp.float32,
    ).astype(jnp.bfloat16)
    grad_out = jnp.einsum(
        "dct,tkl->dckl",
        weighting,
        cotangent.reshape(owned, pieces, lanes),
        precision=highest_prec,
    ).astype(jnp.bfloat16)
    flat_shape = (device_count, capacity * pieces, lanes)
    split_shape = (device_count, capacity, pieces, lanes)
    rows_in = to_experts(outgoing.reshape(flat_shape)).reshape(split_shape)
    grads_in = to_experts(grad_out.reshape(flat_shape)).reshape(split_shape)
    gate_matrix = w_gate[0].reshape(pieces, lanes, -1)
    up_matrix = w_up[0].reshape(pieces, lanes, -1)
    down_matrix = w_down[0].reshape(-1, pieces, lanes)
    gate_pre = jnp.einsum(
        "sckl,klf->scf", rows_in, gate_matrix, preferred_element_type=jnp.float32
    )
    up_pre = jnp.einsum("sckl,klf->scf", rows_in, up_matrix, preferred_element_type=jnp.float32)
    sigma = jax.nn.sigmoid(gate_pre)
    activated = (gate_pre * sigma * up_pre).astype(jnp.bfloat16)
    result = jnp.einsum(
        "scf,fkl->sckl", activated, down_matrix, preferred_element_type=jnp.float32
    ).astype(jnp.bfloat16)
    grad_act = jnp.einsum(
        "sckl,fkl->scf", grads_in, down_matrix, preferred_element_type=jnp.float32
    )
    grad_gate = (grad_act * up_pre * sigma * (1.0 + gate_pre * (1.0 - sigma))).astype(jnp.bfloat16)
    grad_up = (grad_act * gate_pre * sigma).astype(jnp.bfloat16)
    grad_back = jnp.einsum(
        "scf,klf->sckl", grad_gate, gate_matrix, preferred_element_type=jnp.float32
    )
    grad_back = grad_back + jnp.einsum(
        "scf,klf->sckl", grad_up, up_matrix, preferred_element_type=jnp.float32
    )
    grad_back = grad_back.astype(jnp.bfloat16)
    grad_home = from_experts(grad_back.reshape(flat_shape)).reshape(split_shape)
    slots = target.reshape(owned, TOP)
    grad_picked = jnp.take(grad_home.reshape(slot_total, pieces, lanes), slots, axis=0)
    grad_moe = jnp.sum(grad_picked.astype(jnp.float32), axis=1).reshape(owned, width)
    grad_hidden = cotangent + rms_backward(hidden, moe_gain, inverse_two, grad_moe)
    grad_low = grad_hidden.astype(jnp.bfloat16)
    count = lax.axis_size("head")
    grad_low, result = lax.optimization_barrier((grad_low, result))
    grad_parts = [grad_low] + [
        lax.ppermute(grad_low, "head", perm=[(j, (j + shift) % count) for j in range(count)])
        for shift in range(1, count)
    ]
    result_home = from_experts(result.reshape(flat_shape)).reshape(split_shape)
    grad_parts = list(lax.optimization_barrier(tuple(grad_parts)))
    grad_gathered = head_order(grad_parts, 0)
    grad_partial, result_home = attention_backward(
        grad_gathered,
        w_query,
        w_output,
        key_value_weight,
        saved,
        first_head // (QUERY_HEADS // KEY_VALUE_HEADS),
        result_home,
    )
    grad_attn_rows = head_sums(grad_partial)
    input_grad = (
        grad_hidden + rms_backward(hidden_in, attn_gain, inverse_one, grad_attn_rows)
    ).astype(jnp.bfloat16)
    result_picked = jnp.take(result_home.reshape(slot_total, pieces, lanes), slots, axis=0)
    moe_sum = jnp.sum(
        gate_weights[:, :, None, None] * result_picked.astype(jnp.float32), axis=1
    ).reshape(owned, width)
    layer_out = (hidden.astype(jnp.float32) + moe_sum).astype(jnp.bfloat16)
    return (layer_out, input_grad)


def solution(mesh):
    in_specs = (
        P(("groups", "expert", "head"), None),
        P(("groups", "expert", "head"), None),
        P(("groups", "expert", "head")),
        P(("groups", "expert", "head"), None),
        P(("groups", "expert", "head"), None),
        P(("groups", "expert")),
        P(("groups", "expert"), None, None),
        P(("groups", "expert"), None, None),
        P(),
        P(),
        P(None, "head"),
        P(None, "head"),
        P("head", None),
        P(("expert", "head"), None, None),
        P(("expert", "head"), None, None),
        P(("expert", "head"), None, None),
    )
    out_specs = (P(("groups", "expert", "head"), None), P(("groups", "expert", "head"), None))
    return jax.shard_map(body, mesh=mesh, in_specs=in_specs, out_specs=out_specs, check_vma=False)
```

```python
import jax
import jax.numpy as jnp
from jax import lax
from jax.sharding import PartitionSpec as P

QUERY_HEADS = 16
KEY_VALUE_HEADS = 2
HEAD_SIZE = 128
TOP = 8
BLOCK = 16
PREFIX_SLOTS = 32


EPS = 1e-06
NEG_FILL = -1e30


def rms_forward(row_block, gain_vec):
    values = row_block.astype(jnp.float32)
    inverse = lax.rsqrt(jnp.mean(values * values, axis=-1, keepdims=True) + EPS)
    return (values * inverse * gain_vec, inverse)


def rms_backward(row_block, gain_vec, inverse, upstream):
    scaled_rows = row_block.astype(jnp.float32) * inverse
    weighted = upstream * gain_vec
    inner_mean = jnp.mean(weighted * scaled_rows, axis=-1, keepdims=True)
    return inverse * (weighted - scaled_rows * inner_mean)


def attend_forward(queries, key_rows, value_rows, usable):
    factor = queries.shape[-1] ** (-0.5)
    scores = (
        jnp.einsum("sbhd,skd->shbk", queries.astype(jnp.float32), key_rows.astype(jnp.float32))
        * factor
    )
    scores = jnp.where(usable[:, None, None, :], scores, NEG_FILL)
    highest = jnp.max(scores, axis=-1, keepdims=True)
    exponent_terms = jnp.exp(scores - highest)
    probabilities = exponent_terms / jnp.sum(exponent_terms, axis=-1, keepdims=True)
    probs_low = probabilities.astype(jnp.bfloat16)
    attended = jnp.einsum(
        "shbk,skd->sbhd", probs_low.astype(jnp.float32), value_rows.astype(jnp.float32)
    )
    return (probabilities, probs_low, attended.astype(jnp.bfloat16))


def attend_backward(queries, key_rows, value_rows, probabilities, probs_low, grad_attended):
    factor = queries.shape[-1] ** (-0.5)
    grad_probs = jnp.einsum(
        "sbhd,skd->shbk", grad_attended.astype(jnp.float32), value_rows.astype(jnp.float32)
    )
    inner_sum = jnp.sum(probabilities * grad_probs, axis=-1, keepdims=True)
    grad_scores = (probabilities * (grad_probs - inner_sum) * factor).astype(jnp.bfloat16)
    grad_queries = jnp.einsum(
        "shbk,skd->sbhd", grad_scores.astype(jnp.float32), key_rows.astype(jnp.float32)
    )
    grad_keys = jnp.einsum(
        "shbk,sbhd->skd", grad_scores.astype(jnp.float32), queries.astype(jnp.float32)
    )
    grad_values = jnp.einsum(
        "shbk,sbhd->skd", probs_low.astype(jnp.float32), grad_attended.astype(jnp.float32)
    )
    return (grad_queries.astype(jnp.bfloat16), grad_keys, grad_values)


def attention_forward(
    row_block,
    query_weights,
    own_kv_weights,
    key_cache,
    prefix_value_cache,
    lengths,
    first_head,
):
    heads_here = query_weights.shape[1] // HEAD_SIZE
    query_group_count = QUERY_HEADS // KEY_VALUE_HEADS
    row_count = row_block.shape[0]
    seq_count = row_count // BLOCK
    key_value_width = KEY_VALUE_HEADS * HEAD_SIZE
    kv_first = first_head // query_group_count
    queries = jnp.dot(row_block, query_weights, preferred_element_type=jnp.float32).astype(
        jnp.bfloat16
    )
    queries = queries.reshape(seq_count, BLOCK, heads_here, HEAD_SIZE)
    usable = jnp.concatenate(
        [
            jnp.arange(PREFIX_SLOTS)[None, :] < lengths[:, None],
            jnp.ones((seq_count, BLOCK), dtype=jnp.bool_),
        ],
        axis=1,
    )
    kv_now = kv_first + 0
    own_rows = jnp.dot(row_block, own_kv_weights, preferred_element_type=jnp.float32).astype(
        jnp.bfloat16
    )
    kv_rows = head_gather(own_rows, 1)
    pair_rows = jnp.concatenate(
        [
            lax.dynamic_slice_in_dim(kv_rows, kv_now * HEAD_SIZE, HEAD_SIZE, 1),
            lax.dynamic_slice_in_dim(kv_rows, key_value_width + kv_now * HEAD_SIZE, HEAD_SIZE, 1),
        ],
        axis=1,
    )
    key_rows = jnp.concatenate(
        [
            lax.dynamic_slice_in_dim(key_cache, kv_now * HEAD_SIZE, HEAD_SIZE, 2),
            pair_rows[:, :HEAD_SIZE].reshape(seq_count, BLOCK, HEAD_SIZE),
        ],
        axis=1,
    )
    value_rows = jnp.concatenate(
        [
            lax.dynamic_slice_in_dim(prefix_value_cache, kv_now * HEAD_SIZE, HEAD_SIZE, 2),
            pair_rows[:, HEAD_SIZE:].reshape(seq_count, BLOCK, HEAD_SIZE),
        ],
        axis=1,
    )
    probabilities, probs_low, attended = attend_forward(queries, key_rows, value_rows, usable)
    saved = [(queries, key_rows, value_rows, probabilities, probs_low)]
    joined = attended.reshape(row_count, heads_here * HEAD_SIZE)
    return (joined, saved)


def attention_backward(
    grad_rows, query_weights, output_weights, own_kv_weights, saved, kv_now, carried
):
    heads_here = query_weights.shape[1] // HEAD_SIZE
    row_count = grad_rows.shape[0]
    seq_count = row_count // BLOCK
    key_value_width = KEY_VALUE_HEADS * HEAD_SIZE
    grad_attn = jnp.einsum(
        "td,fd->tf", grad_rows, output_weights, preferred_element_type=jnp.float32
    ).astype(jnp.bfloat16)
    grad_attn = grad_attn.reshape(seq_count, BLOCK, heads_here, HEAD_SIZE)
    query_part, key_rows, value_rows, probabilities, probs_low = saved[0]
    grad_queries, grad_keys, grad_values = attend_backward(
        query_part, key_rows, value_rows, probabilities, probs_low, grad_attn
    )
    placed = jnp.zeros((row_count, 2 * key_value_width), jnp.float32)
    placed = lax.dynamic_update_slice_in_dim(
        placed, grad_keys[:, PREFIX_SLOTS:].reshape(row_count, HEAD_SIZE), kv_now * HEAD_SIZE, 1
    )
    placed = lax.dynamic_update_slice_in_dim(
        placed,
        grad_values[:, PREFIX_SLOTS:].reshape(row_count, HEAD_SIZE),
        key_value_width + kv_now * HEAD_SIZE,
        1,
    )
    placed, carried = lax.optimization_barrier((placed, carried))
    own_grads = head_sums(placed, axis=1)
    running = jnp.einsum(
        "tc,dc->td", own_grads, own_kv_weights.astype(jnp.float32), precision=lax.Precision.HIGHEST
    )
    query_flat = grad_queries.reshape(row_count, heads_here * HEAD_SIZE)
    total = running + jnp.einsum(
        "tf,df->td", query_flat, query_weights, preferred_element_type=jnp.float32
    )
    return (total, carried)


def head_gather(block, axis):
    count = lax.axis_size("head")
    me = lax.axis_index("head")
    parts = [block] + [
        lax.ppermute(block, "head", perm=[(j, (j + shift) % count) for j in range(count)])
        for shift in range(1, count)
    ]
    return head_order(parts, axis)


def head_order(parts, axis):
    count = lax.axis_size("head")
    me = lax.axis_index("head")
    block = parts[0]
    slots = []
    for slot in range(count):
        source_shift = (me - slot) % count
        chosen = parts[0]
        for shift in range(1, count):
            chosen = jnp.where(source_shift == shift, parts[shift], chosen)
        slots.append(chosen)
    ordered = jnp.stack(slots)
    ordered = jnp.moveaxis(ordered, 0, axis)
    merged = list(block.shape)
    merged[axis] = count * block.shape[axis]
    return ordered.reshape(merged)


def head_rows(row_block):
    return head_gather(row_block, 0)


def after_first_hop(block, waiting):
    count = lax.axis_size("head")
    first = lax.ppermute(block, "head", perm=[(j, (j + 1) % count) for j in range(count)])
    return lax.optimization_barrier((waiting, first))


def head_sums(partial_rows, axis=0):
    count = lax.axis_size("head")
    me = lax.axis_index("head")
    size = partial_rows.shape[axis] // count

    def chunk(index):
        return lax.dynamic_slice_in_dim(partial_rows, index * size, size, axis)

    total = chunk(me)
    for shift in range(1, count):
        total = total + lax.ppermute(
            chunk((me + shift) % count),
            "head",
            perm=[(j, (j + shift) % count) for j in range(count)],
        )
    return total


def to_experts(outgoing):
    return lax.all_to_all(outgoing, ("expert", "head"), split_axis=0, concat_axis=0, tiled=True)


def from_experts(results):
    return lax.all_to_all(results, ("expert", "head"), split_axis=0, concat_axis=0, tiled=True)


def body(
    hidden_in,
    out_grad,
    loss_mask,
    expert_ids,
    gate_weights,
    cache_lengths,
    key_cache,
    prefix_value_cache,
    attn_gain,
    moe_gain,
    w_query,
    key_value_weight,
    w_output,
    w_gate,
    w_up,
    w_down,
):
    highest_prec = lax.Precision.HIGHEST
    owned = hidden_in.shape[0]
    width = hidden_in.shape[1]
    normed_one, inverse_one = rms_forward(hidden_in, attn_gain)
    attn_rows = normed_one.astype(jnp.bfloat16)
    heads_here = w_query.shape[1] // HEAD_SIZE
    first_head = lax.axis_index("head") * heads_here
    gathered_rows = head_rows(attn_rows)
    attended, saved = attention_forward(
        gathered_rows, w_query, key_value_weight, key_cache, prefix_value_cache, cache_lengths, first_head
    )
    mixed = head_sums(jnp.dot(attended, w_output, preferred_element_type=jnp.float32))
    hidden = (hidden_in.astype(jnp.float32) + mixed).astype(jnp.bfloat16)
    normed_two, inverse_two = rms_forward(hidden, moe_gain)
    moe_rows = normed_two.astype(jnp.bfloat16)
    device_count = lax.axis_size("expert") * lax.axis_size("head")
    capacity = (owned * TOP * 4 + 3 * device_count - 1) // (3 * device_count)
    slot_total = device_count * capacity
    flat_ids = expert_ids.reshape(-1)
    one_hot = (flat_ids[:, None] == jnp.arange(device_count, dtype=jnp.int32)[None, :]).astype(
        jnp.int32
    )
    earlier = jnp.cumsum(one_hot, axis=0) - one_hot
    position = jnp.sum(earlier * one_hot, axis=1)
    target = flat_ids * capacity + position
    matched = (jnp.arange(slot_total, dtype=jnp.int32)[:, None] == target[None, :]).reshape(
        device_count, capacity, owned, TOP
    )
    placement = jnp.any(matched, axis=3).astype(jnp.bfloat16)
    weighting = jnp.sum(jnp.where(matched, gate_weights[None, None, :, :], 0.0), axis=3)
    cotangent = out_grad.astype(jnp.float32) * loss_mask.astype(jnp.float32)[:, None]
    lanes = 128
    pieces = width // lanes
    outgoing = jnp.einsum(
        "dct,tkl->dckl",
        placement,
        moe_rows.reshape(owned, pieces, lanes),
        preferred_element_type=jnp.float32,
    ).astype(jnp.bfloat16)
    grad_out = jnp.einsum(
        "dct,tkl->dckl",
        weighting,
        cotangent.reshape(owned, pieces, lanes),
        precision=highest_prec,
    ).astype(jnp.bfloat16)
    flat_shape = (device_count, capacity * pieces, lanes)
    split_shape = (device_count, capacity, pieces, lanes)
    rows_in = to_experts(outgoing.reshape(flat_shape)).reshape(split_shape)
    grads_in = to_experts(grad_out.reshape(flat_shape)).reshape(split_shape)
    gate_matrix = w_gate[0].reshape(pieces, lanes, -1)
    up_matrix = w_up[0].reshape(pieces, lanes, -1)
    down_matrix = w_down[0].reshape(-1, pieces, lanes)
    gate_pre = jnp.einsum(
        "sckl,klf->scf", rows_in, gate_matrix, preferred_element_type=jnp.float32
    )
    up_pre = jnp.einsum("sckl,klf->scf", rows_in, up_matrix, preferred_element_type=jnp.float32)
    sigma = jax.nn.sigmoid(gate_pre)
    activated = (gate_pre * sigma * up_pre).astype(jnp.bfloat16)
    result = jnp.einsum(
        "scf,fkl->sckl", activated, down_matrix, preferred_element_type=jnp.float32
    ).astype(jnp.bfloat16)
    grad_act = jnp.einsum(
        "sckl,fkl->scf", grads_in, down_matrix, preferred_element_type=jnp.float32
    )
    grad_gate = (grad_act * up_pre * sigma * (1.0 + gate_pre * (1.0 - sigma))).astype(jnp.bfloat16)
    grad_up = (grad_act * gate_pre * sigma).astype(jnp.bfloat16)
    grad_back = jnp.einsum(
        "scf,klf->sckl", grad_gate, gate_matrix, preferred_element_type=jnp.float32
    )
    grad_back = grad_back + jnp.einsum(
        "scf,klf->sckl", grad_up, up_matrix, preferred_element_type=jnp.float32
    )
    grad_back = grad_back.astype(jnp.bfloat16)
    grad_home = from_experts(grad_back.reshape(flat_shape)).reshape(split_shape)
    grad_moe = jnp.einsum(
        "dct,dckl->tkl", placement, grad_home, preferred_element_type=jnp.float32
    ).reshape(owned, width)
    grad_hidden = cotangent + rms_backward(hidden, moe_gain, inverse_two, grad_moe)
    grad_low = grad_hidden.astype(jnp.bfloat16)
    count = lax.axis_size("head")
    grad_low, result = lax.optimization_barrier((grad_low, result))
    grad_parts = [grad_low] + [
        lax.ppermute(grad_low, "head", perm=[(j, (j + shift) % count) for j in range(count)])
        for shift in range(1, count)
    ]
    result_home = from_experts(result.reshape(flat_shape)).reshape(split_shape)
    grad_parts = list(lax.optimization_barrier(tuple(grad_parts)))
    grad_gathered = head_order(grad_parts, 0)
    grad_partial, result_home = attention_backward(
        grad_gathered,
        w_query,
        w_output,
        key_value_weight,
        saved,
        first_head // (QUERY_HEADS // KEY_VALUE_HEADS),
        result_home,
    )
    grad_attn_rows = head_sums(grad_partial)
    input_grad = (
        grad_hidden + rms_backward(hidden_in, attn_gain, inverse_one, grad_attn_rows)
    ).astype(jnp.bfloat16)
    moe_sum = jnp.einsum(
        "dct,dckl->tkl",
        weighting,
        result_home.astype(jnp.float32),
        precision=highest_prec,
    ).reshape(owned, width)
    layer_out = (hidden.astype(jnp.float32) + moe_sum).astype(jnp.bfloat16)
    return (layer_out, input_grad)


def solution(mesh):
    in_specs = (
        P(("groups", "expert", "head"), None),
        P(("groups", "expert", "head"), None),
        P(("groups", "expert", "head")),
        P(("groups", "expert", "head"), None),
        P(("groups", "expert", "head"), None),
        P(("groups", "expert")),
        P(("groups", "expert"), None, None),
        P(("groups", "expert"), None, None),
        P(),
        P(),
        P(None, "head"),
        P(None, "head"),
        P("head", None),
        P(("expert", "head"), None, None),
        P(("expert", "head"), None, None),
        P(("expert", "head"), None, None),
    )
    out_specs = (P(("groups", "expert", "head"), None), P(("groups", "expert", "head"), None))
    return jax.shard_map(body, mesh=mesh, in_specs=in_specs, out_specs=out_specs, check_vma=False)
```

```python
import jax
import jax.numpy as jnp
from jax import lax
from jax.sharding import PartitionSpec as P

QUERY_HEADS = 16
KEY_VALUE_HEADS = 2
HEAD_SIZE = 128
TOP = 8
BLOCK = 16
PREFIX_SLOTS = 32


EPS = 1e-06
NEG_FILL = -1e30


def rms_forward(row_block, gain_vec):
    values = row_block.astype(jnp.float32)
    inverse = lax.rsqrt(jnp.mean(values * values, axis=-1, keepdims=True) + EPS)
    return (values * inverse * gain_vec, inverse)


def rms_backward(row_block, gain_vec, inverse, upstream):
    scaled_rows = row_block.astype(jnp.float32) * inverse
    weighted = upstream * gain_vec
    inner_mean = jnp.mean(weighted * scaled_rows, axis=-1, keepdims=True)
    return inverse * (weighted - scaled_rows * inner_mean)


def attend_forward(queries, key_rows, value_rows, usable):
    factor = queries.shape[-1] ** (-0.5)
    scores = (
        jnp.einsum("sbhd,skd->shbk", queries.astype(jnp.float32), key_rows.astype(jnp.float32))
        * factor
    )
    scores = jnp.where(usable[:, None, None, :], scores, NEG_FILL)
    highest = jnp.max(scores, axis=-1, keepdims=True)
    exponent_terms = jnp.exp(scores - highest)
    probabilities = exponent_terms / jnp.sum(exponent_terms, axis=-1, keepdims=True)
    probs_low = probabilities.astype(jnp.bfloat16)
    attended = jnp.einsum(
        "shbk,skd->sbhd", probs_low.astype(jnp.float32), value_rows.astype(jnp.float32)
    )
    return (probabilities, probs_low, attended.astype(jnp.bfloat16))


def attend_backward(queries, key_rows, value_rows, probabilities, probs_low, grad_attended):
    factor = queries.shape[-1] ** (-0.5)
    grad_probs = jnp.einsum(
        "sbhd,skd->shbk", grad_attended.astype(jnp.float32), value_rows.astype(jnp.float32)
    )
    inner_sum = jnp.sum(probabilities * grad_probs, axis=-1, keepdims=True)
    grad_scores = (probabilities * (grad_probs - inner_sum) * factor).astype(jnp.bfloat16)
    grad_queries = jnp.einsum(
        "shbk,skd->sbhd", grad_scores.astype(jnp.float32), key_rows.astype(jnp.float32)
    )
    grad_keys = jnp.einsum(
        "shbk,sbhd->skd", grad_scores.astype(jnp.float32), queries.astype(jnp.float32)
    )
    grad_values = jnp.einsum(
        "shbk,sbhd->skd", probs_low.astype(jnp.float32), grad_attended.astype(jnp.float32)
    )
    return (grad_queries.astype(jnp.bfloat16), grad_keys, grad_values)


def attention_forward(
    row_block,
    query_weights,
    own_kv_weights,
    key_cache,
    prefix_value_cache,
    lengths,
    first_head,
    carried,
):
    heads_here = query_weights.shape[1] // HEAD_SIZE
    query_group_count = QUERY_HEADS // KEY_VALUE_HEADS
    row_count = row_block.shape[0]
    seq_count = row_count // BLOCK
    key_value_width = KEY_VALUE_HEADS * HEAD_SIZE
    kv_first = first_head // query_group_count
    queries = jnp.dot(row_block, query_weights, preferred_element_type=jnp.float32).astype(
        jnp.bfloat16
    )
    queries = queries.reshape(seq_count, BLOCK, heads_here, HEAD_SIZE)
    usable = jnp.concatenate(
        [
            jnp.arange(PREFIX_SLOTS)[None, :] < lengths[:, None],
            jnp.ones((seq_count, BLOCK), dtype=jnp.bool_),
        ],
        axis=1,
    )
    kv_now = kv_first + 0
    own_rows = jnp.dot(row_block, own_kv_weights, preferred_element_type=jnp.float32).astype(
        jnp.bfloat16
    )
    own_rows, carried = lax.optimization_barrier((own_rows, carried))
    kv_rows = head_gather(own_rows, 1)
    pair_rows = jnp.concatenate(
        [
            lax.dynamic_slice_in_dim(kv_rows, kv_now * HEAD_SIZE, HEAD_SIZE, 1),
            lax.dynamic_slice_in_dim(kv_rows, key_value_width + kv_now * HEAD_SIZE, HEAD_SIZE, 1),
        ],
        axis=1,
    )
    key_rows = jnp.concatenate(
        [
            lax.dynamic_slice_in_dim(key_cache, kv_now * HEAD_SIZE, HEAD_SIZE, 2),
            pair_rows[:, :HEAD_SIZE].reshape(seq_count, BLOCK, HEAD_SIZE),
        ],
        axis=1,
    )
    value_rows = jnp.concatenate(
        [
            lax.dynamic_slice_in_dim(prefix_value_cache, kv_now * HEAD_SIZE, HEAD_SIZE, 2),
            pair_rows[:, HEAD_SIZE:].reshape(seq_count, BLOCK, HEAD_SIZE),
        ],
        axis=1,
    )
    probabilities, probs_low, attended = attend_forward(queries, key_rows, value_rows, usable)
    saved = [(queries, key_rows, value_rows, probabilities, probs_low)]
    joined = attended.reshape(row_count, heads_here * HEAD_SIZE)
    return (joined, saved, carried)


def attention_backward(
    grad_rows, query_weights, output_weights, own_kv_weights, saved, kv_now, carried
):
    heads_here = query_weights.shape[1] // HEAD_SIZE
    row_count = grad_rows.shape[0]
    seq_count = row_count // BLOCK
    key_value_width = KEY_VALUE_HEADS * HEAD_SIZE
    grad_attn = jnp.einsum(
        "td,fd->tf", grad_rows, output_weights, preferred_element_type=jnp.float32
    ).astype(jnp.bfloat16)
    grad_attn = grad_attn.reshape(seq_count, BLOCK, heads_here, HEAD_SIZE)
    query_part, key_rows, value_rows, probabilities, probs_low = saved[0]
    grad_queries, grad_keys, grad_values = attend_backward(
        query_part, key_rows, value_rows, probabilities, probs_low, grad_attn
    )
    placed = jnp.zeros((row_count, 2 * key_value_width), jnp.float32)
    placed = lax.dynamic_update_slice_in_dim(
        placed, grad_keys[:, PREFIX_SLOTS:].reshape(row_count, HEAD_SIZE), kv_now * HEAD_SIZE, 1
    )
    placed = lax.dynamic_update_slice_in_dim(
        placed,
        grad_values[:, PREFIX_SLOTS:].reshape(row_count, HEAD_SIZE),
        key_value_width + kv_now * HEAD_SIZE,
        1,
    )
    placed, carried = lax.optimization_barrier((placed, carried))
    own_grads = head_sums(placed, axis=1)
    running = jnp.einsum(
        "tc,dc->td", own_grads, own_kv_weights.astype(jnp.float32), precision=lax.Precision.HIGHEST
    )
    query_flat = grad_queries.reshape(row_count, heads_here * HEAD_SIZE)
    total = running + jnp.einsum(
        "tf,df->td", query_flat, query_weights, preferred_element_type=jnp.float32
    )
    return (total, carried)


def head_gather(block, axis):
    count = lax.axis_size("head")
    me = lax.axis_index("head")
    parts = [block] + [
        lax.ppermute(block, "head", perm=[(j, (j + shift) % count) for j in range(count)])
        for shift in range(1, count)
    ]
    return head_order(parts, axis)


def head_order(parts, axis):
    count = lax.axis_size("head")
    me = lax.axis_index("head")
    block = parts[0]
    ordered = jnp.take(jnp.stack(parts), (me - jnp.arange(count)) % count, axis=0)
    ordered = jnp.moveaxis(ordered, 0, axis)
    merged = list(block.shape)
    merged[axis] = count * block.shape[axis]
    return ordered.reshape(merged)


def head_rows(row_block):
    return head_gather(row_block, 0)


def after_first_hop(block, waiting):
    count = lax.axis_size("head")
    first = lax.ppermute(block, "head", perm=[(j, (j + 1) % count) for j in range(count)])
    return lax.optimization_barrier((waiting, first))


def head_sums(partial_rows, axis=0):
    count = lax.axis_size("head")
    me = lax.axis_index("head")
    size = partial_rows.shape[axis] // count

    def chunk(index):
        return lax.dynamic_slice_in_dim(partial_rows, index * size, size, axis)

    total = chunk(me)
    for shift in range(1, count):
        total = total + lax.ppermute(
            chunk((me + shift) % count),
            "head",
            perm=[(j, (j + shift) % count) for j in range(count)],
        )
    return total


def to_experts(outgoing):
    return lax.all_to_all(outgoing, ("expert", "head"), split_axis=0, concat_axis=0, tiled=True)


def from_experts(results):
    return lax.all_to_all(results, ("expert", "head"), split_axis=0, concat_axis=0, tiled=True)


def body(
    hidden_in,
    out_grad,
    loss_mask,
    expert_ids,
    gate_weights,
    cache_lengths,
    key_cache,
    prefix_value_cache,
    attn_gain,
    moe_gain,
    w_query,
    key_value_weight,
    w_output,
    w_gate,
    w_up,
    w_down,
):
    highest_prec = lax.Precision.HIGHEST
    owned = hidden_in.shape[0]
    width = hidden_in.shape[1]
    normed_one, inverse_one = rms_forward(hidden_in, attn_gain)
    attn_rows = normed_one.astype(jnp.bfloat16)
    heads_here = w_query.shape[1] // HEAD_SIZE
    first_head = lax.axis_index("head") * heads_here
    gathered_rows = head_rows(attn_rows)
    device_count = lax.axis_size("expert") * lax.axis_size("head")
    capacity = (owned * TOP * 4 + 3 * device_count - 1) // (3 * device_count)
    slot_total = device_count * capacity
    flat_ids = expert_ids.reshape(-1)
    one_hot = (flat_ids[:, None] == jnp.arange(device_count, dtype=jnp.int32)[None, :]).astype(
        jnp.int32
    )
    earlier = jnp.cumsum(one_hot, axis=0) - one_hot
    position = jnp.sum(earlier * one_hot, axis=1)
    target = flat_ids * capacity + position
    matched = (jnp.arange(slot_total, dtype=jnp.int32)[:, None] == target[None, :]).reshape(
        device_count, capacity, owned, TOP
    )
    placement = jnp.any(matched, axis=3).astype(jnp.bfloat16)
    weighting = jnp.sum(jnp.where(matched, gate_weights[None, None, :, :], 0.0), axis=3)
    cotangent = out_grad.astype(jnp.float32) * loss_mask.astype(jnp.float32)[:, None]
    lanes = 128
    pieces = width // lanes
    grad_out = jnp.einsum(
        "dct,tkl->dckl",
        weighting,
        cotangent.reshape(owned, pieces, lanes),
        precision=highest_prec,
    ).astype(jnp.bfloat16)
    attended, saved, grad_out = attention_forward(
        gathered_rows, w_query, key_value_weight, key_cache, prefix_value_cache, cache_lengths, first_head, grad_out
    )
    mixed = head_sums(jnp.dot(attended, w_output, preferred_element_type=jnp.float32))
    hidden = (hidden_in.astype(jnp.float32) + mixed).astype(jnp.bfloat16)
    normed_two, inverse_two = rms_forward(hidden, moe_gain)
    moe_rows = normed_two.astype(jnp.bfloat16)
    outgoing = jnp.einsum(
        "dct,tkl->dckl",
        placement,
        moe_rows.reshape(owned, pieces, lanes),
        preferred_element_type=jnp.float32,
    ).astype(jnp.bfloat16)
    flat_shape = (device_count, capacity * pieces, lanes)
    split_shape = (device_count, capacity, pieces, lanes)
    rows_in = to_experts(outgoing.reshape(flat_shape)).reshape(split_shape)
    grads_in = to_experts(grad_out.reshape(flat_shape)).reshape(split_shape)
    gate_matrix = w_gate[0].reshape(pieces, lanes, -1)
    up_matrix = w_up[0].reshape(pieces, lanes, -1)
    down_matrix = w_down[0].reshape(-1, pieces, lanes)
    gate_pre = jnp.einsum(
        "sckl,klf->scf", rows_in, gate_matrix, preferred_element_type=jnp.float32
    )
    up_pre = jnp.einsum("sckl,klf->scf", rows_in, up_matrix, preferred_element_type=jnp.float32)
    sigma = jax.nn.sigmoid(gate_pre)
    activated = (gate_pre * sigma * up_pre).astype(jnp.bfloat16)
    result = jnp.einsum(
        "scf,fkl->sckl", activated, down_matrix, preferred_element_type=jnp.float32
    ).astype(jnp.bfloat16)
    grad_act = jnp.einsum(
        "sckl,fkl->scf", grads_in, down_matrix, preferred_element_type=jnp.float32
    )
    grad_gate = (grad_act * up_pre * sigma * (1.0 + gate_pre * (1.0 - sigma))).astype(jnp.bfloat16)
    grad_up = (grad_act * gate_pre * sigma).astype(jnp.bfloat16)
    grad_back = jnp.einsum(
        "scf,klf->sckl", grad_gate, gate_matrix, preferred_element_type=jnp.float32
    )
    grad_back = grad_back + jnp.einsum(
        "scf,klf->sckl", grad_up, up_matrix, preferred_element_type=jnp.float32
    )
    grad_back = grad_back.astype(jnp.bfloat16)
    grad_home = from_experts(grad_back.reshape(flat_shape)).reshape(split_shape)
    grad_moe = jnp.einsum(
        "dct,dckl->tkl", placement, grad_home, preferred_element_type=jnp.float32
    ).reshape(owned, width)
    grad_hidden = cotangent + rms_backward(hidden, moe_gain, inverse_two, grad_moe)
    grad_low = grad_hidden.astype(jnp.bfloat16)
    count = lax.axis_size("head")
    grad_low, result = lax.optimization_barrier((grad_low, result))
    grad_parts = [grad_low] + [
        lax.ppermute(grad_low, "head", perm=[(j, (j + shift) % count) for j in range(count)])
        for shift in range(1, count)
    ]
    result_home = from_experts(result.reshape(flat_shape)).reshape(split_shape)
    grad_parts = list(lax.optimization_barrier(tuple(grad_parts)))
    grad_gathered = head_order(grad_parts, 0)
    grad_partial, result_home = attention_backward(
        grad_gathered,
        w_query,
        w_output,
        key_value_weight,
        saved,
        first_head // (QUERY_HEADS // KEY_VALUE_HEADS),
        result_home,
    )
    grad_attn_rows = head_sums(grad_partial)
    input_grad = (
        grad_hidden + rms_backward(hidden_in, attn_gain, inverse_one, grad_attn_rows)
    ).astype(jnp.bfloat16)
    moe_sum = jnp.einsum(
        "dct,dckl->tkl",
        weighting,
        result_home.astype(jnp.float32),
        precision=highest_prec,
    ).reshape(owned, width)
    layer_out = (hidden.astype(jnp.float32) + moe_sum).astype(jnp.bfloat16)
    return (layer_out, input_grad)


def solution(mesh):
    in_specs = (
        P(("groups", "expert", "head"), None),
        P(("groups", "expert", "head"), None),
        P(("groups", "expert", "head")),
        P(("groups", "expert", "head"), None),
        P(("groups", "expert", "head"), None),
        P(("groups", "expert")),
        P(("groups", "expert"), None, None),
        P(("groups", "expert"), None, None),
        P(),
        P(),
        P(None, "head"),
        P(None, "head"),
        P("head", None),
        P(("expert", "head"), None, None),
        P(("expert", "head"), None, None),
        P(("expert", "head"), None, None),
    )
    out_specs = (P(("groups", "expert", "head"), None), P(("groups", "expert", "head"), None))
    return jax.shard_map(body, mesh=mesh, in_specs=in_specs, out_specs=out_specs, check_vma=False)
```

```python
import jax
import jax.numpy as jnp
from jax import lax
from jax.sharding import PartitionSpec as P

QUERY_HEADS = 16
KEY_VALUE_HEADS = 2
HEAD_SIZE = 128
TOP = 8
BLOCK = 16
PREFIX_SLOTS = 32


EPS = 1e-06
NEG_FILL = -1e30


def rms_forward(row_block, gain_vec):
    values = row_block.astype(jnp.float32)
    inverse = lax.rsqrt(jnp.mean(values * values, axis=-1, keepdims=True) + EPS)
    return (values * inverse * gain_vec, inverse)


def rms_backward(row_block, gain_vec, inverse, upstream):
    scaled_rows = row_block.astype(jnp.float32) * inverse
    weighted = upstream * gain_vec
    inner_mean = jnp.mean(weighted * scaled_rows, axis=-1, keepdims=True)
    return inverse * (weighted - scaled_rows * inner_mean)


def attend_forward(queries, key_rows, value_rows, usable):
    factor = queries.shape[-1] ** (-0.5)
    scores = (
        jnp.einsum("sbhd,skd->shbk", queries.astype(jnp.float32), key_rows.astype(jnp.float32))
        * factor
    )
    scores = jnp.where(usable[:, None, None, :], scores, NEG_FILL)
    highest = jnp.max(scores, axis=-1, keepdims=True)
    exponent_terms = jnp.exp(scores - highest)
    probabilities = exponent_terms / jnp.sum(exponent_terms, axis=-1, keepdims=True)
    probs_low = probabilities.astype(jnp.bfloat16)
    attended = jnp.einsum(
        "shbk,skd->sbhd", probs_low.astype(jnp.float32), value_rows.astype(jnp.float32)
    )
    return (probabilities, probs_low, attended.astype(jnp.bfloat16))


def attend_backward(queries, key_rows, value_rows, probabilities, probs_low, grad_attended):
    factor = queries.shape[-1] ** (-0.5)
    grad_probs = jnp.einsum(
        "sbhd,skd->shbk", grad_attended.astype(jnp.float32), value_rows.astype(jnp.float32)
    )
    inner_sum = jnp.sum(probabilities * grad_probs, axis=-1, keepdims=True)
    grad_scores = (probabilities * (grad_probs - inner_sum) * factor).astype(jnp.bfloat16)
    grad_queries = jnp.einsum(
        "shbk,skd->sbhd", grad_scores.astype(jnp.float32), key_rows.astype(jnp.float32)
    )
    grad_keys = jnp.einsum(
        "shbk,sbhd->skd", grad_scores.astype(jnp.float32), queries.astype(jnp.float32)
    )
    grad_values = jnp.einsum(
        "shbk,sbhd->skd", probs_low.astype(jnp.float32), grad_attended.astype(jnp.float32)
    )
    return (grad_queries.astype(jnp.bfloat16), grad_keys, grad_values)


def attention_forward(
    row_block,
    query_weights,
    own_kv_weights,
    key_cache,
    prefix_value_cache,
    lengths,
    first_head,
    carried,
):
    heads_here = query_weights.shape[1] // HEAD_SIZE
    query_group_count = QUERY_HEADS // KEY_VALUE_HEADS
    row_count = row_block.shape[0]
    seq_count = row_count // BLOCK
    key_value_width = KEY_VALUE_HEADS * HEAD_SIZE
    kv_first = first_head // query_group_count
    queries = jnp.dot(row_block, query_weights, preferred_element_type=jnp.float32).astype(
        jnp.bfloat16
    )
    queries = queries.reshape(seq_count, BLOCK, heads_here, HEAD_SIZE)
    usable = jnp.concatenate(
        [
            jnp.arange(PREFIX_SLOTS)[None, :] < lengths[:, None],
            jnp.ones((seq_count, BLOCK), dtype=jnp.bool_),
        ],
        axis=1,
    )
    kv_now = kv_first + 0
    own_rows = jnp.dot(row_block, own_kv_weights, preferred_element_type=jnp.float32).astype(
        jnp.bfloat16
    )
    kv_rows = head_gather(own_rows, 1)
    pair_rows = jnp.concatenate(
        [
            lax.dynamic_slice_in_dim(kv_rows, kv_now * HEAD_SIZE, HEAD_SIZE, 1),
            lax.dynamic_slice_in_dim(kv_rows, key_value_width + kv_now * HEAD_SIZE, HEAD_SIZE, 1),
        ],
        axis=1,
    )
    key_rows = jnp.concatenate(
        [
            lax.dynamic_slice_in_dim(key_cache, kv_now * HEAD_SIZE, HEAD_SIZE, 2),
            pair_rows[:, :HEAD_SIZE].reshape(seq_count, BLOCK, HEAD_SIZE),
        ],
        axis=1,
    )
    value_rows = jnp.concatenate(
        [
            lax.dynamic_slice_in_dim(prefix_value_cache, kv_now * HEAD_SIZE, HEAD_SIZE, 2),
            pair_rows[:, HEAD_SIZE:].reshape(seq_count, BLOCK, HEAD_SIZE),
        ],
        axis=1,
    )
    probabilities, probs_low, attended = attend_forward(queries, key_rows, value_rows, usable)
    saved = [(queries, key_rows, value_rows, probabilities, probs_low)]
    joined = attended.reshape(row_count, heads_here * HEAD_SIZE)
    return (joined, saved, carried)


def attention_backward(
    grad_rows, query_weights, output_weights, own_kv_weights, saved, kv_now, carried
):
    heads_here = query_weights.shape[1] // HEAD_SIZE
    row_count = grad_rows.shape[0]
    seq_count = row_count // BLOCK
    key_value_width = KEY_VALUE_HEADS * HEAD_SIZE
    grad_attn = jnp.einsum(
        "td,fd->tf", grad_rows, output_weights, preferred_element_type=jnp.float32
    ).astype(jnp.bfloat16)
    grad_attn = grad_attn.reshape(seq_count, BLOCK, heads_here, HEAD_SIZE)
    query_part, key_rows, value_rows, probabilities, probs_low = saved[0]
    grad_queries, grad_keys, grad_values = attend_backward(
        query_part, key_rows, value_rows, probabilities, probs_low, grad_attn
    )
    placed = jnp.zeros((row_count, 2 * key_value_width), jnp.float32)
    placed = lax.dynamic_update_slice_in_dim(
        placed, grad_keys[:, PREFIX_SLOTS:].reshape(row_count, HEAD_SIZE), kv_now * HEAD_SIZE, 1
    )
    placed = lax.dynamic_update_slice_in_dim(
        placed,
        grad_values[:, PREFIX_SLOTS:].reshape(row_count, HEAD_SIZE),
        key_value_width + kv_now * HEAD_SIZE,
        1,
    )
    placed, carried = lax.optimization_barrier((placed, carried))
    own_grads = head_sums(placed, axis=1)
    running = jnp.einsum(
        "tc,dc->td", own_grads, own_kv_weights.astype(jnp.float32), precision=lax.Precision.HIGHEST
    )
    query_flat = grad_queries.reshape(row_count, heads_here * HEAD_SIZE)
    total = running + jnp.einsum(
        "tf,df->td", query_flat, query_weights, preferred_element_type=jnp.float32
    )
    return (total, carried)


def head_gather(block, axis):
    count = lax.axis_size("head")
    me = lax.axis_index("head")
    parts = [block] + [
        lax.ppermute(block, "head", perm=[(j, (j + shift) % count) for j in range(count)])
        for shift in range(1, count)
    ]
    return head_order(parts, axis)


def head_order(parts, axis):
    count = lax.axis_size("head")
    me = lax.axis_index("head")
    block = parts[0]
    ordered = jnp.take(jnp.stack(parts), (me - jnp.arange(count)) % count, axis=0)
    ordered = jnp.moveaxis(ordered, 0, axis)
    merged = list(block.shape)
    merged[axis] = count * block.shape[axis]
    return ordered.reshape(merged)


def head_rows(row_block):
    return head_gather(row_block, 0)


def after_first_hop(block, waiting):
    count = lax.axis_size("head")
    first = lax.ppermute(block, "head", perm=[(j, (j + 1) % count) for j in range(count)])
    return lax.optimization_barrier((waiting, first))


def head_sums(partial_rows, axis=0):
    count = lax.axis_size("head")
    me = lax.axis_index("head")
    size = partial_rows.shape[axis] // count

    def chunk(index):
        return lax.dynamic_slice_in_dim(partial_rows, index * size, size, axis)

    total = chunk(me)
    for shift in range(1, count):
        total = total + lax.ppermute(
            chunk((me + shift) % count),
            "head",
            perm=[(j, (j + shift) % count) for j in range(count)],
        )
    return total


def to_experts(outgoing):
    return lax.all_to_all(outgoing, ("expert", "head"), split_axis=0, concat_axis=0, tiled=True)


def from_experts(results):
    return lax.all_to_all(results, ("expert", "head"), split_axis=0, concat_axis=0, tiled=True)


def body(
    hidden_in,
    out_grad,
    loss_mask,
    expert_ids,
    gate_weights,
    cache_lengths,
    key_cache,
    prefix_value_cache,
    attn_gain,
    moe_gain,
    w_query,
    key_value_weight,
    w_output,
    w_gate,
    w_up,
    w_down,
):
    highest_prec = lax.Precision.HIGHEST
    owned = hidden_in.shape[0]
    width = hidden_in.shape[1]
    normed_one, inverse_one = rms_forward(hidden_in, attn_gain)
    attn_rows = normed_one.astype(jnp.bfloat16)
    heads_here = w_query.shape[1] // HEAD_SIZE
    first_head = lax.axis_index("head") * heads_here

    device_count = lax.axis_size("expert") * lax.axis_size("head")
    capacity = (owned * TOP * 4 + 3 * device_count - 1) // (3 * device_count)
    slot_total = device_count * capacity
    flat_ids = expert_ids.reshape(-1)
    one_hot = (flat_ids[:, None] == jnp.arange(device_count, dtype=jnp.int32)[None, :]).astype(
        jnp.int32
    )
    earlier = jnp.cumsum(one_hot, axis=0) - one_hot
    position = jnp.sum(earlier * one_hot, axis=1)
    target = flat_ids * capacity + position
    matched = (jnp.arange(slot_total, dtype=jnp.int32)[:, None] == target[None, :]).reshape(
        device_count, capacity, owned, TOP
    )
    placement = jnp.any(matched, axis=3).astype(jnp.bfloat16)
    weighting = jnp.sum(jnp.where(matched, gate_weights[None, None, :, :], 0.0), axis=3)
    cotangent = out_grad.astype(jnp.float32) * loss_mask.astype(jnp.float32)[:, None]
    lanes = 128
    pieces = width // lanes
    grad_out = jnp.einsum(
        "dct,tkl->dckl",
        weighting,
        cotangent.reshape(owned, pieces, lanes),
        precision=highest_prec,
    ).astype(jnp.bfloat16)
    attn_rows, grad_out = lax.optimization_barrier((attn_rows, grad_out))
    gathered_rows = head_rows(attn_rows)
    attended, saved, grad_out = attention_forward(
        gathered_rows, w_query, key_value_weight, key_cache, prefix_value_cache, cache_lengths, first_head, grad_out
    )
    mixed = head_sums(jnp.dot(attended, w_output, preferred_element_type=jnp.float32))
    hidden = (hidden_in.astype(jnp.float32) + mixed).astype(jnp.bfloat16)
    normed_two, inverse_two = rms_forward(hidden, moe_gain)
    moe_rows = normed_two.astype(jnp.bfloat16)
    outgoing = jnp.einsum(
        "dct,tkl->dckl",
        placement,
        moe_rows.reshape(owned, pieces, lanes),
        preferred_element_type=jnp.float32,
    ).astype(jnp.bfloat16)
    flat_shape = (device_count, capacity * pieces, lanes)
    split_shape = (device_count, capacity, pieces, lanes)
    rows_in = to_experts(outgoing.reshape(flat_shape)).reshape(split_shape)
    grads_in = to_experts(grad_out.reshape(flat_shape)).reshape(split_shape)
    gate_matrix = w_gate[0].reshape(pieces, lanes, -1)
    up_matrix = w_up[0].reshape(pieces, lanes, -1)
    down_matrix = w_down[0].reshape(-1, pieces, lanes)
    gate_pre = jnp.einsum(
        "sckl,klf->scf", rows_in, gate_matrix, preferred_element_type=jnp.float32
    )
    up_pre = jnp.einsum("sckl,klf->scf", rows_in, up_matrix, preferred_element_type=jnp.float32)
    sigma = jax.nn.sigmoid(gate_pre)
    activated = (gate_pre * sigma * up_pre).astype(jnp.bfloat16)
    result = jnp.einsum(
        "scf,fkl->sckl", activated, down_matrix, preferred_element_type=jnp.float32
    ).astype(jnp.bfloat16)
    grad_act = jnp.einsum(
        "sckl,fkl->scf", grads_in, down_matrix, preferred_element_type=jnp.float32
    )
    grad_gate = (grad_act * up_pre * sigma * (1.0 + gate_pre * (1.0 - sigma))).astype(jnp.bfloat16)
    grad_up = (grad_act * gate_pre * sigma).astype(jnp.bfloat16)
    grad_back = jnp.einsum(
        "scf,klf->sckl", grad_gate, gate_matrix, preferred_element_type=jnp.float32
    )
    grad_back = grad_back + jnp.einsum(
        "scf,klf->sckl", grad_up, up_matrix, preferred_element_type=jnp.float32
    )
    grad_back = grad_back.astype(jnp.bfloat16)
    grad_home = from_experts(grad_back.reshape(flat_shape)).reshape(split_shape)
    grad_moe = jnp.einsum(
        "dct,dckl->tkl", placement, grad_home, preferred_element_type=jnp.float32
    ).reshape(owned, width)
    grad_hidden = cotangent + rms_backward(hidden, moe_gain, inverse_two, grad_moe)
    grad_low = grad_hidden.astype(jnp.bfloat16)
    count = lax.axis_size("head")
    grad_low, result = lax.optimization_barrier((grad_low, result))
    grad_parts = [grad_low] + [
        lax.ppermute(grad_low, "head", perm=[(j, (j + shift) % count) for j in range(count)])
        for shift in range(1, count)
    ]
    result_home = from_experts(result.reshape(flat_shape)).reshape(split_shape)
    grad_parts = list(lax.optimization_barrier(tuple(grad_parts)))
    grad_gathered = head_order(grad_parts, 0)
    grad_partial, result_home = attention_backward(
        grad_gathered,
        w_query,
        w_output,
        key_value_weight,
        saved,
        first_head // (QUERY_HEADS // KEY_VALUE_HEADS),
        result_home,
    )
    grad_attn_rows = head_sums(grad_partial)
    input_grad = (
        grad_hidden + rms_backward(hidden_in, attn_gain, inverse_one, grad_attn_rows)
    ).astype(jnp.bfloat16)
    moe_sum = jnp.einsum(
        "dct,dckl->tkl",
        weighting,
        result_home.astype(jnp.float32),
        precision=highest_prec,
    ).reshape(owned, width)
    layer_out = (hidden.astype(jnp.float32) + moe_sum).astype(jnp.bfloat16)
    return (layer_out, input_grad)


def solution(mesh):
    in_specs = (
        P(("groups", "expert", "head"), None),
        P(("groups", "expert", "head"), None),
        P(("groups", "expert", "head")),
        P(("groups", "expert", "head"), None),
        P(("groups", "expert", "head"), None),
        P(("groups", "expert")),
        P(("groups", "expert"), None, None),
        P(("groups", "expert"), None, None),
        P(),
        P(),
        P(None, "head"),
        P(None, "head"),
        P("head", None),
        P(("expert", "head"), None, None),
        P(("expert", "head"), None, None),
        P(("expert", "head"), None, None),
    )
    out_specs = (P(("groups", "expert", "head"), None), P(("groups", "expert", "head"), None))
    return jax.shard_map(body, mesh=mesh, in_specs=in_specs, out_specs=out_specs, check_vma=False)
```
